32 devices in a mesh: groups: 2 (over x), col: 8 (over z, y), row: 2 (over core).
Axes of the slice: x: 2, y: 2, z: 4, core: 2. Of those that a mesh axis runs over, the one named last changes fastest.
Arguments:
- queries: bfloat16 [32, 8, 64, 1536], P(('groups', 'row'), 'col'), parts along dimension 0, may hold values from -300 to 300
- key_mant: bfloat16 [32, 8, 64, 1536], P(('groups', 'row'), 'col'), parts along dimension 0, may hold values from -8 to 8
- key_exp: int32 [32, 8, 2, 1536], P(('groups', 'row'), 'col'), parts along dimension 0, may hold values from -1 to 1
- value_mant: bfloat16 [32, 8, 64, 1536], P(('groups', 'row'), 'col'), parts along dimension 0, may hold values from -4 to 4
- value_exp: int32 [32, 8, 2, 1536], P(('groups', 'row'), 'col'), parts along dimension 0, may hold values from 0 to 2
- cycle_list: int32 [4, 8, 4], P(('groups', 'row'), 'col'), parts along dimension 0, may hold values from 0 to 17, as said below
- dilated_list: int32 [4, 8, 4], P(('groups', 'row'), 'col'), parts along dimension 0, may hold values from 0 to 13, as said below
Outputs:
- attended: bfloat16 [32, 8, 64, 1536], P(('groups', 'row'), 'col'), parts along dimension 0
The draws below stay inside these ranges and needn't reach their ends.
There are 2 independent parts, one for each index of `groups`. The reference program is written for one: setup_inputs(seed, part) draws one part's arguments, and reference() takes and returns one part's arrays. A program takes and returns all parts, laid end to end along the dimension named above; each array names one. Nothing has to cross between parts.
Inputs may be any that keep to these rules, and one draw needn't show every extreme that they name: `cycle_list`: the 4 entries of a tile are distinct; none names a block outside the image, and every side of the cycle that lies inside the image is named at least once. `dilated_list`: the 4 entries of a tile are distinct.
All inputs are finite; a program needn't handle non-finite values.
Results may differ from the reference program's by a relative error of at most 0.0043.
Values may be sent and summed in bfloat16 or wider, within the bound.
No kernel may reach another device: no remote copies, remote signals or barrier semaphores. Data moves between devices by JAX's collectives and lax.ppermute only.
A program may use at most 128 MiB of HBM per device.

```python
import jax
import jax.numpy as jnp
from jax import lax

HEADS = 12
HEAD_DIM = 128
DA = 1536
BLOCK = 64
QG = 32
TILE_BLOCK_ROWS = 8
DILATION_TILES = 8
TILE_ROWS = 2
IMAGE_TILE_COLS = 8
GR = 16
GC = 8
NB = 4
ND = 4


def key_field(key):
    normal_part = jnp.clip(jax.random.normal(jax.random.fold_in(key, 11), (GR, GC, BLOCK, DA), jnp.float32), -4.0, 4.0)
    return normal_part


def draw_key_mant(key, part):
    return key_field(key).astype(jnp.bfloat16)


def draw_queries(key, part):
    drawn = jnp.clip(jax.random.normal(jax.random.fold_in(key, 31), (GR, GC, BLOCK, DA), jnp.float32), -4.0, 4.0)
    return drawn.astype(jnp.bfloat16)


def draw_cycle_list(key, part):
    cycle_count = 2 * TILE_BLOCK_ROWS + 2
    candidate = jnp.arange(cycle_count, dtype=jnp.int32)[None, None, :]
    cycle_side = jnp.where(candidate == 0, 0, jnp.where(candidate == 1, 1, jnp.where(candidate < TILE_BLOCK_ROWS + 2, 2, 3)))
    cycle_place = jnp.where(candidate < 2, 0, jnp.where(candidate < TILE_BLOCK_ROWS + 2, candidate - 2, candidate - 2 - TILE_BLOCK_ROWS))
    tile_row = jnp.arange(TILE_ROWS, dtype=jnp.int32)[:, None, None]
    tile_col = jnp.arange(IMAGE_TILE_COLS, dtype=jnp.int32)[None, :, None]
    inside = (cycle_side == 0) & (tile_row > 0) | (cycle_side == 1) & (tile_row < TILE_ROWS - 1) | (cycle_side == 2) & (tile_col > 0) | (cycle_side == 3) & (tile_col < IMAGE_TILE_COLS - 1)
    picked = jax.random.randint(jax.random.fold_in(key, 41), (TILE_ROWS, IMAGE_TILE_COLS, 2), 0, TILE_BLOCK_ROWS)
    forced = (cycle_side < 2) | (cycle_side == 2) & (cycle_place == picked[:, :, 0:1]) | (cycle_side == 3) & (cycle_place == picked[:, :, 1:2])
    jitter = jax.random.randint(jax.random.fold_in(key, 42), (TILE_ROWS, IMAGE_TILE_COLS, cycle_count), 0, 1 << 20)
    ranking = jitter * cycle_count + candidate + forced.astype(jnp.int32) * (1 << 28)
    ranking = jnp.where(inside, ranking, -1 - candidate)
    return lax.top_k(ranking, NB)[1].astype(jnp.int32)


def draw_dilated_list(key, part):
    distant_count = (DILATION_TILES - 1) * (TILE_BLOCK_ROWS // 4)
    candidate = jnp.arange(distant_count, dtype=jnp.int32)[None, None, :]
    jitter = jax.random.randint(jax.random.fold_in(key, 51), (TILE_ROWS, IMAGE_TILE_COLS, distant_count), 0, 1 << 20)
    ranking = jitter * distant_count + candidate
    return lax.top_k(ranking, ND)[1].astype(jnp.int32)


def plant(drawn, stream_key, smallest, high):
    spot = [jax.random.randint(jax.random.fold_in(stream_key, axis), (), 0, length) for axis, length in enumerate(drawn.shape)]
    main_axis = drawn.shape.index(max(drawn.shape))
    beside = spot[:main_axis] + [(spot[main_axis] + 1) % drawn.shape[main_axis]] + spot[main_axis + 1:]
    return drawn.at[tuple(spot)].set(smallest).at[tuple(beside)].set(high)


def block_levels(key, shape, split, least, top_value):
    loudness = 1.0
    for axis_at, shards_of in split:
        draws = jax.random.uniform(jax.random.fold_in(jax.random.fold_in(key, 6), axis_at), (shards_of,), jnp.float32, least / len(split), top_value / len(split))
        loudness = loudness * jnp.repeat(jnp.exp(draws), shape[axis_at] // shards_of).reshape((-1,) + (1,) * (len(shape) - 1 - axis_at))
    return loudness


def gaussian(own_key, extent, spread, most, cuts=(), kind=jnp.bfloat16):
    loudness = block_levels(own_key, extent, cuts, -0.22, 0.18) if cuts else 1.0
    values = jax.random.normal(own_key, extent, jnp.float32) * spread * loudness
    return jnp.minimum(jnp.maximum(values, -most), most).astype(kind)


def setup_inputs(seed: int = 0, part: int = 0) -> dict:
    splits = jax.random.split(jax.random.key(seed), 8)
    own_keys = jax.random.split(jax.random.fold_in(splits[7], part), 8)
    queries = draw_queries(jax.random.fold_in(jax.random.fold_in(splits[7], part), 71), part)
    key_mant = draw_key_mant(jax.random.fold_in(jax.random.fold_in(splits[7], part), 71), part)
    key_exp = plant(jax.random.randint(own_keys[2], (GR, GC, BLOCK // QG, DA), -1, 2), jax.random.fold_in(own_keys[2], 1), -1, 1).astype(jnp.int32)
    value_mant = gaussian(own_keys[3], (GR, GC, BLOCK, DA), 1.0, 4.0, ((0, 2), (1, 8)))
    value_exp = plant(jax.random.randint(own_keys[4], (GR, GC, BLOCK // QG, DA), 0, 3), jax.random.fold_in(own_keys[4], 1), 0, 2).astype(jnp.int32)
    cycle_list = draw_cycle_list(jax.random.fold_in(jax.random.fold_in(splits[7], part), 71), part)
    dilated_list = draw_dilated_list(jax.random.fold_in(jax.random.fold_in(splits[7], part), 71), part)
    return dict(queries=queries, key_mant=key_mant, key_exp=key_exp, value_mant=value_mant, value_exp=value_exp, cycle_list=cycle_list, dilated_list=dilated_list)


def dequant(mantissa, exponent):
    factor = jnp.exp2(jnp.repeat(exponent, QG, axis=2).astype(jnp.float32))
    return (mantissa.astype(jnp.float32) * factor).astype(jnp.bfloat16)


def attend(query_tile, key_tile, value_tile):
    query_heads = query_tile.astype(jnp.float32).reshape(-1, HEADS, HEAD_DIM)
    key_heads = key_tile.astype(jnp.float32).reshape(-1, HEADS, HEAD_DIM)
    value_heads = value_tile.astype(jnp.float32).reshape(-1, HEADS, HEAD_DIM)
    scores = jnp.einsum("qhd,khd->hqk", query_heads, key_heads) * (HEAD_DIM ** -0.5)
    row_max = jnp.max(scores, axis=-1, keepdims=True)
    weights = jnp.exp(scores - row_max)
    row_total = jnp.sum(weights, axis=-1)
    rounded = lax.optimization_barrier(weights.astype(jnp.bfloat16))
    blended = jnp.einsum("hqk,khd->qhd", rounded.astype(jnp.float32), value_heads)
    return (blended / jnp.transpose(row_total)[:, :, None]).astype(jnp.bfloat16).reshape(-1, DA)


def reference(queries, key_mant, key_exp, value_mant, value_exp, cycle_list, dilated_list):
    stacked = jnp.stack([dequant(key_mant, key_exp), dequant(value_mant, value_exp)])
    step_spacing = IMAGE_TILE_COLS // DILATION_TILES
    distant_rows = TILE_BLOCK_ROWS // 4

    def one_tile(tile_index):
        tile_row = tile_index // IMAGE_TILE_COLS
        tile_col = (tile_index % IMAGE_TILE_COLS).astype(jnp.int32)
        first_row = (tile_row * TILE_BLOCK_ROWS).astype(jnp.int32)
        zero_index = jnp.zeros((), jnp.int32)
        query_tile = lax.dynamic_slice(queries, (first_row, tile_col, zero_index, zero_index), (TILE_BLOCK_ROWS, 1, BLOCK, DA)).reshape(TILE_BLOCK_ROWS * BLOCK, DA)
        own_blocks = lax.dynamic_slice(stacked, (zero_index, first_row, tile_col, zero_index, zero_index), (2, TILE_BLOCK_ROWS, 1, BLOCK, DA)).reshape(2, TILE_BLOCK_ROWS, BLOCK, DA)
        cycle_entry = cycle_list[tile_row, tile_col]
        cycle_row = jnp.where(cycle_entry == 0, -1, jnp.where(cycle_entry == 1, TILE_BLOCK_ROWS, jnp.where(cycle_entry < TILE_BLOCK_ROWS + 2, cycle_entry - 2, cycle_entry - 2 - TILE_BLOCK_ROWS)))
        cycle_col = jnp.where(cycle_entry < 2, 0, jnp.where(cycle_entry < TILE_BLOCK_ROWS + 2, -1, 1))
        source_row = jnp.clip(first_row + cycle_row, 0, GR - 1).astype(jnp.int32)
        source_col = jnp.clip(tile_col + cycle_col, 0, GC - 1).astype(jnp.int32)
        cycle_blocks = stacked[:, source_row, source_col]
        dilated_entry = dilated_list[tile_row, tile_col]
        hop_count = dilated_entry // distant_rows + 1
        row_place = dilated_entry % distant_rows
        far_col = ((tile_col + hop_count * step_spacing) % IMAGE_TILE_COLS).astype(jnp.int32)
        far_row = (first_row + 4 * row_place).astype(jnp.int32)
        dilated_blocks = stacked[:, far_row, far_col]
        key_values = jnp.concatenate([own_blocks, cycle_blocks, dilated_blocks], axis=1).reshape(2, -1, DA)
        return attend(query_tile, key_values[0], key_values[1])

    tiles = lax.map(one_tile, jnp.arange(TILE_ROWS * IMAGE_TILE_COLS, dtype=jnp.int32))
    return tiles.reshape(TILE_ROWS, IMAGE_TILE_COLS, TILE_BLOCK_ROWS, BLOCK, DA).transpose(0, 2, 1, 3, 4).reshape(GR, GC, BLOCK, DA)
```

```python
import jax
import jax.numpy as jnp
from jax import lax
from jax.experimental import pallas as pl
from jax.experimental.pallas import tpu as pltpu
from jax.sharding import PartitionSpec as P

HEAD_DIM = 128
DILATION_TILES = 8


def dequant(mantissa, exponent):
    tile_rows, tile_cols, block_length, feature_channel_width = mantissa.shape
    groups = exponent.shape[2]
    factor = jnp.exp2(exponent.astype(jnp.float32))[:, :, :, None, :]
    scaled = (
        mantissa.reshape(
            tile_rows, tile_cols, groups, block_length // groups, feature_channel_width
        ).astype(jnp.float32)
        * factor
    )
    return scaled.reshape(mantissa.shape).astype(jnp.bfloat16)


def shift(x, axis, count, step):
    if step > 0:
        pairs = [(i, i + step) for i in range(count - step)]
    else:
        pairs = [(i - step, i) for i in range(count + step)]
    if not pairs:
        return jnp.zeros_like(x)
    return lax.ppermute(x, axis, pairs)


def side_slots(entries, low, tile_blocks, cap):
    inside = (entries >= low) & (entries < low + tile_blocks)
    rank = jnp.cumsum(inside.astype(jnp.int32)) - 1
    slot = jnp.arange(cap, dtype=jnp.int32)[:, None]
    hit = inside[None, :] & (rank[None, :] == slot)
    return jnp.sum(jnp.where(hit, entries[None, :] - low, 0), axis=1), inside, rank


def attention_kernel(q_ref, k_ref, v_ref, o_ref):
    scores = lax.dot_general(
        q_ref[...], k_ref[...], (((1,), (1,)), ((), ())), preferred_element_type=jnp.float32
    ) * HEAD_DIM ** (-0.5)
    row_max = jnp.max(scores, axis=1, keepdims=True)
    weights = jnp.exp(scores - row_max)
    row_total = jnp.sum(weights, axis=1, keepdims=True)
    rounded = weights.astype(jnp.bfloat16)
    blended = jnp.dot(rounded, v_ref[...], preferred_element_type=jnp.float32)
    o_ref[...] = (blended / row_total).astype(o_ref.dtype)


def attend(query_rows, key_values):
    token_count, width = query_rows.shape
    key_count = key_values.shape[1]
    heads = width // HEAD_DIM
    return pl.pallas_call(
        attention_kernel,
        out_shape=jax.ShapeDtypeStruct((token_count, width), jnp.bfloat16),
        grid=(heads,),
        in_specs=[
            pl.BlockSpec((token_count, HEAD_DIM), lambda h: (0, h)),
            pl.BlockSpec((None, key_count, HEAD_DIM), lambda h: (0, 0, h)),
            pl.BlockSpec((None, key_count, HEAD_DIM), lambda h: (1, 0, h)),
        ],
        out_specs=pl.BlockSpec((token_count, HEAD_DIM), lambda h: (0, h)),
        cost_estimate=pl.CostEstimate(
            flops=4 * token_count * key_count * width,
            transcendentals=token_count * key_count * heads,
            bytes_accessed=2 * (2 * token_count * width + 2 * key_count * width),
        ),
    )(query_rows, key_values, key_values)


def per_device(queries, key_mant, key_exp, value_mant, value_exp, cycle_list, dilated_list):
    tile_blocks = queries.shape[0]
    block_length = queries.shape[2]
    width = queries.shape[3]
    col_count = lax.axis_size("col")
    row_count = lax.axis_size("row")
    distant_rows = tile_blocks // 4
    step_spacing = col_count // DILATION_TILES
    me_col = lax.axis_index("col")

    stacked = jnp.stack([dequant(key_mant, key_exp), dequant(value_mant, value_exp)])[:, :, 0]

    above = shift(stacked[:, tile_blocks - 1], "row", row_count, 1)
    below = shift(stacked[:, 0], "row", row_count, -1)

    cap = 3 if row_count >= 2 else 4
    cap = min(cap, tile_blocks)
    entries = cycle_list[0, 0]
    right_entries = shift(entries, "col", col_count, -1)
    left_entries = shift(entries, "col", col_count, 1)
    to_right, _, _ = side_slots(right_entries, 2, tile_blocks, cap)
    to_left, _, _ = side_slots(left_entries, 2 + tile_blocks, tile_blocks, cap)
    from_left = shift(jnp.take(stacked, to_right, axis=1), "col", col_count, 1)
    from_right = shift(jnp.take(stacked, to_left, axis=1), "col", col_count, -1)

    _, is_left, left_rank = side_slots(entries, 2, tile_blocks, cap)
    _, is_right, right_rank = side_slots(entries, 2 + tile_blocks, tile_blocks, cap)
    pool_index = jnp.where(
        entries == 0,
        0,
        jnp.where(entries == 1, 1, jnp.where(is_left, 2 + left_rank, 2 + cap + right_rank)),
    )
    pool = jnp.concatenate([above[:, None], below[:, None], from_left, from_right], axis=1)
    cycle_blocks = jnp.take(pool, pool_index, axis=1)

    far_source = stacked[:, 0::4]
    dilated_entries = dilated_list[0, 0]
    if step_spacing == 1:
        gathered = lax.all_gather(far_source, "col", axis=1)
        source_col = (me_col + dilated_entries // distant_rows + 1) % col_count
        dilated_index = source_col * distant_rows + dilated_entries % distant_rows
        dilated_pool = gathered.reshape(2, col_count * distant_rows, block_length, width)
    else:
        hop_tiles = []
        for hop in range(1, DILATION_TILES):
            distance = hop * step_spacing
            route = [((i + distance) % col_count, i) for i in range(col_count)]
            hop_tiles.append(lax.ppermute(far_source, "col", route))
        dilated_index = dilated_entries
        dilated_pool = jnp.stack(hop_tiles, axis=1).reshape(
            2, (DILATION_TILES - 1) * distant_rows, block_length, width
        )
    dilated_blocks = jnp.take(dilated_pool, dilated_index, axis=1)

    key_values = jnp.concatenate([stacked, cycle_blocks, dilated_blocks], axis=1)
    key_values = key_values.reshape(2, -1, width)
    token_count = tile_blocks * block_length
    result = attend(queries.reshape(token_count, width), key_values)
    return result.reshape(queries.shape)


def solution(mesh):
    in_specs = (
        P(("groups", "row"), "col", None, None),
        P(("groups", "row"), "col", None, None),
        P(("groups", "row"), "col", None, None),
        P(("groups", "row"), "col", None, None),
        P(("groups", "row"), "col", None, None),
        P(("groups", "row"), "col", None),
        P(("groups", "row"), "col", None),
    )
    out_specs = P(("groups", "row"), "col", None, None)
    return jax.shard_map(
        per_device, mesh=mesh, in_specs=in_specs, out_specs=out_specs, check_vma=False
    )
```

```python
import jax
import jax.numpy as jnp
from jax import lax
from jax.experimental import pallas as pl
from jax.experimental.pallas import tpu as pltpu
from jax.sharding import PartitionSpec as P

HEAD_DIM = 128
DILATION_TILES = 8


def dequant(mantissa, exponent):
    tile_rows, tile_cols, block_length, feature_channel_width = mantissa.shape
    groups = exponent.shape[2]
    factor = jnp.exp2(exponent.astype(jnp.float32))[:, :, :, None, :]
    scaled = (
        mantissa.reshape(
            tile_rows, tile_cols, groups, block_length // groups, feature_channel_width
        ).astype(jnp.float32)
        * factor
    )
    return scaled.reshape(mantissa.shape).astype(jnp.bfloat16)


def shift(x, axis, count, step):
    if step > 0:
        pairs = [(i, i + step) for i in range(count - step)]
    else:
        pairs = [(i - step, i) for i in range(count + step)]
    if not pairs:
        return jnp.zeros_like(x)
    return lax.ppermute(x, axis, pairs)


def side_slots(entries, low, tile_blocks, cap):
    inside = (entries >= low) & (entries < low + tile_blocks)
    rank = jnp.cumsum(inside.astype(jnp.int32)) - 1
    slot = jnp.arange(cap, dtype=jnp.int32)[:, None]
    hit = inside[None, :] & (rank[None, :] == slot)
    return jnp.sum(jnp.where(hit, entries[None, :] - low, 0), axis=1), inside, rank


def ring_gather(item, count, me):
    order = list(range(0, count, 2)) + list(range(count - 1 - count % 2, 0, -2))
    position = [0] * count
    for place, col in enumerate(order):
        position[col] = place
    forward = [(order[i], order[(i + 1) % count]) for i in range(count)]
    backward = [(order[(i + 1) % count], order[i]) for i in range(count)]
    half = count // 2
    rows = item.shape[1]
    split = (rows + 1) // 2
    ahead, behind = item, item
    slots = [None] * (count - 1)
    for distance in range(1, half + 1):
        if distance == half and count % 2 == 0:
            first = lax.ppermute(ahead[:, :split], "col", forward)
            parts = [first]
            if split < rows:
                parts.append(lax.ppermute(behind[:, split:], "col", backward))
            slots[distance - 1] = jnp.concatenate(parts, axis=1) if len(parts) > 1 else first
            continue
        ahead = lax.ppermute(ahead, "col", forward)
        slots[distance - 1] = ahead
        behind = lax.ppermute(behind, "col", backward)
        slots[count - distance - 1] = behind
    pool = jnp.concatenate(slots, axis=1)
    table = jnp.array(position, dtype=jnp.int32)

    def source_slot(col):
        return (table[me] - table[col]) % count - 1

    return pool, source_slot


def attention_kernel(q_ref, k_ref, v_ref, o_ref):
    scores = lax.dot_general(
        q_ref[...], k_ref[...], (((1,), (1,)), ((), ())), preferred_element_type=jnp.float32
    ) * HEAD_DIM ** (-0.5)
    row_max = jnp.max(scores, axis=1, keepdims=True)
    weights = jnp.exp(scores - row_max)
    row_total = jnp.sum(weights, axis=1, keepdims=True)
    rounded = weights.astype(jnp.bfloat16)
    blended = jnp.dot(rounded, v_ref[...], preferred_element_type=jnp.float32)
    o_ref[...] = (blended / row_total).astype(o_ref.dtype)


def attend(query_rows, key_values):
    token_count, width = query_rows.shape
    key_count = key_values.shape[1]
    heads = width // HEAD_DIM
    return pl.pallas_call(
        attention_kernel,
        out_shape=jax.ShapeDtypeStruct((token_count, width), jnp.bfloat16),
        grid=(heads,),
        in_specs=[
            pl.BlockSpec((token_count, HEAD_DIM), lambda h: (0, h)),
            pl.BlockSpec((None, key_count, HEAD_DIM), lambda h: (0, 0, h)),
            pl.BlockSpec((None, key_count, HEAD_DIM), lambda h: (1, 0, h)),
        ],
        out_specs=pl.BlockSpec((token_count, HEAD_DIM), lambda h: (0, h)),
        cost_estimate=pl.CostEstimate(
            flops=4 * token_count * key_count * width,
            transcendentals=token_count * key_count * heads,
            bytes_accessed=2 * (2 * token_count * width + 2 * key_count * width),
        ),
    )(query_rows, key_values, key_values)


def per_device(queries, key_mant, key_exp, value_mant, value_exp, cycle_list, dilated_list):
    tile_blocks = queries.shape[0]
    block_length = queries.shape[2]
    width = queries.shape[3]
    col_count = lax.axis_size("col")
    row_count = lax.axis_size("row")
    distant_rows = tile_blocks // 4
    step_spacing = col_count // DILATION_TILES
    me_col = lax.axis_index("col")

    stacked = jnp.stack([dequant(key_mant, key_exp), dequant(value_mant, value_exp)])[:, :, 0]

    above = shift(stacked[:, tile_blocks - 1], "row", row_count, 1)
    below = shift(stacked[:, 0], "row", row_count, -1)

    edge_cap = min(3 if row_count >= 2 else 4, tile_blocks)
    main_cap = edge_cap - 1 if col_count >= 3 else edge_cap
    entries = cycle_list[0, 0]
    right_entries = shift(entries, "col", col_count, -1)
    left_entries = shift(entries, "col", col_count, 1)
    to_right, _, _ = side_slots(right_entries, 2, tile_blocks, edge_cap)
    to_left, _, _ = side_slots(left_entries, 2 + tile_blocks, tile_blocks, edge_cap)
    right_payload = jnp.take(stacked, to_right, axis=1)
    left_payload = jnp.take(stacked, to_left, axis=1)
    from_left = shift(right_payload[:, :main_cap], "col", col_count, 1)
    from_right = shift(left_payload[:, :main_cap], "col", col_count, -1)
    if main_cap < edge_cap:
        last = col_count - 1
        from_left = jnp.concatenate(
            [from_left, lax.ppermute(right_payload[:, main_cap:], "col", [(last - 1, last)])], axis=1
        )
        from_right = jnp.concatenate(
            [from_right, lax.ppermute(left_payload[:, main_cap:], "col", [(1, 0)])], axis=1
        )

    _, is_left, left_rank = side_slots(entries, 2, tile_blocks, edge_cap)
    _, is_right, right_rank = side_slots(entries, 2 + tile_blocks, tile_blocks, edge_cap)
    pool_index = jnp.where(
        entries == 0,
        0,
        jnp.where(entries == 1, 1, jnp.where(is_left, 2 + left_rank, 2 + edge_cap + right_rank)),
    )
    pool = jnp.concatenate([above[:, None], below[:, None], from_left, from_right], axis=1)
    cycle_blocks = jnp.take(pool, pool_index, axis=1)

    far_source = stacked[:, 0::4]
    dilated_entries = dilated_list[0, 0]
    if step_spacing == 1:
        dilated_pool, source_slot = ring_gather(far_source, col_count, me_col)
        source_col = (me_col + dilated_entries // distant_rows + 1) % col_count
        dilated_index = source_slot(source_col) * distant_rows + dilated_entries % distant_rows
    else:
        hop_tiles = []
        for hop in range(1, DILATION_TILES):
            distance = hop * step_spacing
            route = [((i + distance) % col_count, i) for i in range(col_count)]
            hop_tiles.append(lax.ppermute(far_source, "col", route))
        dilated_index = dilated_entries
        dilated_pool = jnp.stack(hop_tiles, axis=1).reshape(
            2, (DILATION_TILES - 1) * distant_rows, block_length, width
        )
    dilated_blocks = jnp.take(dilated_pool, dilated_index, axis=1)

    key_values = jnp.concatenate([stacked, cycle_blocks, dilated_blocks], axis=1)
    key_values = key_values.reshape(2, -1, width)
    token_count = tile_blocks * block_length
    result = attend(queries.reshape(token_count, width), key_values)
    return result.reshape(queries.shape)


def solution(mesh):
    in_specs = (
        P(("groups", "row"), "col", None, None),
        P(("groups", "row"), "col", None, None),
        P(("groups", "row"), "col", None, None),
        P(("groups", "row"), "col", None, None),
        P(("groups", "row"), "col", None, None),
        P(("groups", "row"), "col", None),
        P(("groups", "row"), "col", None),
    )
    out_specs = P(("groups", "row"), "col", None, None)
    return jax.shard_map(
        per_device, mesh=mesh, in_specs=in_specs, out_specs=out_specs, check_vma=False
    )
```

```python
import functools

import jax
import jax.numpy as jnp
from jax import lax
from jax.experimental import pallas as pl
from jax.experimental.pallas import tpu as pltpu
from jax.sharding import PartitionSpec as P

HEAD_DIM = 128
DILATION_TILES = 8


def dequant(mantissa, exponent):
    tile_rows, tile_cols, block_length, feature_channel_width = mantissa.shape
    groups = exponent.shape[2]
    factor = jnp.exp2(exponent.astype(jnp.float32))[:, :, :, None, :]
    scaled = (
        mantissa.reshape(
            tile_rows, tile_cols, groups, block_length // groups, feature_channel_width
        ).astype(jnp.float32)
        * factor
    )
    return scaled.reshape(mantissa.shape).astype(jnp.bfloat16)


def shift(x, axis, count, step):
    if step > 0:
        pairs = [(i, i + step) for i in range(count - step)]
    else:
        pairs = [(i - step, i) for i in range(count + step)]
    if not pairs:
        return jnp.zeros_like(x)
    return lax.ppermute(x, axis, pairs)


def side_slots(entries, low, tile_blocks, cap):
    inside = (entries >= low) & (entries < low + tile_blocks)
    rank = jnp.cumsum(inside.astype(jnp.int32)) - 1
    slot = jnp.arange(cap, dtype=jnp.int32)[:, None]
    hit = inside[None, :] & (rank[None, :] == slot)
    return jnp.sum(jnp.where(hit, entries[None, :] - low, 0), axis=1), inside, rank


def ring_gather(item, count, me):
    order = list(range(0, count, 2)) + list(range(count - 1 - count % 2, 0, -2))
    position = [0] * count
    for place, col in enumerate(order):
        position[col] = place
    forward = [(order[i], order[(i + 1) % count]) for i in range(count)]
    backward = [(order[(i + 1) % count], order[i]) for i in range(count)]
    half = count // 2
    rows = item.shape[1]
    split = (rows + 1) // 2
    ahead, behind = item, item
    arrays = []
    lookup = [None] * (count - 1)
    for distance in range(1, half + 1):
        if distance == half and count % 2 == 0:
            arrays.append(lax.ppermute(ahead[:, :split], "col", forward))
            first = len(arrays) - 1
            if split < rows:
                arrays.append(lax.ppermute(behind[:, split:], "col", backward))
            lookup[distance - 1] = [
                (first, r) if r < split else (first + 1, r - split) for r in range(rows)
            ]
            continue
        ahead = lax.ppermute(ahead, "col", forward)
        arrays.append(ahead)
        lookup[distance - 1] = [(len(arrays) - 1, r) for r in range(rows)]
        behind = lax.ppermute(behind, "col", backward)
        arrays.append(behind)
        lookup[count - distance - 1] = [(len(arrays) - 1, r) for r in range(rows)]
    table = jnp.array(position, dtype=jnp.int32)

    def relative(col):
        return (table[me] - table[col]) % count - 1

    return arrays, lookup, relative


def gather_attention_kernel(cycle_sources, far_sources, table_ref, q_hbm, own_hbm, *rest):
    sources = rest[: cycle_sources + far_sources]
    o_ref, q_vmem, k_vmem, v_vmem, sems = rest[cycle_sources + far_sources :]
    tile_blocks = own_hbm.shape[1]
    block_length = own_hbm.shape[2]
    extra = table_ref.shape[0] // 2
    heads = q_vmem.shape[1] // HEAD_DIM

    copies = [pltpu.make_async_copy(q_hbm, q_vmem, sems.at[0, 0])]
    copies.append(pltpu.make_async_copy(own_hbm.at[0], k_vmem.at[pl.ds(0, tile_blocks)], sems.at[0, 1]))
    copies.append(pltpu.make_async_copy(own_hbm.at[1], v_vmem.at[pl.ds(0, tile_blocks)], sems.at[1, 1]))
    for c in copies:
        c.start()
    for slot in range(extra):
        src = table_ref[2 * slot]
        index = table_ref[2 * slot + 1]
        lo, hi = (0, cycle_sources) if slot < extra // 2 else (cycle_sources, cycle_sources + far_sources)
        for cand in range(lo, hi):
            @pl.when(src == cand)
            def _():
                for kv, dst in ((0, k_vmem), (1, v_vmem)):
                    pltpu.make_async_copy(
                        sources[cand].at[kv, index], dst.at[tile_blocks + slot], sems.at[kv, 2 + slot]
                    ).start()
    for c in copies:
        c.wait()
    for slot in range(extra):
        for kv, dst in ((0, k_vmem), (1, v_vmem)):
            pltpu.make_async_copy(
                own_hbm.at[kv, 0], dst.at[tile_blocks + slot], sems.at[kv, 2 + slot]
            ).wait()

    key_count = k_vmem.shape[0] * block_length

    def head(h, carry):
        lanes = pl.ds(pl.multiple_of(h * HEAD_DIM, HEAD_DIM), HEAD_DIM)
        q = q_vmem[:, lanes]
        k = k_vmem[:, :, lanes].reshape(key_count, HEAD_DIM)
        v = v_vmem[:, :, lanes].reshape(key_count, HEAD_DIM)
        scores = lax.dot_general(
            q, k, (((1,), (1,)), ((), ())), preferred_element_type=jnp.float32
        ) * HEAD_DIM ** (-0.5)
        row_max = jnp.max(scores, axis=1, keepdims=True)
        weights = jnp.exp(scores - row_max)
        row_total = jnp.sum(weights, axis=1, keepdims=True)
        rounded = weights.astype(jnp.bfloat16)
        blended = jnp.dot(rounded, v, preferred_element_type=jnp.float32)
        o_ref[:, lanes] = (blended / row_total).astype(o_ref.dtype)
        return carry

    lax.fori_loop(0, heads, head, 0)


def gather_attend(query_rows, own, cycle_list_sources, far_list_sources, table):
    token_count, width = query_rows.shape
    tile_blocks, block_length = own.shape[1], own.shape[2]
    extra = table.shape[0] // 2
    blocks = tile_blocks + extra
    key_count = blocks * block_length
    heads = width // HEAD_DIM
    n_sources = len(cycle_list_sources) + len(far_list_sources)
    kernel = functools.partial(
        gather_attention_kernel, len(cycle_list_sources), len(far_list_sources)
    )
    return pl.pallas_call(
        kernel,
        out_shape=jax.ShapeDtypeStruct((token_count, width), jnp.bfloat16),
        in_specs=[pl.BlockSpec(memory_space=pltpu.SMEM)]
        + [pl.BlockSpec(memory_space=pl.ANY)] * (2 + n_sources),
        out_specs=pl.BlockSpec(memory_space=pltpu.VMEM),
        scratch_shapes=[
            pltpu.VMEM((token_count, width), jnp.bfloat16),
            pltpu.VMEM((blocks, block_length, width), jnp.bfloat16),
            pltpu.VMEM((blocks, block_length, width), jnp.bfloat16),
            pltpu.SemaphoreType.DMA((2, 2 + extra)),
        ],
        compiler_params=pltpu.CompilerParams(vmem_limit_bytes=48 * 1024 * 1024),
        cost_estimate=pl.CostEstimate(
            flops=4 * token_count * key_count * width,
            transcendentals=token_count * key_count * heads,
            bytes_accessed=2 * (2 * token_count * width + 2 * key_count * width),
        ),
    )(table, query_rows, own, *cycle_list_sources, *far_list_sources)


def per_device(queries, key_mant, key_exp, value_mant, value_exp, cycle_list, dilated_list):
    tile_blocks = queries.shape[0]
    block_length = queries.shape[2]
    width = queries.shape[3]
    col_count = lax.axis_size("col")
    row_count = lax.axis_size("row")
    distant_rows = tile_blocks // 4
    step_spacing = col_count // DILATION_TILES
    me_col = lax.axis_index("col")

    stacked = jnp.stack([dequant(key_mant, key_exp), dequant(value_mant, value_exp)])[:, :, 0]

    above = shift(stacked[:, tile_blocks - 1 :], "row", row_count, 1)
    below = shift(stacked[:, :1], "row", row_count, -1)

    edge_cap = min(3 if row_count >= 2 else 4, tile_blocks)
    main_cap = edge_cap - 1 if col_count >= 3 else edge_cap
    entries = cycle_list[0, 0]
    right_entries = shift(entries, "col", col_count, -1)
    left_entries = shift(entries, "col", col_count, 1)
    to_right, _, _ = side_slots(right_entries, 2, tile_blocks, edge_cap)
    to_left, _, _ = side_slots(left_entries, 2 + tile_blocks, tile_blocks, edge_cap)
    right_payload = jnp.take(stacked, to_right, axis=1)
    left_payload = jnp.take(stacked, to_left, axis=1)
    cycle_sources = [above, below]
    cycle_sources.append(shift(right_payload[:, :main_cap], "col", col_count, 1))
    cycle_sources.append(shift(left_payload[:, :main_cap], "col", col_count, -1))
    if main_cap < edge_cap:
        last = col_count - 1
        cycle_sources.append(lax.ppermute(right_payload[:, main_cap:], "col", [(last - 1, last)]))
        cycle_sources.append(lax.ppermute(left_payload[:, main_cap:], "col", [(1, 0)]))

    _, is_left, left_rank = side_slots(entries, 2, tile_blocks, edge_cap)
    _, is_right, right_rank = side_slots(entries, 2 + tile_blocks, tile_blocks, edge_cap)
    side_rank = jnp.where(is_left, left_rank, right_rank)
    overflow = side_rank >= main_cap
    cycle_src = jnp.where(
        entries == 0,
        0,
        jnp.where(entries == 1, 1, 2 + is_right.astype(jnp.int32) + 2 * overflow.astype(jnp.int32)),
    )
    cycle_idx = jnp.where(entries < 2, 0, jnp.where(overflow, side_rank - main_cap, side_rank))

    far_source = stacked[:, 0::4]
    dilated_entries = dilated_list[0, 0]
    hop_slot = dilated_entries // distant_rows
    far_row = dilated_entries % distant_rows
    if step_spacing == 1:
        far_sources, lookup, relative = ring_gather(far_source, col_count, me_col)
        hop_slot = relative((me_col + hop_slot + 1) % col_count)
    else:
        far_sources = []
        lookup = []
        for hop in range(1, DILATION_TILES):
            distance = hop * step_spacing
            route = [((i + distance) % col_count, i) for i in range(col_count)]
            far_sources.append(lax.ppermute(far_source, "col", route))
            lookup.append([(hop - 1, r) for r in range(distant_rows)])
    lookup_src = jnp.array([[a for a, _ in row] for row in lookup], dtype=jnp.int32)
    lookup_idx = jnp.array([[b for _, b in row] for row in lookup], dtype=jnp.int32)
    far_src = len(cycle_sources) + lookup_src[hop_slot, far_row]
    far_idx = lookup_idx[hop_slot, far_row]

    table = jnp.stack(
        [jnp.concatenate([cycle_src, far_src]), jnp.concatenate([cycle_idx, far_idx])], axis=1
    ).reshape(-1)
    token_count = tile_blocks * block_length
    result = gather_attend(
        queries.reshape(token_count, width), stacked, cycle_sources, far_sources, table
    )
    return result.reshape(queries.shape)


def solution(mesh):
    in_specs = (
        P(("groups", "row"), "col", None, None),
        P(("groups", "row"), "col", None, None),
        P(("groups", "row"), "col", None, None),
        P(("groups", "row"), "col", None, None),
        P(("groups", "row"), "col", None, None),
        P(("groups", "row"), "col", None),
        P(("groups", "row"), "col", None),
    )
    out_specs = P(("groups", "row"), "col", None, None)
    return jax.shard_map(
        per_device, mesh=mesh, in_specs=in_specs, out_specs=out_specs, check_vma=False
    )
```

```python
import functools

import jax
import jax.numpy as jnp
from jax import lax
from jax.experimental import pallas as pl
from jax.experimental.pallas import tpu as pltpu
from jax.sharding import PartitionSpec as P

HEAD_DIM = 128
DILATION_TILES = 8


def dequant(mantissa, exponent):
    tile_rows, tile_cols, block_length, feature_channel_width = mantissa.shape
    groups = exponent.shape[2]
    factor = jnp.exp2(exponent.astype(jnp.float32))[:, :, :, None, :]
    scaled = (
        mantissa.reshape(
            tile_rows, tile_cols, groups, block_length // groups, feature_channel_width
        ).astype(jnp.float32)
        * factor
    )
    return scaled.reshape(mantissa.shape).astype(jnp.bfloat16)


def shift(x, axis, count, step):
    if step > 0:
        pairs = [(i, i + step) for i in range(count - step)]
    else:
        pairs = [(i - step, i) for i in range(count + step)]
    if not pairs:
        return jnp.zeros_like(x)
    return lax.ppermute(x, axis, pairs)


def side_slots(entries, low, tile_blocks, cap):
    inside = (entries >= low) & (entries < low + tile_blocks)
    rank = jnp.cumsum(inside.astype(jnp.int32)) - 1
    slot = jnp.arange(cap, dtype=jnp.int32)[:, None]
    hit = inside[None, :] & (rank[None, :] == slot)
    return jnp.sum(jnp.where(hit, entries[None, :] - low, 0), axis=1), inside, rank


def ring_gather(item, count, me):
    order = list(range(0, count, 2)) + list(range(count - 1 - count % 2, 0, -2))
    position = [0] * count
    for place, col in enumerate(order):
        position[col] = place
    forward = [(order[i], order[(i + 1) % count]) for i in range(count)]
    backward = [(order[(i + 1) % count], order[i]) for i in range(count)]
    half = count // 2
    rows = item.shape[1]
    split = (rows + 1) // 2
    ahead, behind = item, item
    arrays = []
    lookup = [None] * (count - 1)
    for distance in range(1, half + 1):
        if distance == half and count % 2 == 0:
            arrays.append(lax.ppermute(ahead[:, :split], "col", forward))
            first = len(arrays) - 1
            if split < rows:
                arrays.append(lax.ppermute(behind[:, split:], "col", backward))
            lookup[distance - 1] = [
                (first, r) if r < split else (first + 1, r - split) for r in range(rows)
            ]
            continue
        ahead = lax.ppermute(ahead, "col", forward)
        arrays.append(ahead)
        lookup[distance - 1] = [(len(arrays) - 1, r) for r in range(rows)]
        behind = lax.ppermute(behind, "col", backward)
        arrays.append(behind)
        lookup[count - distance - 1] = [(len(arrays) - 1, r) for r in range(rows)]
    table = jnp.array(position, dtype=jnp.int32)

    def relative(col):
        return (table[me] - table[col]) % count - 1

    return arrays, lookup, relative


def own_attention_kernel(q_ref, k_ref, v_ref, acc_ref, max_ref, total_ref):
    scores = lax.dot_general(
        q_ref[...], k_ref[...], (((1,), (1,)), ((), ())), preferred_element_type=jnp.float32
    ) * HEAD_DIM ** (-0.5)
    row_max = jnp.max(scores, axis=1, keepdims=True)
    weights = jnp.exp(scores - row_max)
    max_ref[...] = row_max
    total_ref[...] = jnp.sum(weights, axis=1, keepdims=True)
    acc_ref[...] = jnp.dot(
        weights.astype(jnp.bfloat16), v_ref[...], preferred_element_type=jnp.float32
    )


def own_attend(query_rows, own):
    token_count, width = query_rows.shape
    key_count = own.shape[1] * own.shape[2]
    heads = width // HEAD_DIM
    key_values = own.reshape(2, key_count, width)
    return pl.pallas_call(
        own_attention_kernel,
        out_shape=(
            jax.ShapeDtypeStruct((token_count, width), jnp.float32),
            jax.ShapeDtypeStruct((heads, token_count, 1), jnp.float32),
            jax.ShapeDtypeStruct((heads, token_count, 1), jnp.float32),
        ),
        grid=(heads,),
        in_specs=[
            pl.BlockSpec((token_count, HEAD_DIM), lambda h: (0, h)),
            pl.BlockSpec((None, key_count, HEAD_DIM), lambda h: (0, 0, h)),
            pl.BlockSpec((None, key_count, HEAD_DIM), lambda h: (1, 0, h)),
        ],
        out_specs=(
            pl.BlockSpec((token_count, HEAD_DIM), lambda h: (0, h)),
            pl.BlockSpec((None, token_count, 1), lambda h: (h, 0, 0)),
            pl.BlockSpec((None, token_count, 1), lambda h: (h, 0, 0)),
        ),
        cost_estimate=pl.CostEstimate(
            flops=4 * token_count * key_count * width,
            transcendentals=token_count * key_count * heads,
            bytes_accessed=2 * token_count * width + 4 * key_count * width + 4 * token_count * width,
        ),
    )(query_rows, key_values, key_values)


def gather_attention_kernel(
    cycle_sources, far_sources, table_ref, q_hbm, acc_ref, max_ref, total_ref, *rest
):
    sources = rest[: cycle_sources + far_sources]
    o_ref, q_vmem, k_vmem, v_vmem, sems = rest[cycle_sources + far_sources :]
    extra = table_ref.shape[0] // 2
    block_length = k_vmem.shape[1]
    heads = q_vmem.shape[1] // HEAD_DIM

    query_copy = pltpu.make_async_copy(q_hbm, q_vmem, sems.at[0, extra])
    query_copy.start()
    for slot in range(extra):
        src = table_ref[2 * slot]
        index = table_ref[2 * slot + 1]
        lo, hi = (0, cycle_sources) if slot < extra // 2 else (cycle_sources, cycle_sources + far_sources)
        for cand in range(lo, hi):
            @pl.when(src == cand)
            def _():
                for kv, dst in ((0, k_vmem), (1, v_vmem)):
                    pltpu.make_async_copy(
                        sources[cand].at[kv, index], dst.at[slot], sems.at[kv, slot]
                    ).start()
    query_copy.wait()
    for slot in range(extra):
        for kv, dst in ((0, k_vmem), (1, v_vmem)):
            pltpu.make_async_copy(sources[0].at[kv, 0], dst.at[slot], sems.at[kv, slot]).wait()

    key_count = extra * block_length

    def head(h, carry):
        lanes = pl.ds(pl.multiple_of(h * HEAD_DIM, HEAD_DIM), HEAD_DIM)
        q = q_vmem[:, lanes]
        k = k_vmem[:, :, lanes].reshape(key_count, HEAD_DIM)
        v = v_vmem[:, :, lanes].reshape(key_count, HEAD_DIM)
        scores = lax.dot_general(
            q, k, (((1,), (1,)), ((), ())), preferred_element_type=jnp.float32
        ) * HEAD_DIM ** (-0.5)
        own_max = max_ref[h]
        row_max = jnp.maximum(own_max, jnp.max(scores, axis=1, keepdims=True))
        weights = jnp.exp(scores - row_max)
        scale = jnp.exp(own_max - row_max)
        row_total = total_ref[h] * scale + jnp.sum(weights, axis=1, keepdims=True)
        blended = acc_ref[:, lanes] * scale + jnp.dot(
            weights.astype(jnp.bfloat16), v, preferred_element_type=jnp.float32
        )
        o_ref[:, lanes] = (blended / row_total).astype(o_ref.dtype)
        return carry

    lax.fori_loop(0, heads, head, 0)


def gather_attend(query_rows, partial, cycle_list_sources, far_list_sources, table):
    token_count, width = query_rows.shape
    block_length = cycle_list_sources[0].shape[2]
    extra = table.shape[0] // 2
    key_count = extra * block_length
    heads = width // HEAD_DIM
    n_sources = len(cycle_list_sources) + len(far_list_sources)
    kernel = functools.partial(
        gather_attention_kernel, len(cycle_list_sources), len(far_list_sources)
    )
    return pl.pallas_call(
        kernel,
        out_shape=jax.ShapeDtypeStruct((token_count, width), jnp.bfloat16),
        in_specs=[pl.BlockSpec(memory_space=pltpu.SMEM), pl.BlockSpec(memory_space=pl.ANY)]
        + [pl.BlockSpec(memory_space=pltpu.VMEM)] * 3
        + [pl.BlockSpec(memory_space=pl.ANY)] * n_sources,
        out_specs=pl.BlockSpec(memory_space=pltpu.VMEM),
        scratch_shapes=[
            pltpu.VMEM((token_count, width), jnp.bfloat16),
            pltpu.VMEM((extra, block_length, width), jnp.bfloat16),
            pltpu.VMEM((extra, block_length, width), jnp.bfloat16),
            pltpu.SemaphoreType.DMA((2, extra + 1)),
        ],
        compiler_params=pltpu.CompilerParams(vmem_limit_bytes=48 * 1024 * 1024),
        cost_estimate=pl.CostEstimate(
            flops=4 * token_count * key_count * width,
            transcendentals=token_count * key_count * heads,
            bytes_accessed=2 * token_count * width * 2 + 4 * key_count * width + 4 * token_count * width,
        ),
    )(table, query_rows, *partial, *cycle_list_sources, *far_list_sources)


def per_device(queries, key_mant, key_exp, value_mant, value_exp, cycle_list, dilated_list):
    tile_blocks = queries.shape[0]
    block_length = queries.shape[2]
    width = queries.shape[3]
    col_count = lax.axis_size("col")
    row_count = lax.axis_size("row")
    distant_rows = tile_blocks // 4
    step_spacing = col_count // DILATION_TILES
    me_col = lax.axis_index("col")

    stacked = jnp.stack([dequant(key_mant, key_exp), dequant(value_mant, value_exp)])[:, :, 0]

    above = shift(stacked[:, tile_blocks - 1 :], "row", row_count, 1)
    below = shift(stacked[:, :1], "row", row_count, -1)

    edge_cap = min(3 if row_count >= 2 else 4, tile_blocks)
    main_cap = edge_cap - 1 if col_count >= 3 else edge_cap
    entries = cycle_list[0, 0]
    right_entries = shift(entries, "col", col_count, -1)
    left_entries = shift(entries, "col", col_count, 1)
    to_right, _, _ = side_slots(right_entries, 2, tile_blocks, edge_cap)
    to_left, _, _ = side_slots(left_entries, 2 + tile_blocks, tile_blocks, edge_cap)
    right_payload = jnp.take(stacked, to_right, axis=1)
    left_payload = jnp.take(stacked, to_left, axis=1)
    cycle_sources = [above, below]
    cycle_sources.append(shift(right_payload[:, :main_cap], "col", col_count, 1))
    cycle_sources.append(shift(left_payload[:, :main_cap], "col", col_count, -1))
    if main_cap < edge_cap:
        last = col_count - 1
        cycle_sources.append(lax.ppermute(right_payload[:, main_cap:], "col", [(last - 1, last)]))
        cycle_sources.append(lax.ppermute(left_payload[:, main_cap:], "col", [(1, 0)]))

    _, is_left, left_rank = side_slots(entries, 2, tile_blocks, edge_cap)
    _, is_right, right_rank = side_slots(entries, 2 + tile_blocks, tile_blocks, edge_cap)
    side_rank = jnp.where(is_left, left_rank, right_rank)
    overflow = side_rank >= main_cap
    cycle_src = jnp.where(
        entries == 0,
        0,
        jnp.where(entries == 1, 1, 2 + is_right.astype(jnp.int32) + 2 * overflow.astype(jnp.int32)),
    )
    cycle_idx = jnp.where(entries < 2, 0, jnp.where(overflow, side_rank - main_cap, side_rank))

    far_source = stacked[:, 0::4]
    dilated_entries = dilated_list[0, 0]
    hop_slot = dilated_entries // distant_rows
    far_row = dilated_entries % distant_rows
    if step_spacing == 1:
        far_sources, lookup, relative = ring_gather(far_source, col_count, me_col)
        hop_slot = relative((me_col + hop_slot + 1) % col_count)
    else:
        far_sources = []
        lookup = []
        for hop in range(1, DILATION_TILES):
            distance = hop * step_spacing
            route = [((i + distance) % col_count, i) for i in range(col_count)]
            far_sources.append(lax.ppermute(far_source, "col", route))
            lookup.append([(hop - 1, r) for r in range(distant_rows)])
    lookup_src = jnp.array([[a for a, _ in row] for row in lookup], dtype=jnp.int32)
    lookup_idx = jnp.array([[b for _, b in row] for row in lookup], dtype=jnp.int32)
    far_src = len(cycle_sources) + lookup_src[hop_slot, far_row]
    far_idx = lookup_idx[hop_slot, far_row]

    table = jnp.stack(
        [jnp.concatenate([cycle_src, far_src]), jnp.concatenate([cycle_idx, far_idx])], axis=1
    ).reshape(-1)
    token_count = tile_blocks * block_length
    query_rows = queries.reshape(token_count, width)
    partial = own_attend(query_rows, stacked)
    result = gather_attend(query_rows, partial, cycle_sources, far_sources, table)
    return result.reshape(queries.shape)


def solution(mesh):
    in_specs = (
        P(("groups", "row"), "col", None, None),
        P(("groups", "row"), "col", None, None),
        P(("groups", "row"), "col", None, None),
        P(("groups", "row"), "col", None, None),
        P(("groups", "row"), "col", None, None),
        P(("groups", "row"), "col", None),
        P(("groups", "row"), "col", None),
    )
    out_specs = P(("groups", "row"), "col", None, None)
    return jax.shard_map(
        per_device, mesh=mesh, in_specs=in_specs, out_specs=out_specs, check_vma=False
    )
```

```python
import functools

import jax
import jax.numpy as jnp
from jax import lax
from jax.experimental import pallas as pl
from jax.experimental.pallas import tpu as pltpu
from jax.sharding import PartitionSpec as P

HEAD_DIM = 128
DILATION_TILES = 8


def dequant(mantissa, exponent):
    tile_rows, tile_cols, block_length, feature_channel_width = mantissa.shape
    groups = exponent.shape[2]
    factor = jnp.exp2(exponent.astype(jnp.float32))[:, :, :, None, :]
    scaled = (
        mantissa.reshape(
            tile_rows, tile_cols, groups, block_length // groups, feature_channel_width
        ).astype(jnp.float32)
        * factor
    )
    return scaled.reshape(mantissa.shape).astype(jnp.bfloat16)


def shift(x, axis, count, step):
    if step > 0:
        pairs = [(i, i + step) for i in range(count - step)]
    else:
        pairs = [(i - step, i) for i in range(count + step)]
    if not pairs:
        return jnp.zeros_like(x)
    return lax.ppermute(x, axis, pairs)


def side_slots(entries, low, tile_blocks, cap):
    inside = (entries >= low) & (entries < low + tile_blocks)
    rank = jnp.cumsum(inside.astype(jnp.int32)) - 1
    slot = jnp.arange(cap, dtype=jnp.int32)[:, None]
    hit = inside[None, :] & (rank[None, :] == slot)
    return jnp.sum(jnp.where(hit, entries[None, :] - low, 0), axis=1), inside, rank


def ring_gather(item, count, me):
    order = list(range(0, count, 2)) + list(range(count - 1 - count % 2, 0, -2))
    position = [0] * count
    for place, col in enumerate(order):
        position[col] = place
    forward = [(order[i], order[(i + 1) % count]) for i in range(count)]
    backward = [(order[(i + 1) % count], order[i]) for i in range(count)]
    half = count // 2
    rows = item.shape[1]
    split = (rows + 1) // 2
    arrays = []
    lookup = [[None] * rows for _ in range(count - 1)]
    for r in range(rows):
        ahead = behind = item[:, r : r + 1]
        for distance in range(1, half + 1):
            if distance == half and count % 2 == 0:
                if r < split:
                    arrays.append(lax.ppermute(ahead, "col", forward))
                else:
                    arrays.append(lax.ppermute(behind, "col", backward))
                lookup[distance - 1][r] = (len(arrays) - 1, 0)
                continue
            ahead = lax.ppermute(ahead, "col", forward)
            arrays.append(ahead)
            lookup[distance - 1][r] = (len(arrays) - 1, 0)
            behind = lax.ppermute(behind, "col", backward)
            arrays.append(behind)
            lookup[count - distance - 1][r] = (len(arrays) - 1, 0)
    table = jnp.array(position, dtype=jnp.int32)

    def relative(col):
        return (table[me] - table[col]) % count - 1

    return arrays, lookup, relative


def gather_attention_kernel(cycle_sources, far_sources, table_ref, q_hbm, own_hbm, *rest):
    sources = rest[: cycle_sources + far_sources]
    o_ref, q_vmem, k_vmem, v_vmem, sems = rest[cycle_sources + far_sources :]
    tile_blocks = own_hbm.shape[1]
    block_length = own_hbm.shape[2]
    extra = table_ref.shape[0] // 2
    heads = q_vmem.shape[1] // HEAD_DIM

    copies = [pltpu.make_async_copy(q_hbm, q_vmem, sems.at[0, 0])]
    copies.append(pltpu.make_async_copy(own_hbm.at[0], k_vmem.at[pl.ds(0, tile_blocks)], sems.at[0, 1]))
    copies.append(pltpu.make_async_copy(own_hbm.at[1], v_vmem.at[pl.ds(0, tile_blocks)], sems.at[1, 1]))
    for c in copies:
        c.start()
    for slot in range(extra):
        src = table_ref[2 * slot]
        index = table_ref[2 * slot + 1]
        lo, hi = (0, cycle_sources) if slot < extra // 2 else (cycle_sources, cycle_sources + far_sources)
        for cand in range(lo, hi):
            @pl.when(src == cand)
            def _():
                for kv, dst in ((0, k_vmem), (1, v_vmem)):
                    pltpu.make_async_copy(
                        sources[cand].at[kv, index], dst.at[tile_blocks + slot], sems.at[kv, 2 + slot]
                    ).start()
    for c in copies:
        c.wait()
    for slot in range(extra):
        for kv, dst in ((0, k_vmem), (1, v_vmem)):
            pltpu.make_async_copy(
                own_hbm.at[kv, 0], dst.at[tile_blocks + slot], sems.at[kv, 2 + slot]
            ).wait()

    key_count = k_vmem.shape[0] * block_length

    def head(h, carry):
        lanes = pl.ds(pl.multiple_of(h * HEAD_DIM, HEAD_DIM), HEAD_DIM)
        q = q_vmem[:, lanes]
        k = k_vmem[:, :, lanes].reshape(key_count, HEAD_DIM)
        v = v_vmem[:, :, lanes].reshape(key_count, HEAD_DIM)
        scores = lax.dot_general(
            q, k, (((1,), (1,)), ((), ())), preferred_element_type=jnp.float32
        ) * HEAD_DIM ** (-0.5)
        row_max = jnp.max(scores, axis=1, keepdims=True)
        weights = jnp.exp(scores - row_max)
        row_total = jnp.sum(weights, axis=1, keepdims=True)
        rounded = weights.astype(jnp.bfloat16)
        blended = jnp.dot(rounded, v, preferred_element_type=jnp.float32)
        o_ref[:, lanes] = (blended / row_total).astype(o_ref.dtype)
        return carry

    lax.fori_loop(0, heads, head, 0)


def gather_attend(query_rows, own, cycle_list_sources, far_list_sources, table):
    token_count, width = query_rows.shape
    tile_blocks, block_length = own.shape[1], own.shape[2]
    extra = table.shape[0] // 2
    blocks = tile_blocks + extra
    key_count = blocks * block_length
    heads = width // HEAD_DIM
    n_sources = len(cycle_list_sources) + len(far_list_sources)
    kernel = functools.partial(
        gather_attention_kernel, len(cycle_list_sources), len(far_list_sources)
    )
    return pl.pallas_call(
        kernel,
        out_shape=jax.ShapeDtypeStruct((token_count, width), jnp.bfloat16),
        in_specs=[pl.BlockSpec(memory_space=pltpu.SMEM)]
        + [pl.BlockSpec(memory_space=pl.ANY)] * (2 + n_sources),
        out_specs=pl.BlockSpec(memory_space=pltpu.VMEM),
        scratch_shapes=[
            pltpu.VMEM((token_count, width), jnp.bfloat16),
            pltpu.VMEM((blocks, block_length, width), jnp.bfloat16),
            pltpu.VMEM((blocks, block_length, width), jnp.bfloat16),
            pltpu.SemaphoreType.DMA((2, 2 + extra)),
        ],
        compiler_params=pltpu.CompilerParams(vmem_limit_bytes=48 * 1024 * 1024),
        cost_estimate=pl.CostEstimate(
            flops=4 * token_count * key_count * width,
            transcendentals=token_count * key_count * heads,
            bytes_accessed=2 * (2 * token_count * width + 2 * key_count * width),
        ),
    )(table, query_rows, own, *cycle_list_sources, *far_list_sources)


def per_device(queries, key_mant, key_exp, value_mant, value_exp, cycle_list, dilated_list):
    tile_blocks = queries.shape[0]
    block_length = queries.shape[2]
    width = queries.shape[3]
    col_count = lax.axis_size("col")
    row_count = lax.axis_size("row")
    distant_rows = tile_blocks // 4
    step_spacing = col_count // DILATION_TILES
    me_col = lax.axis_index("col")

    stacked = jnp.stack([dequant(key_mant, key_exp), dequant(value_mant, value_exp)])[:, :, 0]

    above = shift(stacked[:, tile_blocks - 1 :], "row", row_count, 1)
    below = shift(stacked[:, :1], "row", row_count, -1)

    edge_cap = min(3 if row_count >= 2 else 4, tile_blocks)
    main_cap = edge_cap - 1 if col_count >= 3 else edge_cap
    entries = cycle_list[0, 0]
    right_entries = shift(entries, "col", col_count, -1)
    left_entries = shift(entries, "col", col_count, 1)
    to_right, _, _ = side_slots(right_entries, 2, tile_blocks, edge_cap)
    to_left, _, _ = side_slots(left_entries, 2 + tile_blocks, tile_blocks, edge_cap)
    right_payload = jnp.take(stacked, to_right, axis=1)
    left_payload = jnp.take(stacked, to_left, axis=1)
    cycle_sources = [above, below]
    cycle_sources.append(shift(right_payload[:, :main_cap], "col", col_count, 1))
    cycle_sources.append(shift(left_payload[:, :main_cap], "col", col_count, -1))
    if main_cap < edge_cap:
        last = col_count - 1
        cycle_sources.append(lax.ppermute(right_payload[:, main_cap:], "col", [(last - 1, last)]))
        cycle_sources.append(lax.ppermute(left_payload[:, main_cap:], "col", [(1, 0)]))

    _, is_left, left_rank = side_slots(entries, 2, tile_blocks, edge_cap)
    _, is_right, right_rank = side_slots(entries, 2 + tile_blocks, tile_blocks, edge_cap)
    side_rank = jnp.where(is_left, left_rank, right_rank)
    overflow = side_rank >= main_cap
    cycle_src = jnp.where(
        entries == 0,
        0,
        jnp.where(entries == 1, 1, 2 + is_right.astype(jnp.int32) + 2 * overflow.astype(jnp.int32)),
    )
    cycle_idx = jnp.where(entries < 2, 0, jnp.where(overflow, side_rank - main_cap, side_rank))

    far_source = stacked[:, 0::4]
    dilated_entries = dilated_list[0, 0]
    hop_slot = dilated_entries // distant_rows
    far_row = dilated_entries % distant_rows
    if step_spacing == 1:
        far_sources, lookup, relative = ring_gather(far_source, col_count, me_col)
        hop_slot = relative((me_col + hop_slot + 1) % col_count)
    else:
        far_sources = []
        lookup = []
        for hop in range(1, DILATION_TILES):
            distance = hop * step_spacing
            route = [((i + distance) % col_count, i) for i in range(col_count)]
            far_sources.append(lax.ppermute(far_source, "col", route))
            lookup.append([(hop - 1, r) for r in range(distant_rows)])
    lookup_src = jnp.array([[a for a, _ in row] for row in lookup], dtype=jnp.int32)
    lookup_idx = jnp.array([[b for _, b in row] for row in lookup], dtype=jnp.int32)
    far_src = len(cycle_sources) + lookup_src[hop_slot, far_row]
    far_idx = lookup_idx[hop_slot, far_row]

    table = jnp.stack(
        [jnp.concatenate([cycle_src, far_src]), jnp.concatenate([cycle_idx, far_idx])], axis=1
    ).reshape(-1)
    token_count = tile_blocks * block_length
    result = gather_attend(
        queries.reshape(token_count, width), stacked, cycle_sources, far_sources, table
    )
    return result.reshape(queries.shape)


def solution(mesh):
    in_specs = (
        P(("groups", "row"), "col", None, None),
        P(("groups", "row"), "col", None, None),
        P(("groups", "row"), "col", None, None),
        P(("groups", "row"), "col", None, None),
        P(("groups", "row"), "col", None, None),
        P(("groups", "row"), "col", None),
        P(("groups", "row"), "col", None),
    )
    out_specs = P(("groups", "row"), "col", None, None)
    return jax.shard_map(
        per_device, mesh=mesh, in_specs=in_specs, out_specs=out_specs, check_vma=False
    )
```

```python
import functools

import jax
import jax.numpy as jnp
from jax import lax
from jax.experimental import pallas as pl
from jax.experimental.pallas import tpu as pltpu
from jax.sharding import PartitionSpec as P

HEAD_DIM = 128
DILATION_TILES = 8


def dequant(mantissa, exponent):
    tile_rows, tile_cols, block_length, feature_channel_width = mantissa.shape
    groups = exponent.shape[2]
    factor = jnp.exp2(exponent.astype(jnp.float32))[:, :, :, None, :]
    scaled = (
        mantissa.reshape(
            tile_rows, tile_cols, groups, block_length // groups, feature_channel_width
        ).astype(jnp.float32)
        * factor
    )
    return scaled.reshape(mantissa.shape).astype(jnp.bfloat16)


def shift(x, axis, count, step):
    if step > 0:
        pairs = [(i, i + step) for i in range(count - step)]
    else:
        pairs = [(i - step, i) for i in range(count + step)]
    if not pairs:
        return jnp.zeros_like(x)
    return lax.ppermute(x, axis, pairs)


def side_slots(entries, low, tile_blocks, cap):
    inside = (entries >= low) & (entries < low + tile_blocks)
    rank = jnp.cumsum(inside.astype(jnp.int32)) - 1
    slot = jnp.arange(cap, dtype=jnp.int32)[:, None]
    hit = inside[None, :] & (rank[None, :] == slot)
    return jnp.sum(jnp.where(hit, entries[None, :] - low, 0), axis=1), inside, rank


def ring_gather(item, count, me):
    order = list(range(0, count, 2)) + list(range(count - 1 - count % 2, 0, -2))
    position = [0] * count
    for place, col in enumerate(order):
        position[col] = place
    forward = [(order[i], order[(i + 1) % count]) for i in range(count)]
    backward = [(order[(i + 1) % count], order[i]) for i in range(count)]
    half = count // 2
    rows = item.shape[1]
    split = (rows + 1) // 2
    arrays = []
    lookup = [[None] * rows for _ in range(count - 1)]
    for r in range(rows):
        ahead = behind = item[:, r : r + 1]
        for distance in range(1, half + 1):
            if distance == half and count % 2 == 0:
                if r < split:
                    arrays.append(lax.ppermute(ahead, "col", forward))
                else:
                    arrays.append(lax.ppermute(behind, "col", backward))
                lookup[distance - 1][r] = (len(arrays) - 1, 0)
                continue
            ahead = lax.ppermute(ahead, "col", forward)
            arrays.append(ahead)
            lookup[distance - 1][r] = (len(arrays) - 1, 0)
            behind = lax.ppermute(behind, "col", backward)
            arrays.append(behind)
            lookup[count - distance - 1][r] = (len(arrays) - 1, 0)
    table = jnp.array(position, dtype=jnp.int32)

    def relative(col):
        return (table[me] - table[col]) % count - 1

    return arrays, lookup, relative


def own_attention_kernel(q_ref, k_ref, v_ref, acc_ref, max_ref, total_ref):
    scores = lax.dot_general(
        q_ref[...], k_ref[...], (((1,), (1,)), ((), ())), preferred_element_type=jnp.float32
    ) * HEAD_DIM ** (-0.5)
    row_max = jnp.max(scores, axis=1, keepdims=True)
    weights = jnp.exp(scores - row_max)
    max_ref[...] = row_max
    total_ref[...] = jnp.sum(weights, axis=1, keepdims=True)
    acc_ref[...] = jnp.dot(
        weights.astype(jnp.bfloat16), v_ref[...], preferred_element_type=jnp.float32
    )


def own_attend(query_rows, keys, values):
    token_count, width = query_rows.shape
    key_count = keys.shape[0]
    heads = width // HEAD_DIM
    return pl.pallas_call(
        own_attention_kernel,
        out_shape=(
            jax.ShapeDtypeStruct((token_count, width), jnp.float32),
            jax.ShapeDtypeStruct((heads, token_count, 1), jnp.float32),
            jax.ShapeDtypeStruct((heads, token_count, 1), jnp.float32),
        ),
        grid=(heads,),
        in_specs=[
            pl.BlockSpec((token_count, HEAD_DIM), lambda h: (0, h)),
            pl.BlockSpec((key_count, HEAD_DIM), lambda h: (0, h)),
            pl.BlockSpec((key_count, HEAD_DIM), lambda h: (0, h)),
        ],
        out_specs=(
            pl.BlockSpec((token_count, HEAD_DIM), lambda h: (0, h)),
            pl.BlockSpec((None, token_count, 1), lambda h: (h, 0, 0)),
            pl.BlockSpec((None, token_count, 1), lambda h: (h, 0, 0)),
        ),
        cost_estimate=pl.CostEstimate(
            flops=4 * token_count * key_count * width,
            transcendentals=token_count * key_count * heads,
            bytes_accessed=2 * token_count * width + 4 * key_count * width + 4 * token_count * width,
        ),
    )(query_rows, keys, values)


def gather_attention_kernel(
    cycle_sources, far_sources, table_ref, q_ref, acc_ref, max_ref, total_ref, *rest
):
    sources = rest[: cycle_sources + far_sources]
    o_ref, k_vmem, v_vmem, sems = rest[cycle_sources + far_sources :]
    extra = table_ref.shape[0] // 2
    block_length = k_vmem.shape[1]
    h = pl.program_id(0)

    @pl.when(h == 0)
    def _():
        for slot in range(extra):
            src = table_ref[2 * slot]
            index = table_ref[2 * slot + 1]
            lo, hi = (0, cycle_sources) if slot < extra // 2 else (cycle_sources, cycle_sources + far_sources)
            for cand in range(lo, hi):
                @pl.when(src == cand)
                def _():
                    for kv, dst in ((0, k_vmem), (1, v_vmem)):
                        pltpu.make_async_copy(
                            sources[cand].at[kv, index], dst.at[slot], sems.at[kv, slot]
                        ).start()
        for slot in range(extra):
            for kv, dst in ((0, k_vmem), (1, v_vmem)):
                pltpu.make_async_copy(sources[0].at[kv, 0], dst.at[slot], sems.at[kv, slot]).wait()

    key_count = extra * block_length
    lanes = pl.ds(pl.multiple_of(h * HEAD_DIM, HEAD_DIM), HEAD_DIM)
    k = k_vmem[:, :, lanes].reshape(key_count, HEAD_DIM)
    v = v_vmem[:, :, lanes].reshape(key_count, HEAD_DIM)
    scores = lax.dot_general(
        q_ref[...], k, (((1,), (1,)), ((), ())), preferred_element_type=jnp.float32
    ) * HEAD_DIM ** (-0.5)
    own_max = max_ref[...]
    row_max = jnp.maximum(own_max, jnp.max(scores, axis=1, keepdims=True))
    weights = jnp.exp(scores - row_max)
    scale = jnp.exp(own_max - row_max)
    row_total = total_ref[...] * scale + jnp.sum(weights, axis=1, keepdims=True)
    blended = acc_ref[...] * scale + jnp.dot(
        weights.astype(jnp.bfloat16), v, preferred_element_type=jnp.float32
    )
    o_ref[...] = (blended / row_total).astype(o_ref.dtype)


def gather_attend(query_rows, partial, cycle_list_sources, far_list_sources, table):
    token_count, width = query_rows.shape
    block_length = cycle_list_sources[0].shape[2]
    extra = table.shape[0] // 2
    key_count = extra * block_length
    heads = width // HEAD_DIM
    n_sources = len(cycle_list_sources) + len(far_list_sources)
    kernel = functools.partial(
        gather_attention_kernel, len(cycle_list_sources), len(far_list_sources)
    )
    column = pl.BlockSpec((token_count, HEAD_DIM), lambda h, t: (0, h))
    per_head = pl.BlockSpec((None, token_count, 1), lambda h, t: (h, 0, 0))
    return pl.pallas_call(
        kernel,
        out_shape=jax.ShapeDtypeStruct((token_count, width), jnp.bfloat16),
        grid_spec=pltpu.PrefetchScalarGridSpec(
            num_scalar_prefetch=1,
            grid=(heads,),
            in_specs=[column, column, per_head, per_head]
            + [pl.BlockSpec(memory_space=pl.ANY)] * n_sources,
            out_specs=column,
            scratch_shapes=[
                pltpu.VMEM((extra, block_length, width), jnp.bfloat16),
                pltpu.VMEM((extra, block_length, width), jnp.bfloat16),
                pltpu.SemaphoreType.DMA((2, extra)),
            ],
        ),
        cost_estimate=pl.CostEstimate(
            flops=4 * token_count * key_count * width,
            transcendentals=token_count * key_count * heads,
            bytes_accessed=2 * token_count * width * 2 + 4 * key_count * width + 4 * token_count * width,
        ),
    )(table, query_rows, *partial, *cycle_list_sources, *far_list_sources)


def per_device(queries, key_mant, key_exp, value_mant, value_exp, cycle_list, dilated_list):
    tile_blocks = queries.shape[0]
    block_length = queries.shape[2]
    width = queries.shape[3]
    col_count = lax.axis_size("col")
    row_count = lax.axis_size("row")
    distant_rows = tile_blocks // 4
    step_spacing = col_count // DILATION_TILES
    me_col = lax.axis_index("col")

    keys = dequant(key_mant, key_exp)
    values = dequant(value_mant, value_exp)
    stacked = jnp.stack([keys, values])[:, :, 0]

    above = shift(stacked[:, tile_blocks - 1 :], "row", row_count, 1)
    below = shift(stacked[:, :1], "row", row_count, -1)

    edge_cap = min(3 if row_count >= 2 else 4, tile_blocks)
    main_cap = edge_cap - 1 if col_count >= 3 else edge_cap
    entries = cycle_list[0, 0]
    right_entries = shift(entries, "col", col_count, -1)
    left_entries = shift(entries, "col", col_count, 1)
    to_right, _, _ = side_slots(right_entries, 2, tile_blocks, edge_cap)
    to_left, _, _ = side_slots(left_entries, 2 + tile_blocks, tile_blocks, edge_cap)
    right_payload = jnp.take(stacked, to_right, axis=1)
    left_payload = jnp.take(stacked, to_left, axis=1)
    cycle_sources = [above, below]
    cycle_sources.append(shift(right_payload[:, :main_cap], "col", col_count, 1))
    cycle_sources.append(shift(left_payload[:, :main_cap], "col", col_count, -1))
    if main_cap < edge_cap:
        last = col_count - 1
        cycle_sources.append(lax.ppermute(right_payload[:, main_cap:], "col", [(last - 1, last)]))
        cycle_sources.append(lax.ppermute(left_payload[:, main_cap:], "col", [(1, 0)]))

    _, is_left, left_rank = side_slots(entries, 2, tile_blocks, edge_cap)
    _, is_right, right_rank = side_slots(entries, 2 + tile_blocks, tile_blocks, edge_cap)
    side_rank = jnp.where(is_left, left_rank, right_rank)
    overflow = side_rank >= main_cap
    cycle_src = jnp.where(
        entries == 0,
        0,
        jnp.where(entries == 1, 1, 2 + is_right.astype(jnp.int32) + 2 * overflow.astype(jnp.int32)),
    )
    cycle_idx = jnp.where(entries < 2, 0, jnp.where(overflow, side_rank - main_cap, side_rank))

    far_source = stacked[:, 0::4]
    dilated_entries = dilated_list[0, 0]
    hop_slot = dilated_entries // distant_rows
    far_row = dilated_entries % distant_rows
    if step_spacing == 1:
        far_sources, lookup, relative = ring_gather(far_source, col_count, me_col)
        hop_slot = relative((me_col + hop_slot + 1) % col_count)
    else:
        far_sources = []
        lookup = []
        for hop in range(1, DILATION_TILES):
            distance = hop * step_spacing
            route = [((i + distance) % col_count, i) for i in range(col_count)]
            far_sources.append(lax.ppermute(far_source, "col", route))
            lookup.append([(hop - 1, r) for r in range(distant_rows)])
    lookup_src = jnp.array([[a for a, _ in row] for row in lookup], dtype=jnp.int32)
    lookup_idx = jnp.array([[b for _, b in row] for row in lookup], dtype=jnp.int32)
    far_src = len(cycle_sources) + lookup_src[hop_slot, far_row]
    far_idx = lookup_idx[hop_slot, far_row]

    table = jnp.stack(
        [jnp.concatenate([cycle_src, far_src]), jnp.concatenate([cycle_idx, far_idx])], axis=1
    ).reshape(-1)
    token_count = tile_blocks * block_length
    query_rows = queries.reshape(token_count, width)
    partial = own_attend(
        query_rows, keys.reshape(token_count, width), values.reshape(token_count, width)
    )
    result = gather_attend(query_rows, partial, cycle_sources, far_sources, table)
    return result.reshape(queries.shape)


def solution(mesh):
    in_specs = (
        P(("groups", "row"), "col", None, None),
        P(("groups", "row"), "col", None, None),
        P(("groups", "row"), "col", None, None),
        P(("groups", "row"), "col", None, None),
        P(("groups", "row"), "col", None, None),
        P(("groups", "row"), "col", None),
        P(("groups", "row"), "col", None),
    )
    out_specs = P(("groups", "row"), "col", None, None)
    return jax.shard_map(
        per_device, mesh=mesh, in_specs=in_specs, out_specs=out_specs, check_vma=False
    )
```

```python
import functools

import jax
import jax.numpy as jnp
from jax import lax
from jax.experimental import pallas as pl
from jax.experimental.pallas import tpu as pltpu
from jax.sharding import PartitionSpec as P

HEAD_DIM = 128
DILATION_TILES = 8


def dequant(mantissa, exponent):
    tile_rows, tile_cols, block_length, feature_channel_width = mantissa.shape
    groups = exponent.shape[2]
    factor = jnp.exp2(exponent.astype(jnp.float32))[:, :, :, None, :]
    scaled = (
        mantissa.reshape(
            tile_rows, tile_cols, groups, block_length // groups, feature_channel_width
        ).astype(jnp.float32)
        * factor
    )
    return scaled.reshape(mantissa.shape).astype(jnp.bfloat16)


def shift(x, axis, count, step):
    if step > 0:
        pairs = [(i, i + step) for i in range(count - step)]
    else:
        pairs = [(i - step, i) for i in range(count + step)]
    if not pairs:
        return jnp.zeros_like(x)
    return lax.ppermute(x, axis, pairs)


def side_slots(entries, low, tile_blocks, cap):
    inside = (entries >= low) & (entries < low + tile_blocks)
    rank = jnp.cumsum(inside.astype(jnp.int32)) - 1
    slot = jnp.arange(cap, dtype=jnp.int32)[:, None]
    hit = inside[None, :] & (rank[None, :] == slot)
    return jnp.sum(jnp.where(hit, entries[None, :] - low, 0), axis=1), inside, rank


def ring_gather(item, count, me):
    order = list(range(0, count, 2)) + list(range(count - 1 - count % 2, 0, -2))
    position = [0] * count
    for place, col in enumerate(order):
        position[col] = place
    forward = [(order[i], order[(i + 1) % count]) for i in range(count)]
    backward = [(order[(i + 1) % count], order[i]) for i in range(count)]
    half = count // 2
    rows = item.shape[1]
    split = (rows + 1) // 2
    arrays = []
    lookup = [[None] * rows for _ in range(count - 1)]
    for r in range(rows):
        ahead = behind = item[:, r : r + 1]
        for distance in range(1, half + 1):
            if distance == half and count % 2 == 0:
                if r < split:
                    arrays.append(lax.ppermute(ahead, "col", forward))
                else:
                    arrays.append(lax.ppermute(behind, "col", backward))
                lookup[distance - 1][r] = (len(arrays) - 1, 0)
                continue
            ahead = lax.ppermute(ahead, "col", forward)
            arrays.append(ahead)
            lookup[distance - 1][r] = (len(arrays) - 1, 0)
            behind = lax.ppermute(behind, "col", backward)
            arrays.append(behind)
            lookup[count - distance - 1][r] = (len(arrays) - 1, 0)
    table = jnp.array(position, dtype=jnp.int32)

    def relative(col):
        return (table[me] - table[col]) % count - 1

    return arrays, lookup, relative


def gather_attention_kernel(cycle_sources, far_sources, table_ref, q_hbm, own_hbm, *rest):
    sources = rest[: cycle_sources + far_sources]
    o_ref, q_vmem, k_vmem, v_vmem, sems = rest[cycle_sources + far_sources :]
    tile_blocks = own_hbm.shape[1]
    block_length = own_hbm.shape[2]
    extra = table_ref.shape[0] // 2
    heads = q_vmem.shape[1] // HEAD_DIM

    copies = [pltpu.make_async_copy(q_hbm, q_vmem, sems.at[0, 0])]
    copies.append(pltpu.make_async_copy(own_hbm.at[0], k_vmem.at[pl.ds(0, tile_blocks)], sems.at[0, 1]))
    copies.append(pltpu.make_async_copy(own_hbm.at[1], v_vmem.at[pl.ds(0, tile_blocks)], sems.at[1, 1]))
    for c in copies:
        c.start()
    for slot in range(extra):
        src = table_ref[2 * slot]
        index = table_ref[2 * slot + 1]
        lo, hi = (0, cycle_sources) if slot < extra // 2 else (cycle_sources, cycle_sources + far_sources)
        for cand in range(lo, hi):
            @pl.when(src == cand)
            def _():
                for kv, dst in ((0, k_vmem), (1, v_vmem)):
                    pltpu.make_async_copy(
                        sources[cand].at[kv, index], dst.at[tile_blocks + slot], sems.at[kv, 2 + slot]
                    ).start()
    for c in copies:
        c.wait()
    for slot in range(extra):
        for kv, dst in ((0, k_vmem), (1, v_vmem)):
            pltpu.make_async_copy(
                own_hbm.at[kv, 0], dst.at[tile_blocks + slot], sems.at[kv, 2 + slot]
            ).wait()

    key_count = k_vmem.shape[0] * block_length

    for h in range(heads):
        lanes = pl.ds(h * HEAD_DIM, HEAD_DIM)
        q = q_vmem[:, lanes]
        k = k_vmem[:, :, lanes].reshape(key_count, HEAD_DIM)
        v = v_vmem[:, :, lanes].reshape(key_count, HEAD_DIM)
        scores = lax.dot_general(
            q, k, (((1,), (1,)), ((), ())), preferred_element_type=jnp.float32
        ) * HEAD_DIM ** (-0.5)
        row_max = jnp.max(scores, axis=1, keepdims=True)
        weights = jnp.exp(scores - row_max)
        row_total = jnp.sum(weights, axis=1, keepdims=True)
        rounded = weights.astype(jnp.bfloat16)
        blended = jnp.dot(rounded, v, preferred_element_type=jnp.float32)
        o_ref[:, lanes] = (blended / row_total).astype(o_ref.dtype)


def gather_attend(query_rows, own, cycle_list_sources, far_list_sources, table):
    token_count, width = query_rows.shape
    tile_blocks, block_length = own.shape[1], own.shape[2]
    extra = table.shape[0] // 2
    blocks = tile_blocks + extra
    key_count = blocks * block_length
    heads = width // HEAD_DIM
    n_sources = len(cycle_list_sources) + len(far_list_sources)
    kernel = functools.partial(
        gather_attention_kernel, len(cycle_list_sources), len(far_list_sources)
    )
    return pl.pallas_call(
        kernel,
        out_shape=jax.ShapeDtypeStruct((token_count, width), jnp.bfloat16),
        in_specs=[pl.BlockSpec(memory_space=pltpu.SMEM)]
        + [pl.BlockSpec(memory_space=pl.ANY)] * (2 + n_sources),
        out_specs=pl.BlockSpec(memory_space=pltpu.VMEM),
        scratch_shapes=[
            pltpu.VMEM((token_count, width), jnp.bfloat16),
            pltpu.VMEM((blocks, block_length, width), jnp.bfloat16),
            pltpu.VMEM((blocks, block_length, width), jnp.bfloat16),
            pltpu.SemaphoreType.DMA((2, 2 + extra)),
        ],
        compiler_params=pltpu.CompilerParams(vmem_limit_bytes=48 * 1024 * 1024),
        cost_estimate=pl.CostEstimate(
            flops=4 * token_count * key_count * width,
            transcendentals=token_count * key_count * heads,
            bytes_accessed=2 * (2 * token_count * width + 2 * key_count * width),
        ),
    )(table, query_rows, own, *cycle_list_sources, *far_list_sources)


def per_device(queries, key_mant, key_exp, value_mant, value_exp, cycle_list, dilated_list):
    tile_blocks = queries.shape[0]
    block_length = queries.shape[2]
    width = queries.shape[3]
    col_count = lax.axis_size("col")
    row_count = lax.axis_size("row")
    distant_rows = tile_blocks // 4
    step_spacing = col_count // DILATION_TILES
    me_col = lax.axis_index("col")

    stacked = jnp.stack([dequant(key_mant, key_exp), dequant(value_mant, value_exp)])[:, :, 0]

    above = shift(stacked[:, tile_blocks - 1 :], "row", row_count, 1)
    below = shift(stacked[:, :1], "row", row_count, -1)

    edge_cap = min(3 if row_count >= 2 else 4, tile_blocks)
    main_cap = edge_cap - 1 if col_count >= 3 else edge_cap
    entries = cycle_list[0, 0]
    right_entries = shift(entries, "col", col_count, -1)
    left_entries = shift(entries, "col", col_count, 1)
    to_right, _, _ = side_slots(right_entries, 2, tile_blocks, edge_cap)
    to_left, _, _ = side_slots(left_entries, 2 + tile_blocks, tile_blocks, edge_cap)
    right_payload = jnp.take(stacked, to_right, axis=1)
    left_payload = jnp.take(stacked, to_left, axis=1)
    cycle_sources = [above, below]
    cycle_sources.append(shift(right_payload[:, :main_cap], "col", col_count, 1))
    cycle_sources.append(shift(left_payload[:, :main_cap], "col", col_count, -1))
    if main_cap < edge_cap:
        last = col_count - 1
        cycle_sources.append(lax.ppermute(right_payload[:, main_cap:], "col", [(last - 1, last)]))
        cycle_sources.append(lax.ppermute(left_payload[:, main_cap:], "col", [(1, 0)]))

    _, is_left, left_rank = side_slots(entries, 2, tile_blocks, edge_cap)
    _, is_right, right_rank = side_slots(entries, 2 + tile_blocks, tile_blocks, edge_cap)
    side_rank = jnp.where(is_left, left_rank, right_rank)
    overflow = side_rank >= main_cap
    cycle_src = jnp.where(
        entries == 0,
        0,
        jnp.where(entries == 1, 1, 2 + is_right.astype(jnp.int32) + 2 * overflow.astype(jnp.int32)),
    )
    cycle_idx = jnp.where(entries < 2, 0, jnp.where(overflow, side_rank - main_cap, side_rank))

    far_source = stacked[:, 0::4]
    dilated_entries = dilated_list[0, 0]
    hop_slot = dilated_entries // distant_rows
    far_row = dilated_entries % distant_rows
    if step_spacing == 1:
        far_sources, lookup, relative = ring_gather(far_source, col_count, me_col)
        hop_slot = relative((me_col + hop_slot + 1) % col_count)
    else:
        far_sources = []
        lookup = []
        for hop in range(1, DILATION_TILES):
            distance = hop * step_spacing
            route = [((i + distance) % col_count, i) for i in range(col_count)]
            far_sources.append(lax.ppermute(far_source, "col", route))
            lookup.append([(hop - 1, r) for r in range(distant_rows)])
    lookup_src = jnp.array([[a for a, _ in row] for row in lookup], dtype=jnp.int32)
    lookup_idx = jnp.array([[b for _, b in row] for row in lookup], dtype=jnp.int32)
    far_src = len(cycle_sources) + lookup_src[hop_slot, far_row]
    far_idx = lookup_idx[hop_slot, far_row]

    table = jnp.stack(
        [jnp.concatenate([cycle_src, far_src]), jnp.concatenate([cycle_idx, far_idx])], axis=1
    ).reshape(-1)
    token_count = tile_blocks * block_length
    result = gather_attend(
        queries.reshape(token_count, width), stacked, cycle_sources, far_sources, table
    )
    return result.reshape(queries.shape)


def solution(mesh):
    in_specs = (
        P(("groups", "row"), "col", None, None),
        P(("groups", "row"), "col", None, None),
        P(("groups", "row"), "col", None, None),
        P(("groups", "row"), "col", None, None),
        P(("groups", "row"), "col", None, None),
        P(("groups", "row"), "col", None),
        P(("groups", "row"), "col", None),
    )
    out_specs = P(("groups", "row"), "col", None, None)
    return jax.shard_map(
        per_device, mesh=mesh, in_specs=in_specs, out_specs=out_specs, check_vma=False
    )
```

```python
import functools

import jax
import jax.numpy as jnp
from jax import lax
from jax.experimental import pallas as pl
from jax.experimental.pallas import tpu as pltpu
from jax.sharding import PartitionSpec as P

HEAD_DIM = 128
DILATION_TILES = 8


def dequant(mantissa, exponent):
    tile_rows, tile_cols, block_length, feature_channel_width = mantissa.shape
    groups = exponent.shape[2]
    factor = jnp.exp2(exponent.astype(jnp.float32))[:, :, :, None, :]
    scaled = (
        mantissa.reshape(
            tile_rows, tile_cols, groups, block_length // groups, feature_channel_width
        ).astype(jnp.float32)
        * factor
    )
    return scaled.reshape(mantissa.shape).astype(jnp.bfloat16)


def shift(x, axis, count, step):
    if step > 0:
        pairs = [(i, i + step) for i in range(count - step)]
    else:
        pairs = [(i - step, i) for i in range(count + step)]
    if not pairs:
        return jnp.zeros_like(x)
    return lax.ppermute(x, axis, pairs)


def side_slots(entries, low, tile_blocks, cap):
    inside = (entries >= low) & (entries < low + tile_blocks)
    rank = jnp.cumsum(inside.astype(jnp.int32)) - 1
    slot = jnp.arange(cap, dtype=jnp.int32)[:, None]
    hit = inside[None, :] & (rank[None, :] == slot)
    return jnp.sum(jnp.where(hit, entries[None, :] - low, 0), axis=1), inside, rank


def ring_gather(item, count, me):
    order = list(range(0, count, 2)) + list(range(count - 1 - count % 2, 0, -2))
    position = [0] * count
    for place, col in enumerate(order):
        position[col] = place
    forward = [(order[i], order[(i + 1) % count]) for i in range(count)]
    backward = [(order[(i + 1) % count], order[i]) for i in range(count)]
    half = count // 2
    rows = item.shape[1]
    split = (rows + 1) // 2
    arrays = []
    lookup = [[None] * rows for _ in range(count - 1)]
    for r in range(rows):
        ahead = behind = item[:, r : r + 1]
        for distance in range(1, half + 1):
            if distance == half and count % 2 == 0:
                if r < split:
                    arrays.append(lax.ppermute(ahead, "col", forward))
                else:
                    arrays.append(lax.ppermute(behind, "col", backward))
                lookup[distance - 1][r] = (len(arrays) - 1, 0)
                continue
            ahead = lax.ppermute(ahead, "col", forward)
            arrays.append(ahead)
            lookup[distance - 1][r] = (len(arrays) - 1, 0)
            behind = lax.ppermute(behind, "col", backward)
            arrays.append(behind)
            lookup[count - distance - 1][r] = (len(arrays) - 1, 0)
    table = jnp.array(position, dtype=jnp.int32)

    def relative(col):
        return (table[me] - table[col]) % count - 1

    return arrays, lookup, relative


def gather_attention_kernel(cycle_sources, far_sources, table_ref, q_hbm, own_hbm, *rest):
    sources = rest[: cycle_sources + far_sources]
    o_ref, q_vmem, k_vmem, v_vmem, sems = rest[cycle_sources + far_sources :]
    tile_blocks = own_hbm.shape[1]
    block_length = own_hbm.shape[2]
    extra = table_ref.shape[0] // 2
    heads = q_vmem.shape[1] // HEAD_DIM
    chunks = sems.shape[0]
    chunk_heads = heads // chunks
    chunk_width = chunk_heads * HEAD_DIM

    def chunk_copies(c):
        lanes = pl.ds(c * chunk_width, chunk_width)
        fixed = [
            (q_hbm.at[:, lanes], q_vmem.at[:, lanes], sems.at[c, 0, 0]),
            (own_hbm.at[0, :, :, lanes], k_vmem.at[pl.ds(0, tile_blocks), :, lanes], sems.at[c, 0, 1]),
            (own_hbm.at[1, :, :, lanes], v_vmem.at[pl.ds(0, tile_blocks), :, lanes], sems.at[c, 1, 1]),
        ]
        return lanes, fixed

    for c in range(chunks):
        lanes, fixed = chunk_copies(c)
        for src, dst, sem in fixed:
            pltpu.make_async_copy(src, dst, sem).start()
        for slot in range(extra):
            src = table_ref[2 * slot]
            index = table_ref[2 * slot + 1]
            lo, hi = (0, cycle_sources) if slot < extra // 2 else (cycle_sources, cycle_sources + far_sources)
            for cand in range(lo, hi):
                @pl.when(src == cand)
                def _():
                    for kv, dst in ((0, k_vmem), (1, v_vmem)):
                        pltpu.make_async_copy(
                            sources[cand].at[kv, index, :, lanes],
                            dst.at[tile_blocks + slot, :, lanes],
                            sems.at[c, kv, 2 + slot],
                        ).start()

    key_count = k_vmem.shape[0] * block_length

    for c in range(chunks):
        lanes, fixed = chunk_copies(c)
        for src, dst, sem in fixed:
            pltpu.make_async_copy(src, dst, sem).wait()
        for slot in range(extra):
            for kv, dst in ((0, k_vmem), (1, v_vmem)):
                pltpu.make_async_copy(
                    own_hbm.at[kv, 0, :, lanes], dst.at[tile_blocks + slot, :, lanes], sems.at[c, kv, 2 + slot]
                ).wait()
        for h in range(c * chunk_heads, (c + 1) * chunk_heads):
            lanes = pl.ds(h * HEAD_DIM, HEAD_DIM)
            q = q_vmem[:, lanes]
            k = k_vmem[:, :, lanes].reshape(key_count, HEAD_DIM)
            v = v_vmem[:, :, lanes].reshape(key_count, HEAD_DIM)
            scores = lax.dot_general(
                q, k, (((1,), (1,)), ((), ())), preferred_element_type=jnp.float32
            ) * HEAD_DIM ** (-0.5)
            row_max = jnp.max(scores, axis=1, keepdims=True)
            weights = jnp.exp(scores - row_max)
            row_total = jnp.sum(weights, axis=1, keepdims=True)
            rounded = weights.astype(jnp.bfloat16)
            blended = jnp.dot(rounded, v, preferred_element_type=jnp.float32)
            o_ref[:, lanes] = (blended / row_total).astype(o_ref.dtype)


def lane_chunks(heads):
    return 3 if heads % 3 == 0 else (2 if heads % 2 == 0 else 1)


def gather_attend(query_rows, own, cycle_list_sources, far_list_sources, table):
    token_count, width = query_rows.shape
    tile_blocks, block_length = own.shape[1], own.shape[2]
    extra = table.shape[0] // 2
    blocks = tile_blocks + extra
    key_count = blocks * block_length
    heads = width // HEAD_DIM
    n_sources = len(cycle_list_sources) + len(far_list_sources)
    kernel = functools.partial(
        gather_attention_kernel, len(cycle_list_sources), len(far_list_sources)
    )
    return pl.pallas_call(
        kernel,
        out_shape=jax.ShapeDtypeStruct((token_count, width), jnp.bfloat16),
        in_specs=[pl.BlockSpec(memory_space=pltpu.SMEM)]
        + [pl.BlockSpec(memory_space=pl.ANY)] * (2 + n_sources),
        out_specs=pl.BlockSpec(memory_space=pltpu.VMEM),
        scratch_shapes=[
            pltpu.VMEM((token_count, width), jnp.bfloat16),
            pltpu.VMEM((blocks, block_length, width), jnp.bfloat16),
            pltpu.VMEM((blocks, block_length, width), jnp.bfloat16),
            pltpu.SemaphoreType.DMA((lane_chunks(heads), 2, 2 + extra)),
        ],
        compiler_params=pltpu.CompilerParams(vmem_limit_bytes=48 * 1024 * 1024),
        cost_estimate=pl.CostEstimate(
            flops=4 * token_count * key_count * width,
            transcendentals=token_count * key_count * heads,
            bytes_accessed=2 * (2 * token_count * width + 2 * key_count * width),
        ),
    )(table, query_rows, own, *cycle_list_sources, *far_list_sources)


def per_device(queries, key_mant, key_exp, value_mant, value_exp, cycle_list, dilated_list):
    tile_blocks = queries.shape[0]
    block_length = queries.shape[2]
    width = queries.shape[3]
    col_count = lax.axis_size("col")
    row_count = lax.axis_size("row")
    distant_rows = tile_blocks // 4
    step_spacing = col_count // DILATION_TILES
    me_col = lax.axis_index("col")

    stacked = jnp.stack([dequant(key_mant, key_exp), dequant(value_mant, value_exp)])[:, :, 0]

    above = shift(stacked[:, tile_blocks - 1 :], "row", row_count, 1)
    below = shift(stacked[:, :1], "row", row_count, -1)

    edge_cap = min(3 if row_count >= 2 else 4, tile_blocks)
    main_cap = edge_cap - 1 if col_count >= 3 else edge_cap
    entries = cycle_list[0, 0]
    right_entries = shift(entries, "col", col_count, -1)
    left_entries = shift(entries, "col", col_count, 1)
    to_right, _, _ = side_slots(right_entries, 2, tile_blocks, edge_cap)
    to_left, _, _ = side_slots(left_entries, 2 + tile_blocks, tile_blocks, edge_cap)
    right_payload = jnp.take(stacked, to_right, axis=1)
    left_payload = jnp.take(stacked, to_left, axis=1)
    cycle_sources = [above, below]
    cycle_sources.append(shift(right_payload[:, :main_cap], "col", col_count, 1))
    cycle_sources.append(shift(left_payload[:, :main_cap], "col", col_count, -1))
    if main_cap < edge_cap:
        last = col_count - 1
        cycle_sources.append(lax.ppermute(right_payload[:, main_cap:], "col", [(last - 1, last)]))
        cycle_sources.append(lax.ppermute(left_payload[:, main_cap:], "col", [(1, 0)]))

    _, is_left, left_rank = side_slots(entries, 2, tile_blocks, edge_cap)
    _, is_right, right_rank = side_slots(entries, 2 + tile_blocks, tile_blocks, edge_cap)
    side_rank = jnp.where(is_left, left_rank, right_rank)
    overflow = side_rank >= main_cap
    cycle_src = jnp.where(
        entries == 0,
        0,
        jnp.where(entries == 1, 1, 2 + is_right.astype(jnp.int32) + 2 * overflow.astype(jnp.int32)),
    )
    cycle_idx = jnp.where(entries < 2, 0, jnp.where(overflow, side_rank - main_cap, side_rank))

    far_source = stacked[:, 0::4]
    dilated_entries = dilated_list[0, 0]
    hop_slot = dilated_entries // distant_rows
    far_row = dilated_entries % distant_rows
    if step_spacing == 1:
        far_sources, lookup, relative = ring_gather(far_source, col_count, me_col)
        hop_slot = relative((me_col + hop_slot + 1) % col_count)
    else:
        far_sources = []
        lookup = []
        for hop in range(1, DILATION_TILES):
            distance = hop * step_spacing
            route = [((i + distance) % col_count, i) for i in range(col_count)]
            far_sources.append(lax.ppermute(far_source, "col", route))
            lookup.append([(hop - 1, r) for r in range(distant_rows)])
    lookup_src = jnp.array([[a for a, _ in row] for row in lookup], dtype=jnp.int32)
    lookup_idx = jnp.array([[b for _, b in row] for row in lookup], dtype=jnp.int32)
    far_src = len(cycle_sources) + lookup_src[hop_slot, far_row]
    far_idx = lookup_idx[hop_slot, far_row]

    table = jnp.stack(
        [jnp.concatenate([cycle_src, far_src]), jnp.concatenate([cycle_idx, far_idx])], axis=1
    ).reshape(-1)
    token_count = tile_blocks * block_length
    result = gather_attend(
        queries.reshape(token_count, width), stacked, cycle_sources, far_sources, table
    )
    return result.reshape(queries.shape)


def solution(mesh):
    in_specs = (
        P(("groups", "row"), "col", None, None),
        P(("groups", "row"), "col", None, None),
        P(("groups", "row"), "col", None, None),
        P(("groups", "row"), "col", None, None),
        P(("groups", "row"), "col", None, None),
        P(("groups", "row"), "col", None),
        P(("groups", "row"), "col", None),
    )
    out_specs = P(("groups", "row"), "col", None, None)
    return jax.shard_map(
        per_device, mesh=mesh, in_specs=in_specs, out_specs=out_specs, check_vma=False
    )
```

```python
import functools

import jax
import jax.numpy as jnp
from jax import lax
from jax.experimental import pallas as pl
from jax.experimental.pallas import tpu as pltpu
from jax.sharding import PartitionSpec as P

HEAD_DIM = 128
DILATION_TILES = 8


def dequant(mantissa, exponent):
    tile_rows, tile_cols, block_length, feature_channel_width = mantissa.shape
    groups = exponent.shape[2]
    factor = jnp.exp2(exponent.astype(jnp.float32))[:, :, :, None, :]
    scaled = (
        mantissa.reshape(
            tile_rows, tile_cols, groups, block_length // groups, feature_channel_width
        ).astype(jnp.float32)
        * factor
    )
    return scaled.reshape(mantissa.shape).astype(jnp.bfloat16)


def shift(x, axis, count, step):
    if step > 0:
        pairs = [(i, i + step) for i in range(count - step)]
    else:
        pairs = [(i - step, i) for i in range(count + step)]
    if not pairs:
        return jnp.zeros_like(x)
    return lax.ppermute(x, axis, pairs)


def side_slots(entries, low, tile_blocks, cap):
    inside = (entries >= low) & (entries < low + tile_blocks)
    rank = jnp.cumsum(inside.astype(jnp.int32)) - 1
    slot = jnp.arange(cap, dtype=jnp.int32)[:, None]
    hit = inside[None, :] & (rank[None, :] == slot)
    return jnp.sum(jnp.where(hit, entries[None, :] - low, 0), axis=1), inside, rank


def ring_gather(item, count, me):
    order = list(range(0, count, 2)) + list(range(count - 1 - count % 2, 0, -2))
    position = [0] * count
    for place, col in enumerate(order):
        position[col] = place
    forward = [(order[i], order[(i + 1) % count]) for i in range(count)]
    backward = [(order[(i + 1) % count], order[i]) for i in range(count)]
    half = count // 2
    rows = item.shape[1]
    split = (rows + 1) // 2
    arrays = []
    lookup = [[None] * rows for _ in range(count - 1)]
    for r in range(rows):
        ahead = behind = item[:, r : r + 1]
        for distance in range(1, half + 1):
            if distance == half and count % 2 == 0:
                if r < split:
                    arrays.append(lax.ppermute(ahead, "col", forward))
                else:
                    arrays.append(lax.ppermute(behind, "col", backward))
                lookup[distance - 1][r] = (len(arrays) - 1, 0)
                continue
            ahead = lax.ppermute(ahead, "col", forward)
            arrays.append(ahead)
            lookup[distance - 1][r] = (len(arrays) - 1, 0)
            behind = lax.ppermute(behind, "col", backward)
            arrays.append(behind)
            lookup[count - distance - 1][r] = (len(arrays) - 1, 0)
    table = jnp.array(position, dtype=jnp.int32)

    def relative(col):
        return (table[me] - table[col]) % count - 1

    return arrays, lookup, relative


def gather_attention_kernel(cycle_sources, far_sources, table_ref, q_hbm, own_hbm, *rest):
    sources = rest[: cycle_sources + far_sources]
    o_ref, q_vmem, k_vmem, v_vmem, sems = rest[cycle_sources + far_sources :]
    tile_blocks = own_hbm.shape[1]
    block_length = own_hbm.shape[2]
    extra = table_ref.shape[0] // 2
    heads = q_vmem.shape[1] // HEAD_DIM

    copies = [pltpu.make_async_copy(q_hbm, q_vmem, sems.at[0, 0])]
    copies.append(pltpu.make_async_copy(own_hbm.at[0], k_vmem.at[pl.ds(0, tile_blocks)], sems.at[0, 1]))
    copies.append(pltpu.make_async_copy(own_hbm.at[1], v_vmem.at[pl.ds(0, tile_blocks)], sems.at[1, 1]))
    for c in copies:
        c.start()
    for slot in range(extra):
        src = table_ref[2 * slot]
        index = table_ref[2 * slot + 1]
        lo, hi = (0, cycle_sources) if slot < extra // 2 else (cycle_sources, cycle_sources + far_sources)
        for cand in range(lo, hi):
            @pl.when(src == cand)
            def _():
                for kv, dst in ((0, k_vmem), (1, v_vmem)):
                    pltpu.make_async_copy(
                        sources[cand].at[kv, index], dst.at[tile_blocks + slot], sems.at[kv, 2 + slot]
                    ).start()
    for c in copies:
        c.wait()
    for slot in range(extra):
        for kv, dst in ((0, k_vmem), (1, v_vmem)):
            pltpu.make_async_copy(
                own_hbm.at[kv, 0], dst.at[tile_blocks + slot], sems.at[kv, 2 + slot]
            ).wait()

    key_count = k_vmem.shape[0] * block_length

    for h in range(heads):
        lanes = pl.ds(h * HEAD_DIM, HEAD_DIM)
        q = q_vmem[:, lanes]
        k = k_vmem[:, :, lanes].reshape(key_count, HEAD_DIM)
        v = v_vmem[:, :, lanes].reshape(key_count, HEAD_DIM)
        scores = lax.dot_general(
            q, k, (((1,), (1,)), ((), ())), preferred_element_type=jnp.float32
        ) * HEAD_DIM ** (-0.5)
        row_max = jnp.max(scores, axis=1, keepdims=True)
        weights = jnp.exp(scores - row_max)
        row_total = jnp.sum(weights, axis=1, keepdims=True)
        rounded = weights.astype(jnp.bfloat16)
        blended = jnp.dot(rounded, v, preferred_element_type=jnp.float32)
        o_ref[:, lanes] = (blended / row_total).astype(o_ref.dtype)


def gather_attend(query_rows, own, cycle_list_sources, far_list_sources, table):
    token_count, width = query_rows.shape
    tile_blocks, block_length = own.shape[1], own.shape[2]
    extra = table.shape[0] // 2
    blocks = tile_blocks + extra
    key_count = blocks * block_length
    heads = width // HEAD_DIM
    n_sources = len(cycle_list_sources) + len(far_list_sources)
    kernel = functools.partial(
        gather_attention_kernel, len(cycle_list_sources), len(far_list_sources)
    )
    return pl.pallas_call(
        kernel,
        out_shape=jax.ShapeDtypeStruct((token_count, width), jnp.bfloat16),
        in_specs=[pl.BlockSpec(memory_space=pltpu.SMEM)]
        + [pl.BlockSpec(memory_space=pl.ANY)] * (2 + n_sources),
        out_specs=pl.BlockSpec(memory_space=pltpu.VMEM),
        scratch_shapes=[
            pltpu.VMEM((token_count, width), jnp.bfloat16),
            pltpu.VMEM((blocks, block_length, width), jnp.bfloat16),
            pltpu.VMEM((blocks, block_length, width), jnp.bfloat16),
            pltpu.SemaphoreType.DMA((2, 2 + extra)),
        ],
        compiler_params=pltpu.CompilerParams(vmem_limit_bytes=48 * 1024 * 1024),
        cost_estimate=pl.CostEstimate(
            flops=4 * token_count * key_count * width,
            transcendentals=token_count * key_count * heads,
            bytes_accessed=2 * (2 * token_count * width + 2 * key_count * width),
        ),
    )(table, query_rows, own, *cycle_list_sources, *far_list_sources)


def per_device(queries, key_mant, key_exp, value_mant, value_exp, cycle_list, dilated_list):
    tile_blocks = queries.shape[0]
    block_length = queries.shape[2]
    width = queries.shape[3]
    col_count = lax.axis_size("col")
    row_count = lax.axis_size("row")
    distant_rows = tile_blocks // 4
    step_spacing = col_count // DILATION_TILES
    me_col = lax.axis_index("col")

    stacked = jnp.stack([dequant(key_mant, key_exp), dequant(value_mant, value_exp)])[:, :, 0]

    above = shift(stacked[:, tile_blocks - 1 :], "row", row_count, 1)
    below = shift(stacked[:, :1], "row", row_count, -1)

    far_source = stacked[:, 0::4]
    dilated_entries = dilated_list[0, 0]
    hop_slot = dilated_entries // distant_rows
    far_row = dilated_entries % distant_rows
    if step_spacing == 1:
        far_sources, lookup, relative = ring_gather(far_source, col_count, me_col)
        hop_slot = relative((me_col + hop_slot + 1) % col_count)
    else:
        far_sources = []
        lookup = []
        for hop in range(1, DILATION_TILES):
            distance = hop * step_spacing
            route = [((i + distance) % col_count, i) for i in range(col_count)]
            far_sources.append(lax.ppermute(far_source, "col", route))
            lookup.append([(hop - 1, r) for r in range(distant_rows)])
    entries, _ = lax.optimization_barrier((cycle_list[0, 0], far_sources[0]))
    edge_cap = min(3 if row_count >= 2 else 4, tile_blocks)
    main_cap = edge_cap - 1 if col_count >= 3 else edge_cap
    right_entries = shift(entries, "col", col_count, -1)
    left_entries = shift(entries, "col", col_count, 1)
    to_right, _, _ = side_slots(right_entries, 2, tile_blocks, edge_cap)
    to_left, _, _ = side_slots(left_entries, 2 + tile_blocks, tile_blocks, edge_cap)
    right_payload = jnp.take(stacked, to_right, axis=1)
    left_payload = jnp.take(stacked, to_left, axis=1)
    cycle_sources = [above, below]
    cycle_sources.append(shift(right_payload[:, :main_cap], "col", col_count, 1))
    cycle_sources.append(shift(left_payload[:, :main_cap], "col", col_count, -1))
    if main_cap < edge_cap:
        last = col_count - 1
        cycle_sources.append(lax.ppermute(right_payload[:, main_cap:], "col", [(last - 1, last)]))
        cycle_sources.append(lax.ppermute(left_payload[:, main_cap:], "col", [(1, 0)]))

    _, is_left, left_rank = side_slots(entries, 2, tile_blocks, edge_cap)
    _, is_right, right_rank = side_slots(entries, 2 + tile_blocks, tile_blocks, edge_cap)
    side_rank = jnp.where(is_left, left_rank, right_rank)
    overflow = side_rank >= main_cap
    cycle_src = jnp.where(
        entries == 0,
        0,
        jnp.where(entries == 1, 1, 2 + is_right.astype(jnp.int32) + 2 * overflow.astype(jnp.int32)),
    )
    cycle_idx = jnp.where(entries < 2, 0, jnp.where(overflow, side_rank - main_cap, side_rank))

    lookup_src = jnp.array([[a for a, _ in row] for row in lookup], dtype=jnp.int32)
    lookup_idx = jnp.array([[b for _, b in row] for row in lookup], dtype=jnp.int32)
    far_src = len(cycle_sources) + lookup_src[hop_slot, far_row]
    far_idx = lookup_idx[hop_slot, far_row]

    table = jnp.stack(
        [jnp.concatenate([cycle_src, far_src]), jnp.concatenate([cycle_idx, far_idx])], axis=1
    ).reshape(-1)
    token_count = tile_blocks * block_length
    result = gather_attend(
        queries.reshape(token_count, width), stacked, cycle_sources, far_sources, table
    )
    return result.reshape(queries.shape)


def solution(mesh):
    in_specs = (
        P(("groups", "row"), "col", None, None),
        P(("groups", "row"), "col", None, None),
        P(("groups", "row"), "col", None, None),
        P(("groups", "row"), "col", None, None),
        P(("groups", "row"), "col", None, None),
        P(("groups", "row"), "col", None),
        P(("groups", "row"), "col", None),
    )
    out_specs = P(("groups", "row"), "col", None, None)
    return jax.shard_map(
        per_device, mesh=mesh, in_specs=in_specs, out_specs=out_specs, check_vma=False
    )
```

```python
import functools

import jax
import jax.numpy as jnp
from jax import lax
from jax.experimental import pallas as pl
from jax.experimental.pallas import tpu as pltpu
from jax.sharding import PartitionSpec as P

HEAD_DIM = 128
DILATION_TILES = 8


def dequant(mantissa, exponent):
    tile_rows, tile_cols, block_length, feature_channel_width = mantissa.shape
    groups = exponent.shape[2]
    factor = jnp.exp2(exponent.astype(jnp.float32))[:, :, :, None, :]
    scaled = (
        mantissa.reshape(
            tile_rows, tile_cols, groups, block_length // groups, feature_channel_width
        ).astype(jnp.float32)
        * factor
    )
    return scaled.reshape(mantissa.shape).astype(jnp.bfloat16)


def shift(x, axis, count, step):
    if step > 0:
        pairs = [(i, i + step) for i in range(count - step)]
    else:
        pairs = [(i - step, i) for i in range(count + step)]
    if not pairs:
        return jnp.zeros_like(x)
    return lax.ppermute(x, axis, pairs)


def side_slots(entries, low, tile_blocks, cap):
    inside = (entries >= low) & (entries < low + tile_blocks)
    rank = jnp.cumsum(inside.astype(jnp.int32)) - 1
    slot = jnp.arange(cap, dtype=jnp.int32)[:, None]
    hit = inside[None, :] & (rank[None, :] == slot)
    return jnp.sum(jnp.where(hit, entries[None, :] - low, 0), axis=1), inside, rank


def ring_gather(item, count, me):
    order = list(range(0, count, 2)) + list(range(count - 1 - count % 2, 0, -2))
    position = [0] * count
    for place, col in enumerate(order):
        position[col] = place
    forward = [(order[i], order[(i + 1) % count]) for i in range(count)]
    backward = [(order[(i + 1) % count], order[i]) for i in range(count)]
    half = count // 2
    rows = item.shape[1]
    split = (rows + 1) // 2
    arrays = []
    lookup = [[None] * rows for _ in range(count - 1)]
    for r in range(rows):
        ahead = behind = item[:, r : r + 1]
        for distance in range(1, half + 1):
            if distance == half and count % 2 == 0:
                if r < split:
                    arrays.append(lax.ppermute(ahead, "col", forward))
                else:
                    arrays.append(lax.ppermute(behind, "col", backward))
                lookup[distance - 1][r] = (len(arrays) - 1, 0)
                continue
            ahead = lax.ppermute(ahead, "col", forward)
            arrays.append(ahead)
            lookup[distance - 1][r] = (len(arrays) - 1, 0)
            behind = lax.ppermute(behind, "col", backward)
            arrays.append(behind)
            lookup[count - distance - 1][r] = (len(arrays) - 1, 0)
    table = jnp.array(position, dtype=jnp.int32)

    def relative(col):
        return (table[me] - table[col]) % count - 1

    return arrays, lookup, relative


def gather_attention_kernel(cycle_sources, far_sources, table_ref, q_hbm, own_hbm, *rest):
    sources = rest[: cycle_sources + far_sources]
    o_ref, q_vmem, k_vmem, v_vmem, sems = rest[cycle_sources + far_sources :]
    tile_blocks = own_hbm.shape[1]
    block_length = own_hbm.shape[2]
    extra = table_ref.shape[0] // 2
    heads = q_vmem.shape[1] // HEAD_DIM

    copies = [pltpu.make_async_copy(q_hbm, q_vmem, sems.at[0, 0])]
    copies.append(pltpu.make_async_copy(own_hbm.at[0], k_vmem.at[pl.ds(0, tile_blocks)], sems.at[0, 1]))
    copies.append(pltpu.make_async_copy(own_hbm.at[1], v_vmem.at[pl.ds(0, tile_blocks)], sems.at[1, 1]))
    for c in copies:
        c.start()
    for slot in range(extra):
        src = table_ref[2 * slot]
        index = table_ref[2 * slot + 1]
        lo, hi = (0, cycle_sources) if slot < extra // 2 else (cycle_sources, cycle_sources + far_sources)
        for cand in range(lo, hi):
            @pl.when(src == cand)
            def _():
                for kv, dst in ((0, k_vmem), (1, v_vmem)):
                    pltpu.make_async_copy(
                        sources[cand].at[kv, index], dst.at[tile_blocks + slot], sems.at[kv, 2 + slot]
                    ).start()
    for c in copies:
        c.wait()
    for slot in range(extra):
        for kv, dst in ((0, k_vmem), (1, v_vmem)):
            pltpu.make_async_copy(
                own_hbm.at[kv, 0], dst.at[tile_blocks + slot], sems.at[kv, 2 + slot]
            ).wait()

    key_count = k_vmem.shape[0] * block_length

    for h in range(heads):
        lanes = pl.ds(h * HEAD_DIM, HEAD_DIM)
        q = q_vmem[:, lanes]
        k = k_vmem[:, :, lanes].reshape(key_count, HEAD_DIM)
        v = v_vmem[:, :, lanes].reshape(key_count, HEAD_DIM)
        scores = lax.dot_general(
            q, k, (((1,), (1,)), ((), ())), preferred_element_type=jnp.float32
        ) * HEAD_DIM ** (-0.5)
        row_max = jnp.max(scores, axis=1, keepdims=True)
        weights = jnp.exp(scores - row_max)
        row_total = jnp.sum(weights, axis=1, keepdims=True)
        rounded = weights.astype(jnp.bfloat16)
        blended = jnp.dot(rounded, v, preferred_element_type=jnp.float32)
        o_ref[:, lanes] = (blended / row_total).astype(o_ref.dtype)


def gather_attend(query_rows, own, cycle_list_sources, far_list_sources, table):
    token_count, width = query_rows.shape
    tile_blocks, block_length = own.shape[1], own.shape[2]
    extra = table.shape[0] // 2
    blocks = tile_blocks + extra
    key_count = blocks * block_length
    heads = width // HEAD_DIM
    n_sources = len(cycle_list_sources) + len(far_list_sources)
    kernel = functools.partial(
        gather_attention_kernel, len(cycle_list_sources), len(far_list_sources)
    )
    return pl.pallas_call(
        kernel,
        out_shape=jax.ShapeDtypeStruct((token_count, width), jnp.bfloat16),
        in_specs=[pl.BlockSpec(memory_space=pltpu.SMEM)]
        + [pl.BlockSpec(memory_space=pl.ANY)] * (2 + n_sources),
        out_specs=pl.BlockSpec(memory_space=pltpu.VMEM),
        scratch_shapes=[
            pltpu.VMEM((token_count, width), jnp.bfloat16),
            pltpu.VMEM((blocks, block_length, width), jnp.bfloat16),
            pltpu.VMEM((blocks, block_length, width), jnp.bfloat16),
            pltpu.SemaphoreType.DMA((2, 2 + extra)),
        ],
        compiler_params=pltpu.CompilerParams(vmem_limit_bytes=48 * 1024 * 1024),
        cost_estimate=pl.CostEstimate(
            flops=4 * token_count * key_count * width,
            transcendentals=token_count * key_count * heads,
            bytes_accessed=2 * (2 * token_count * width + 2 * key_count * width),
        ),
    )(table, query_rows, own, *cycle_list_sources, *far_list_sources)


def per_device(queries, key_mant, key_exp, value_mant, value_exp, cycle_list, dilated_list):
    tile_blocks = queries.shape[0]
    block_length = queries.shape[2]
    width = queries.shape[3]
    col_count = lax.axis_size("col")
    row_count = lax.axis_size("row")
    distant_rows = tile_blocks // 4
    step_spacing = col_count // DILATION_TILES
    me_col = lax.axis_index("col")

    stacked = jnp.stack([dequant(key_mant, key_exp), dequant(value_mant, value_exp)])[:, :, 0]

    above = shift(stacked[:, tile_blocks - 1 :], "row", row_count, 1)
    below = shift(stacked[:, :1], "row", row_count, -1)

    edge_cap = min(3 if row_count >= 2 else 4, tile_blocks)
    main_cap = edge_cap - 1 if col_count >= 3 else edge_cap
    entries = cycle_list[0, me_col]
    right_entries = cycle_list[0, jnp.minimum(me_col + 1, col_count - 1)]
    left_entries = cycle_list[0, jnp.maximum(me_col - 1, 0)]
    to_right, _, _ = side_slots(right_entries, 2, tile_blocks, edge_cap)
    to_left, _, _ = side_slots(left_entries, 2 + tile_blocks, tile_blocks, edge_cap)
    right_payload = jnp.take(stacked, to_right, axis=1)
    left_payload = jnp.take(stacked, to_left, axis=1)
    cycle_sources = [above, below]
    cycle_sources.append(shift(right_payload[:, :main_cap], "col", col_count, 1))
    cycle_sources.append(shift(left_payload[:, :main_cap], "col", col_count, -1))
    if main_cap < edge_cap:
        last = col_count - 1
        cycle_sources.append(lax.ppermute(right_payload[:, main_cap:], "col", [(last - 1, last)]))
        cycle_sources.append(lax.ppermute(left_payload[:, main_cap:], "col", [(1, 0)]))

    _, is_left, left_rank = side_slots(entries, 2, tile_blocks, edge_cap)
    _, is_right, right_rank = side_slots(entries, 2 + tile_blocks, tile_blocks, edge_cap)
    side_rank = jnp.where(is_left, left_rank, right_rank)
    overflow = side_rank >= main_cap
    cycle_src = jnp.where(
        entries == 0,
        0,
        jnp.where(entries == 1, 1, 2 + is_right.astype(jnp.int32) + 2 * overflow.astype(jnp.int32)),
    )
    cycle_idx = jnp.where(entries < 2, 0, jnp.where(overflow, side_rank - main_cap, side_rank))

    far_source = stacked[:, 0::4]
    dilated_entries = dilated_list[0, 0]
    hop_slot = dilated_entries // distant_rows
    far_row = dilated_entries % distant_rows
    if step_spacing == 1:
        far_sources, lookup, relative = ring_gather(far_source, col_count, me_col)
        hop_slot = relative((me_col + hop_slot + 1) % col_count)
    else:
        far_sources = []
        lookup = []
        for hop in range(1, DILATION_TILES):
            distance = hop * step_spacing
            route = [((i + distance) % col_count, i) for i in range(col_count)]
            far_sources.append(lax.ppermute(far_source, "col", route))
            lookup.append([(hop - 1, r) for r in range(distant_rows)])
    lookup_src = jnp.array([[a for a, _ in row] for row in lookup], dtype=jnp.int32)
    lookup_idx = jnp.array([[b for _, b in row] for row in lookup], dtype=jnp.int32)
    far_src = len(cycle_sources) + lookup_src[hop_slot, far_row]
    far_idx = lookup_idx[hop_slot, far_row]

    table = jnp.stack(
        [jnp.concatenate([cycle_src, far_src]), jnp.concatenate([cycle_idx, far_idx])], axis=1
    ).reshape(-1)
    token_count = tile_blocks * block_length
    result = gather_attend(
        queries.reshape(token_count, width), stacked, cycle_sources, far_sources, table
    )
    return result.reshape(queries.shape)


def solution(mesh):
    in_specs = (
        P(("groups", "row"), "col", None, None),
        P(("groups", "row"), "col", None, None),
        P(("groups", "row"), "col", None, None),
        P(("groups", "row"), "col", None, None),
        P(("groups", "row"), "col", None, None),
        P(("groups", "row"), None, None),
        P(("groups", "row"), "col", None),
    )
    out_specs = P(("groups", "row"), "col", None, None)
    return jax.shard_map(
        per_device, mesh=mesh, in_specs=in_specs, out_specs=out_specs, check_vma=False
    )
```

```python
import functools

import jax
import jax.numpy as jnp
from jax import lax
from jax.experimental import pallas as pl
from jax.experimental.pallas import tpu as pltpu
from jax.sharding import PartitionSpec as P

HEAD_DIM = 128
DILATION_TILES = 8


def dequant(mantissa, exponent):
    tile_rows, tile_cols, block_length, feature_channel_width = mantissa.shape
    groups = exponent.shape[2]
    factor = jnp.exp2(exponent.astype(jnp.float32))[:, :, :, None, :]
    scaled = (
        mantissa.reshape(
            tile_rows, tile_cols, groups, block_length // groups, feature_channel_width
        ).astype(jnp.float32)
        * factor
    )
    return scaled.reshape(mantissa.shape).astype(jnp.bfloat16)


def shift(x, axis, count, step):
    if step > 0:
        pairs = [(i, i + step) for i in range(count - step)]
    else:
        pairs = [(i - step, i) for i in range(count + step)]
    if not pairs:
        return jnp.zeros_like(x)
    return lax.ppermute(x, axis, pairs)


def side_slots(entries, low, tile_blocks, cap):
    inside = (entries >= low) & (entries < low + tile_blocks)
    rank = jnp.cumsum(inside.astype(jnp.int32)) - 1
    slot = jnp.arange(cap, dtype=jnp.int32)[:, None]
    hit = inside[None, :] & (rank[None, :] == slot)
    return jnp.sum(jnp.where(hit, entries[None, :] - low, 0), axis=1), inside, rank


def ring_gather(item, count, me):
    order = list(range(0, count, 2)) + list(range(count - 1 - count % 2, 0, -2))
    position = [0] * count
    for place, col in enumerate(order):
        position[col] = place
    forward = [(order[i], order[(i + 1) % count]) for i in range(count)]
    backward = [(order[(i + 1) % count], order[i]) for i in range(count)]
    half = count // 2
    rows = item.shape[1]
    split = (rows + 1) // 2
    arrays = []
    lookup = [[None] * rows for _ in range(count - 1)]
    for r in range(rows):
        ahead = behind = item[:, r : r + 1]
        for distance in range(1, half + 1):
            if distance == half and count % 2 == 0:
                if r < split:
                    arrays.append(lax.ppermute(ahead, "col", forward))
                else:
                    arrays.append(lax.ppermute(behind, "col", backward))
                lookup[distance - 1][r] = (len(arrays) - 1, 0)
                continue
            ahead = lax.ppermute(ahead, "col", forward)
            arrays.append(ahead)
            lookup[distance - 1][r] = (len(arrays) - 1, 0)
            behind = lax.ppermute(behind, "col", backward)
            arrays.append(behind)
            lookup[count - distance - 1][r] = (len(arrays) - 1, 0)
    table = jnp.array(position, dtype=jnp.int32)

    def relative(col):
        return (table[me] - table[col]) % count - 1

    return arrays, lookup, relative


def gather_attention_kernel(cycle_sources, far_sources, table_ref, q_hbm, own_hbm, *rest):
    sources = rest[: cycle_sources + far_sources]
    o_ref, q_vmem, k_vmem, v_vmem, sems = rest[cycle_sources + far_sources :]
    tile_blocks = own_hbm.shape[1]
    block_length = own_hbm.shape[2]
    extra = table_ref.shape[0] // 2
    heads = q_vmem.shape[1] // HEAD_DIM

    copies = [pltpu.make_async_copy(q_hbm, q_vmem, sems.at[0, 0])]
    copies.append(pltpu.make_async_copy(own_hbm.at[0], k_vmem.at[pl.ds(0, tile_blocks)], sems.at[0, 1]))
    copies.append(pltpu.make_async_copy(own_hbm.at[1], v_vmem.at[pl.ds(0, tile_blocks)], sems.at[1, 1]))
    for c in copies:
        c.start()
    for slot in range(extra):
        src = table_ref[2 * slot]
        index = table_ref[2 * slot + 1]
        lo, hi = (0, cycle_sources) if slot < extra // 2 else (cycle_sources, cycle_sources + far_sources)
        for cand in range(lo, hi):
            @pl.when(src == cand)
            def _():
                for kv, dst in ((0, k_vmem), (1, v_vmem)):
                    pltpu.make_async_copy(
                        sources[cand].at[kv, index], dst.at[tile_blocks + slot], sems.at[kv, 2 + slot]
                    ).start()
    for c in copies:
        c.wait()
    for slot in range(extra):
        for kv, dst in ((0, k_vmem), (1, v_vmem)):
            pltpu.make_async_copy(
                own_hbm.at[kv, 0], dst.at[tile_blocks + slot], sems.at[kv, 2 + slot]
            ).wait()

    key_count = k_vmem.shape[0] * block_length

    for h in range(heads):
        lanes = pl.ds(h * HEAD_DIM, HEAD_DIM)
        q = q_vmem[:, lanes]
        k = k_vmem[:, :, lanes].reshape(key_count, HEAD_DIM)
        v = v_vmem[:, :, lanes].reshape(key_count, HEAD_DIM)
        scores = lax.dot_general(
            q, k, (((1,), (1,)), ((), ())), preferred_element_type=jnp.float32
        ) * HEAD_DIM ** (-0.5)
        row_max = jnp.max(scores, axis=1, keepdims=True)
        weights = jnp.exp(scores - row_max)
        row_total = jnp.sum(weights, axis=1, keepdims=True)
        rounded = weights.astype(jnp.bfloat16)
        blended = jnp.dot(rounded, v, preferred_element_type=jnp.float32)
        o_ref[:, lanes] = (blended / row_total).astype(o_ref.dtype)


def gather_attend(query_rows, own, cycle_list_sources, far_list_sources, table):
    token_count, width = query_rows.shape
    tile_blocks, block_length = own.shape[1], own.shape[2]
    extra = table.shape[0] // 2
    blocks = tile_blocks + extra
    key_count = blocks * block_length
    heads = width // HEAD_DIM
    n_sources = len(cycle_list_sources) + len(far_list_sources)
    kernel = functools.partial(
        gather_attention_kernel, len(cycle_list_sources), len(far_list_sources)
    )
    return pl.pallas_call(
        kernel,
        out_shape=jax.ShapeDtypeStruct((token_count, width), jnp.bfloat16),
        in_specs=[pl.BlockSpec(memory_space=pltpu.SMEM)]
        + [pl.BlockSpec(memory_space=pl.ANY)] * (2 + n_sources),
        out_specs=pl.BlockSpec(memory_space=pltpu.VMEM),
        scratch_shapes=[
            pltpu.VMEM((token_count, width), jnp.bfloat16),
            pltpu.VMEM((blocks, block_length, width), jnp.bfloat16),
            pltpu.VMEM((blocks, block_length, width), jnp.bfloat16),
            pltpu.SemaphoreType.DMA((2, 2 + extra)),
        ],
        compiler_params=pltpu.CompilerParams(vmem_limit_bytes=48 * 1024 * 1024),
        cost_estimate=pl.CostEstimate(
            flops=4 * token_count * key_count * width,
            transcendentals=token_count * key_count * heads,
            bytes_accessed=2 * (2 * token_count * width + 2 * key_count * width),
        ),
    )(table, query_rows, own, *cycle_list_sources, *far_list_sources)


def per_device(queries, key_mant, key_exp, value_mant, value_exp, cycle_list, dilated_list):
    tile_blocks = queries.shape[0]
    block_length = queries.shape[2]
    width = queries.shape[3]
    col_count = lax.axis_size("col")
    row_count = lax.axis_size("row")
    distant_rows = tile_blocks // 4
    step_spacing = col_count // DILATION_TILES
    me_col = lax.axis_index("col")

    stacked = jnp.stack([dequant(key_mant, key_exp), dequant(value_mant, value_exp)])[:, :, 0]

    above = shift(stacked[:, tile_blocks - 1 :], "row", row_count, 1)
    below = shift(stacked[:, :1], "row", row_count, -1)

    far_source = stacked[:, 0::4]
    dilated_entries = dilated_list[0, 0]
    hop_slot = dilated_entries // distant_rows
    far_row = dilated_entries % distant_rows
    if step_spacing == 1:
        far_sources, lookup, relative = ring_gather(far_source, col_count, me_col)
        hop_slot = relative((me_col + hop_slot + 1) % col_count)
    else:
        far_sources = []
        lookup = []
        for hop in range(1, DILATION_TILES):
            distance = hop * step_spacing
            route = [((i + distance) % col_count, i) for i in range(col_count)]
            far_sources.append(lax.ppermute(far_source, "col", route))
            lookup.append([(hop - 1, r) for r in range(distant_rows)])
    edge_cap = min(3 if row_count >= 2 else 4, tile_blocks)
    main_cap = edge_cap - 1 if col_count >= 3 else edge_cap
    entries = cycle_list[0, 0]
    right_entries = shift(entries, "col", col_count, -1)
    left_entries = shift(entries, "col", col_count, 1)
    to_right, _, _ = side_slots(right_entries, 2, tile_blocks, edge_cap)
    to_left, _, _ = side_slots(left_entries, 2 + tile_blocks, tile_blocks, edge_cap)
    right_payload = jnp.take(stacked, to_right, axis=1)
    left_payload = jnp.take(stacked, to_left, axis=1)
    later = far_sources[min(2, len(far_sources) - 1)]
    cycle_sources = [above, below]
    last = col_count - 1
    for slot in range(edge_cap):
        to_r = right_payload[:, slot : slot + 1]
        to_l = left_payload[:, slot : slot + 1]
        if slot > 0:
            to_r, to_l, _ = lax.optimization_barrier((to_r, to_l, later))
        if slot < main_cap:
            cycle_sources.append(shift(to_r, "col", col_count, 1))
            cycle_sources.append(shift(to_l, "col", col_count, -1))
        else:
            cycle_sources.append(lax.ppermute(to_r, "col", [(last - 1, last)]))
            cycle_sources.append(lax.ppermute(to_l, "col", [(1, 0)]))

    _, is_left, left_rank = side_slots(entries, 2, tile_blocks, edge_cap)
    _, is_right, right_rank = side_slots(entries, 2 + tile_blocks, tile_blocks, edge_cap)
    side_rank = jnp.where(is_left, left_rank, right_rank)
    cycle_src = jnp.where(
        entries == 0, 0, jnp.where(entries == 1, 1, 2 + is_right.astype(jnp.int32) + 2 * side_rank)
    )
    cycle_idx = jnp.zeros_like(entries)

    lookup_src = jnp.array([[a for a, _ in row] for row in lookup], dtype=jnp.int32)
    lookup_idx = jnp.array([[b for _, b in row] for row in lookup], dtype=jnp.int32)
    far_src = len(cycle_sources) + lookup_src[hop_slot, far_row]
    far_idx = lookup_idx[hop_slot, far_row]

    table = jnp.stack(
        [jnp.concatenate([cycle_src, far_src]), jnp.concatenate([cycle_idx, far_idx])], axis=1
    ).reshape(-1)
    token_count = tile_blocks * block_length
    result = gather_attend(
        queries.reshape(token_count, width), stacked, cycle_sources, far_sources, table
    )
    return result.reshape(queries.shape)


def solution(mesh):
    in_specs = (
        P(("groups", "row"), "col", None, None),
        P(("groups", "row"), "col", None, None),
        P(("groups", "row"), "col", None, None),
        P(("groups", "row"), "col", None, None),
        P(("groups", "row"), "col", None, None),
        P(("groups", "row"), "col", None),
        P(("groups", "row"), "col", None),
    )
    out_specs = P(("groups", "row"), "col", None, None)
    return jax.shard_map(
        per_device, mesh=mesh, in_specs=in_specs, out_specs=out_specs, check_vma=False
    )
```

```python
import functools

import jax
import jax.numpy as jnp
from jax import lax
from jax.experimental import pallas as pl
from jax.experimental.pallas import tpu as pltpu
from jax.sharding import PartitionSpec as P

HEAD_DIM = 128
DILATION_TILES = 8


def dequant(mantissa, exponent):
    tile_rows, tile_cols, block_length, feature_channel_width = mantissa.shape
    groups = exponent.shape[2]
    factor = jnp.exp2(exponent.astype(jnp.float32))[:, :, :, None, :]
    scaled = (
        mantissa.reshape(
            tile_rows, tile_cols, groups, block_length // groups, feature_channel_width
        ).astype(jnp.float32)
        * factor
    )
    return scaled.reshape(mantissa.shape).astype(jnp.bfloat16)


def shift(x, axis, count, step):
    if step > 0:
        pairs = [(i, i + step) for i in range(count - step)]
    else:
        pairs = [(i - step, i) for i in range(count + step)]
    if not pairs:
        return jnp.zeros_like(x)
    return lax.ppermute(x, axis, pairs)


def side_slots(entries, low, tile_blocks, cap):
    inside = (entries >= low) & (entries < low + tile_blocks)
    rank = jnp.cumsum(inside.astype(jnp.int32)) - 1
    slot = jnp.arange(cap, dtype=jnp.int32)[:, None]
    hit = inside[None, :] & (rank[None, :] == slot)
    return jnp.sum(jnp.where(hit, entries[None, :] - low, 0), axis=1), inside, rank


def ring_gather(item, count, me):
    order = list(range(0, count, 2)) + list(range(count - 1 - count % 2, 0, -2))
    position = [0] * count
    for place, col in enumerate(order):
        position[col] = place
    forward = [(order[i], order[(i + 1) % count]) for i in range(count)]
    backward = [(order[(i + 1) % count], order[i]) for i in range(count)]
    half = count // 2
    rows = item.shape[1]
    split = (rows + 1) // 2
    arrays = []
    lookup = [[None] * rows for _ in range(count - 1)]
    for r in range(rows):
        ahead = behind = item[:, r : r + 1]
        for distance in range(1, half + 1):
            if distance == half and count % 2 == 0:
                if r < split:
                    arrays.append(lax.ppermute(ahead, "col", forward))
                else:
                    arrays.append(lax.ppermute(behind, "col", backward))
                lookup[distance - 1][r] = (len(arrays) - 1, 0)
                continue
            ahead = lax.ppermute(ahead, "col", forward)
            arrays.append(ahead)
            lookup[distance - 1][r] = (len(arrays) - 1, 0)
            behind = lax.ppermute(behind, "col", backward)
            arrays.append(behind)
            lookup[count - distance - 1][r] = (len(arrays) - 1, 0)
    table = jnp.array(position, dtype=jnp.int32)

    def relative(col):
        return (table[me] - table[col]) % count - 1

    return arrays, lookup, relative


def gather_attention_kernel(cycle_sources, far_sources, table_ref, q_hbm, own_hbm, *rest):
    sources = rest[: cycle_sources + far_sources]
    o_ref, q_vmem, k_vmem, v_vmem, sems = rest[cycle_sources + far_sources :]
    tile_blocks = own_hbm.shape[1]
    block_length = own_hbm.shape[2]
    extra = table_ref.shape[0] // 2
    heads = q_vmem.shape[1] // HEAD_DIM

    copies = [pltpu.make_async_copy(q_hbm, q_vmem, sems.at[0, 0])]
    copies.append(pltpu.make_async_copy(own_hbm.at[0], k_vmem.at[pl.ds(0, tile_blocks)], sems.at[0, 1]))
    copies.append(pltpu.make_async_copy(own_hbm.at[1], v_vmem.at[pl.ds(0, tile_blocks)], sems.at[1, 1]))
    for c in copies:
        c.start()
    for slot in range(extra):
        src = table_ref[2 * slot]
        index = table_ref[2 * slot + 1]
        lo, hi = (0, cycle_sources) if slot < extra // 2 else (cycle_sources, cycle_sources + far_sources)
        for cand in range(lo, hi):
            @pl.when(src == cand)
            def _():
                for kv, dst in ((0, k_vmem), (1, v_vmem)):
                    pltpu.make_async_copy(
                        sources[cand].at[kv, index], dst.at[tile_blocks + slot], sems.at[kv, 2 + slot]
                    ).start()
    for c in copies:
        c.wait()
    for slot in range(extra):
        for kv, dst in ((0, k_vmem), (1, v_vmem)):
            pltpu.make_async_copy(
                own_hbm.at[kv, 0], dst.at[tile_blocks + slot], sems.at[kv, 2 + slot]
            ).wait()

    key_count = k_vmem.shape[0] * block_length

    for h in range(heads):
        lanes = pl.ds(h * HEAD_DIM, HEAD_DIM)
        q = q_vmem[:, lanes]
        k = k_vmem[:, :, lanes].reshape(key_count, HEAD_DIM)
        v = v_vmem[:, :, lanes].reshape(key_count, HEAD_DIM)
        scores = lax.dot_general(
            q, k, (((1,), (1,)), ((), ())), preferred_element_type=jnp.float32
        ) * HEAD_DIM ** (-0.5)
        row_max = jnp.max(scores, axis=1, keepdims=True)
        weights = jnp.exp(scores - row_max)
        row_total = jnp.sum(weights, axis=1, keepdims=True)
        rounded = weights.astype(jnp.bfloat16)
        blended = jnp.dot(rounded, v, preferred_element_type=jnp.float32)
        o_ref[:, lanes] = (blended / row_total).astype(o_ref.dtype)


def gather_attend(query_rows, own, cycle_list_sources, far_list_sources, table):
    token_count, width = query_rows.shape
    tile_blocks, block_length = own.shape[1], own.shape[2]
    extra = table.shape[0] // 2
    blocks = tile_blocks + extra
    key_count = blocks * block_length
    heads = width // HEAD_DIM
    n_sources = len(cycle_list_sources) + len(far_list_sources)
    kernel = functools.partial(
        gather_attention_kernel, len(cycle_list_sources), len(far_list_sources)
    )
    return pl.pallas_call(
        kernel,
        out_shape=jax.ShapeDtypeStruct((token_count, width), jnp.bfloat16),
        in_specs=[pl.BlockSpec(memory_space=pltpu.SMEM)]
        + [pl.BlockSpec(memory_space=pl.ANY)] * (2 + n_sources),
        out_specs=pl.BlockSpec(memory_space=pltpu.VMEM),
        scratch_shapes=[
            pltpu.VMEM((token_count, width), jnp.bfloat16),
            pltpu.VMEM((blocks, block_length, width), jnp.bfloat16),
            pltpu.VMEM((blocks, block_length, width), jnp.bfloat16),
            pltpu.SemaphoreType.DMA((2, 2 + extra)),
        ],
        compiler_params=pltpu.CompilerParams(vmem_limit_bytes=48 * 1024 * 1024),
        cost_estimate=pl.CostEstimate(
            flops=4 * token_count * key_count * width,
            transcendentals=token_count * key_count * heads,
            bytes_accessed=2 * (2 * token_count * width + 2 * key_count * width),
        ),
    )(table, query_rows, own, *cycle_list_sources, *far_list_sources)


def per_device(queries, key_mant, key_exp, value_mant, value_exp, cycle_list, dilated_list):
    tile_blocks = queries.shape[0]
    block_length = queries.shape[2]
    width = queries.shape[3]
    col_count = lax.axis_size("col")
    row_count = lax.axis_size("row")
    distant_rows = tile_blocks // 4
    step_spacing = col_count // DILATION_TILES
    me_col = lax.axis_index("col")

    stacked = jnp.stack([dequant(key_mant, key_exp), dequant(value_mant, value_exp)])[:, :, 0]

    above = shift(stacked[:, tile_blocks - 1 :], "row", row_count, 1)
    below = shift(stacked[:, :1], "row", row_count, -1)

    far_source = stacked[:, 0::4]
    dilated_entries = dilated_list[0, 0]
    hop_slot = dilated_entries // distant_rows
    far_row = dilated_entries % distant_rows
    if step_spacing == 1:
        far_sources, lookup, relative = ring_gather(far_source, col_count, me_col)
        hop_slot = relative((me_col + hop_slot + 1) % col_count)
    else:
        far_sources = []
        lookup = []
        for hop in range(1, DILATION_TILES):
            distance = hop * step_spacing
            route = [((i + distance) % col_count, i) for i in range(col_count)]
            far_sources.append(lax.ppermute(far_source, "col", route))
            lookup.append([(hop - 1, r) for r in range(distant_rows)])
    edge_cap = min(3 if row_count >= 2 else 4, tile_blocks)
    main_cap = edge_cap - 1 if col_count >= 3 else edge_cap
    entries = cycle_list[0, 0]
    right_entries = shift(entries, "col", col_count, -1)
    left_entries = shift(entries, "col", col_count, 1)
    to_right, _, _ = side_slots(right_entries, 2, tile_blocks, edge_cap)
    to_left, _, _ = side_slots(left_entries, 2 + tile_blocks, tile_blocks, edge_cap)
    right_payload = jnp.take(stacked, to_right, axis=1)
    left_payload = jnp.take(stacked, to_left, axis=1)
    cycle_sources = [above, below]
    last = col_count - 1
    for slot in range(edge_cap):
        to_r = right_payload[:, slot : slot + 1]
        to_l = left_payload[:, slot : slot + 1]
        later = far_sources[min(2 * slot, len(far_sources) - 1)]
        to_r, to_l, _ = lax.optimization_barrier((to_r, to_l, later))
        if slot < main_cap:
            cycle_sources.append(shift(to_r, "col", col_count, 1))
            cycle_sources.append(shift(to_l, "col", col_count, -1))
        else:
            cycle_sources.append(lax.ppermute(to_r, "col", [(last - 1, last)]))
            cycle_sources.append(lax.ppermute(to_l, "col", [(1, 0)]))

    _, is_left, left_rank = side_slots(entries, 2, tile_blocks, edge_cap)
    _, is_right, right_rank = side_slots(entries, 2 + tile_blocks, tile_blocks, edge_cap)
    side_rank = jnp.where(is_left, left_rank, right_rank)
    cycle_src = jnp.where(
        entries == 0, 0, jnp.where(entries == 1, 1, 2 + is_right.astype(jnp.int32) + 2 * side_rank)
    )
    cycle_idx = jnp.zeros_like(entries)

    lookup_src = jnp.array([[a for a, _ in row] for row in lookup], dtype=jnp.int32)
    lookup_idx = jnp.array([[b for _, b in row] for row in lookup], dtype=jnp.int32)
    far_src = len(cycle_sources) + lookup_src[hop_slot, far_row]
    far_idx = lookup_idx[hop_slot, far_row]

    table = jnp.stack(
        [jnp.concatenate([cycle_src, far_src]), jnp.concatenate([cycle_idx, far_idx])], axis=1
    ).reshape(-1)
    token_count = tile_blocks * block_length
    result = gather_attend(
        queries.reshape(token_count, width), stacked, cycle_sources, far_sources, table
    )
    return result.reshape(queries.shape)


def solution(mesh):
    in_specs = (
        P(("groups", "row"), "col", None, None),
        P(("groups", "row"), "col", None, None),
        P(("groups", "row"), "col", None, None),
        P(("groups", "row"), "col", None, None),
        P(("groups", "row"), "col", None, None),
        P(("groups", "row"), "col", None),
        P(("groups", "row"), "col", None),
    )
    out_specs = P(("groups", "row"), "col", None, None)
    return jax.shard_map(
        per_device, mesh=mesh, in_specs=in_specs, out_specs=out_specs, check_vma=False
    )
```

```python
import functools

import jax
import jax.numpy as jnp
from jax import lax
from jax.experimental import pallas as pl
from jax.experimental.pallas import tpu as pltpu
from jax.sharding import PartitionSpec as P

HEAD_DIM = 128
DILATION_TILES = 8


def dequant(mantissa, exponent):
    tile_rows, tile_cols, block_length, feature_channel_width = mantissa.shape
    groups = exponent.shape[2]
    factor = jnp.exp2(exponent.astype(jnp.float32))[:, :, :, None, :]
    scaled = (
        mantissa.reshape(
            tile_rows, tile_cols, groups, block_length // groups, feature_channel_width
        ).astype(jnp.float32)
        * factor
    )
    return scaled.reshape(mantissa.shape).astype(jnp.bfloat16)


def shift(x, axis, count, step):
    if step > 0:
        pairs = [(i, i + step) for i in range(count - step)]
    else:
        pairs = [(i - step, i) for i in range(count + step)]
    if not pairs:
        return jnp.zeros_like(x)
    return lax.ppermute(x, axis, pairs)


def side_slots(entries, low, tile_blocks, cap):
    inside = (entries >= low) & (entries < low + tile_blocks)
    rank = jnp.cumsum(inside.astype(jnp.int32)) - 1
    slot = jnp.arange(cap, dtype=jnp.int32)[:, None]
    hit = inside[None, :] & (rank[None, :] == slot)
    return jnp.sum(jnp.where(hit, entries[None, :] - low, 0), axis=1), inside, rank


def ring_gather(item, count, me):
    order = list(range(0, count, 2)) + list(range(count - 1 - count % 2, 0, -2))
    position = [0] * count
    for place, col in enumerate(order):
        position[col] = place
    forward = [(order[i], order[(i + 1) % count]) for i in range(count)]
    backward = [(order[(i + 1) % count], order[i]) for i in range(count)]
    half = count // 2
    rows = item.shape[1]
    split = (rows + 1) // 2
    arrays = []
    lookup = [[None] * rows for _ in range(count - 1)]
    for r in range(rows):
        ahead = behind = item[:, r : r + 1]
        for distance in range(1, half + 1):
            if distance == half and count % 2 == 0:
                if r < split:
                    arrays.append(lax.ppermute(ahead, "col", forward))
                else:
                    arrays.append(lax.ppermute(behind, "col", backward))
                lookup[distance - 1][r] = (len(arrays) - 1, 0)
                continue
            ahead = lax.ppermute(ahead, "col", forward)
            arrays.append(ahead)
            lookup[distance - 1][r] = (len(arrays) - 1, 0)
            behind = lax.ppermute(behind, "col", backward)
            arrays.append(behind)
            lookup[count - distance - 1][r] = (len(arrays) - 1, 0)
    table = jnp.array(position, dtype=jnp.int32)

    def relative(col):
        return (table[me] - table[col]) % count - 1

    return arrays, lookup, relative


def gather_attention_kernel(cycle_sources, far_sources, table_ref, q_hbm, own_hbm, *rest):
    sources = rest[: cycle_sources + far_sources]
    o_ref, q_vmem, k_vmem, v_vmem, sems = rest[cycle_sources + far_sources :]
    tile_blocks = own_hbm.shape[1]
    block_length = own_hbm.shape[2]
    extra = table_ref.shape[0] // 2
    heads = q_vmem.shape[1] // HEAD_DIM

    copies = [pltpu.make_async_copy(q_hbm, q_vmem, sems.at[0, 0])]
    copies.append(pltpu.make_async_copy(own_hbm.at[0], k_vmem.at[pl.ds(0, tile_blocks)], sems.at[0, 1]))
    copies.append(pltpu.make_async_copy(own_hbm.at[1], v_vmem.at[pl.ds(0, tile_blocks)], sems.at[1, 1]))
    for c in copies:
        c.start()
    for slot in range(extra):
        src = table_ref[2 * slot]
        index = table_ref[2 * slot + 1]
        lo, hi = (0, cycle_sources) if slot < extra // 2 else (cycle_sources, cycle_sources + far_sources)
        for cand in range(lo, hi):
            @pl.when(src == cand)
            def _():
                for kv, dst in ((0, k_vmem), (1, v_vmem)):
                    pltpu.make_async_copy(
                        sources[cand].at[kv, index], dst.at[tile_blocks + slot], sems.at[kv, 2 + slot]
                    ).start()
    for c in copies:
        c.wait()
    for slot in range(extra):
        for kv, dst in ((0, k_vmem), (1, v_vmem)):
            pltpu.make_async_copy(
                own_hbm.at[kv, 0], dst.at[tile_blocks + slot], sems.at[kv, 2 + slot]
            ).wait()

    key_count = k_vmem.shape[0] * block_length

    for h in range(heads):
        lanes = pl.ds(h * HEAD_DIM, HEAD_DIM)
        q = q_vmem[:, lanes]
        k = k_vmem[:, :, lanes].reshape(key_count, HEAD_DIM)
        v = v_vmem[:, :, lanes].reshape(key_count, HEAD_DIM)
        scores = lax.dot_general(
            q, k, (((1,), (1,)), ((), ())), preferred_element_type=jnp.float32
        ) * HEAD_DIM ** (-0.5)
        row_max = jnp.max(scores, axis=1, keepdims=True)
        weights = jnp.exp(scores - row_max)
        row_total = jnp.sum(weights, axis=1, keepdims=True)
        rounded = weights.astype(jnp.bfloat16)
        blended = jnp.dot(rounded, v, preferred_element_type=jnp.float32)
        o_ref[:, lanes] = (blended / row_total).astype(o_ref.dtype)


def gather_attend(query_rows, own, cycle_list_sources, far_list_sources, table):
    token_count, width = query_rows.shape
    tile_blocks, block_length = own.shape[1], own.shape[2]
    extra = table.shape[0] // 2
    blocks = tile_blocks + extra
    key_count = blocks * block_length
    heads = width // HEAD_DIM
    n_sources = len(cycle_list_sources) + len(far_list_sources)
    kernel = functools.partial(
        gather_attention_kernel, len(cycle_list_sources), len(far_list_sources)
    )
    return pl.pallas_call(
        kernel,
        out_shape=jax.ShapeDtypeStruct((token_count, width), jnp.bfloat16),
        in_specs=[pl.BlockSpec(memory_space=pltpu.SMEM)]
        + [pl.BlockSpec(memory_space=pl.ANY)] * (2 + n_sources),
        out_specs=pl.BlockSpec(memory_space=pltpu.VMEM),
        scratch_shapes=[
            pltpu.VMEM((token_count, width), jnp.bfloat16),
            pltpu.VMEM((blocks, block_length, width), jnp.bfloat16),
            pltpu.VMEM((blocks, block_length, width), jnp.bfloat16),
            pltpu.SemaphoreType.DMA((2, 2 + extra)),
        ],
        compiler_params=pltpu.CompilerParams(vmem_limit_bytes=48 * 1024 * 1024),
        cost_estimate=pl.CostEstimate(
            flops=4 * token_count * key_count * width,
            transcendentals=token_count * key_count * heads,
            bytes_accessed=2 * (2 * token_count * width + 2 * key_count * width),
        ),
    )(table, query_rows, own, *cycle_list_sources, *far_list_sources)


def per_device(queries, key_mant, key_exp, value_mant, value_exp, cycle_list, dilated_list):
    tile_blocks = queries.shape[0]
    block_length = queries.shape[2]
    width = queries.shape[3]
    col_count = lax.axis_size("col")
    row_count = lax.axis_size("row")
    distant_rows = tile_blocks // 4
    step_spacing = col_count // DILATION_TILES
    me_col = lax.axis_index("col")

    stacked = jnp.stack([dequant(key_mant, key_exp), dequant(value_mant, value_exp)])[:, :, 0]

    above = shift(stacked[:, tile_blocks - 1 :], "row", row_count, 1)
    below = shift(stacked[:, :1], "row", row_count, -1)

    far_source = jnp.stack(
        [dequant(key_mant[0::4], key_exp[0::4]), dequant(value_mant[0::4], value_exp[0::4])]
    )[:, :, 0]
    dilated_entries = dilated_list[0, 0]
    hop_slot = dilated_entries // distant_rows
    far_row = dilated_entries % distant_rows
    if step_spacing == 1:
        far_sources, lookup, relative = ring_gather(far_source, col_count, me_col)
        hop_slot = relative((me_col + hop_slot + 1) % col_count)
    else:
        far_sources = []
        lookup = []
        for hop in range(1, DILATION_TILES):
            distance = hop * step_spacing
            route = [((i + distance) % col_count, i) for i in range(col_count)]
            far_sources.append(lax.ppermute(far_source, "col", route))
            lookup.append([(hop - 1, r) for r in range(distant_rows)])
    edge_cap = min(3 if row_count >= 2 else 4, tile_blocks)
    main_cap = edge_cap - 1 if col_count >= 3 else edge_cap
    entries = cycle_list[0, 0]
    right_entries = shift(entries, "col", col_count, -1)
    left_entries = shift(entries, "col", col_count, 1)
    to_right, _, _ = side_slots(right_entries, 2, tile_blocks, edge_cap)
    to_left, _, _ = side_slots(left_entries, 2 + tile_blocks, tile_blocks, edge_cap)
    right_payload = jnp.take(stacked, to_right, axis=1)
    left_payload = jnp.take(stacked, to_left, axis=1)
    cycle_sources = [above, below]
    last = col_count - 1
    for slot in range(edge_cap):
        to_r = right_payload[:, slot : slot + 1]
        to_l = left_payload[:, slot : slot + 1]
        later = far_sources[min(2 * slot, len(far_sources) - 1)]
        to_r, to_l, _ = lax.optimization_barrier((to_r, to_l, later))
        if slot < main_cap:
            cycle_sources.append(shift(to_r, "col", col_count, 1))
            cycle_sources.append(shift(to_l, "col", col_count, -1))
        else:
            cycle_sources.append(lax.ppermute(to_r, "col", [(last - 1, last)]))
            cycle_sources.append(lax.ppermute(to_l, "col", [(1, 0)]))

    _, is_left, left_rank = side_slots(entries, 2, tile_blocks, edge_cap)
    _, is_right, right_rank = side_slots(entries, 2 + tile_blocks, tile_blocks, edge_cap)
    side_rank = jnp.where(is_left, left_rank, right_rank)
    cycle_src = jnp.where(
        entries == 0, 0, jnp.where(entries == 1, 1, 2 + is_right.astype(jnp.int32) + 2 * side_rank)
    )
    cycle_idx = jnp.zeros_like(entries)

    lookup_src = jnp.array([[a for a, _ in row] for row in lookup], dtype=jnp.int32)
    lookup_idx = jnp.array([[b for _, b in row] for row in lookup], dtype=jnp.int32)
    far_src = len(cycle_sources) + lookup_src[hop_slot, far_row]
    far_idx = lookup_idx[hop_slot, far_row]

    table = jnp.stack(
        [jnp.concatenate([cycle_src, far_src]), jnp.concatenate([cycle_idx, far_idx])], axis=1
    ).reshape(-1)
    token_count = tile_blocks * block_length
    result = gather_attend(
        queries.reshape(token_count, width), stacked, cycle_sources, far_sources, table
    )
    return result.reshape(queries.shape)


def solution(mesh):
    in_specs = (
        P(("groups", "row"), "col", None, None),
        P(("groups", "row"), "col", None, None),
        P(("groups", "row"), "col", None, None),
        P(("groups", "row"), "col", None, None),
        P(("groups", "row"), "col", None, None),
        P(("groups", "row"), "col", None),
        P(("groups", "row"), "col", None),
    )
    out_specs = P(("groups", "row"), "col", None, None)
    return jax.shard_map(
        per_device, mesh=mesh, in_specs=in_specs, out_specs=out_specs, check_vma=False
    )
```

```python
import functools

import jax
import jax.numpy as jnp
from jax import lax
from jax.experimental import pallas as pl
from jax.experimental.pallas import tpu as pltpu
from jax.sharding import PartitionSpec as P

HEAD_DIM = 128
DILATION_TILES = 8


def dequant(mantissa, exponent):
    tile_rows, tile_cols, block_length, feature_channel_width = mantissa.shape
    groups = exponent.shape[2]
    factor = jnp.exp2(exponent.astype(jnp.float32))[:, :, :, None, :]
    scaled = (
        mantissa.reshape(
            tile_rows, tile_cols, groups, block_length // groups, feature_channel_width
        ).astype(jnp.float32)
        * factor
    )
    return scaled.reshape(mantissa.shape).astype(jnp.bfloat16)


def shift(x, axis, count, step):
    if step > 0:
        pairs = [(i, i + step) for i in range(count - step)]
    else:
        pairs = [(i - step, i) for i in range(count + step)]
    if not pairs:
        return jnp.zeros_like(x)
    return lax.ppermute(x, axis, pairs)


def side_slots(entries, low, tile_blocks, cap):
    inside = (entries >= low) & (entries < low + tile_blocks)
    rank = jnp.cumsum(inside.astype(jnp.int32)) - 1
    slot = jnp.arange(cap, dtype=jnp.int32)[:, None]
    hit = inside[None, :] & (rank[None, :] == slot)
    return jnp.sum(jnp.where(hit, entries[None, :] - low, 0), axis=1), inside, rank


def ring_gather(item, count, me):
    order = list(range(0, count, 2)) + list(range(count - 1 - count % 2, 0, -2))
    position = [0] * count
    for place, col in enumerate(order):
        position[col] = place
    forward = [(order[i], order[(i + 1) % count]) for i in range(count)]
    backward = [(order[(i + 1) % count], order[i]) for i in range(count)]
    half = count // 2
    rows = item.shape[1]
    split = (rows + 1) // 2
    arrays = []
    lookup = [[None] * rows for _ in range(count - 1)]
    first_hop = None
    for r in range(rows):
        ahead = behind = item[:, r : r + 1]
        if first_hop is not None:
            ahead, _ = lax.optimization_barrier((ahead, arrays[first_hop]))
            behind = ahead
        first_hop = len(arrays)
        for distance in range(1, half + 1):
            if distance == half and count % 2 == 0:
                if r < split:
                    arrays.append(lax.ppermute(ahead, "col", forward))
                else:
                    arrays.append(lax.ppermute(behind, "col", backward))
                lookup[distance - 1][r] = (len(arrays) - 1, 0)
                continue
            ahead = lax.ppermute(ahead, "col", forward)
            arrays.append(ahead)
            lookup[distance - 1][r] = (len(arrays) - 1, 0)
            behind = lax.ppermute(behind, "col", backward)
            arrays.append(behind)
            lookup[count - distance - 1][r] = (len(arrays) - 1, 0)
    table = jnp.array(position, dtype=jnp.int32)

    def relative(col):
        return (table[me] - table[col]) % count - 1

    return arrays, lookup, relative


def gather_attention_kernel(cycle_sources, far_sources, table_ref, q_hbm, own_hbm, *rest):
    sources = rest[: cycle_sources + far_sources]
    o_ref, q_vmem, k_vmem, v_vmem, sems = rest[cycle_sources + far_sources :]
    tile_blocks = own_hbm.shape[1]
    block_length = own_hbm.shape[2]
    extra = table_ref.shape[0] // 2
    heads = q_vmem.shape[1] // HEAD_DIM

    copies = [pltpu.make_async_copy(q_hbm, q_vmem, sems.at[0, 0])]
    copies.append(pltpu.make_async_copy(own_hbm.at[0], k_vmem.at[pl.ds(0, tile_blocks)], sems.at[0, 1]))
    copies.append(pltpu.make_async_copy(own_hbm.at[1], v_vmem.at[pl.ds(0, tile_blocks)], sems.at[1, 1]))
    for c in copies:
        c.start()
    for slot in range(extra):
        src = table_ref[2 * slot]
        index = table_ref[2 * slot + 1]
        lo, hi = (0, cycle_sources) if slot < extra // 2 else (cycle_sources, cycle_sources + far_sources)
        for cand in range(lo, hi):
            @pl.when(src == cand)
            def _():
                for kv, dst in ((0, k_vmem), (1, v_vmem)):
                    pltpu.make_async_copy(
                        sources[cand].at[kv, index], dst.at[tile_blocks + slot], sems.at[kv, 2 + slot]
                    ).start()
    for c in copies:
        c.wait()
    for slot in range(extra):
        for kv, dst in ((0, k_vmem), (1, v_vmem)):
            pltpu.make_async_copy(
                own_hbm.at[kv, 0], dst.at[tile_blocks + slot], sems.at[kv, 2 + slot]
            ).wait()

    key_count = k_vmem.shape[0] * block_length

    for h in range(heads):
        lanes = pl.ds(h * HEAD_DIM, HEAD_DIM)
        q = q_vmem[:, lanes]
        k = k_vmem[:, :, lanes].reshape(key_count, HEAD_DIM)
        v = v_vmem[:, :, lanes].reshape(key_count, HEAD_DIM)
        scores = lax.dot_general(
            q, k, (((1,), (1,)), ((), ())), preferred_element_type=jnp.float32
        ) * HEAD_DIM ** (-0.5)
        row_max = jnp.max(scores, axis=1, keepdims=True)
        weights = jnp.exp(scores - row_max)
        row_total = jnp.sum(weights, axis=1, keepdims=True)
        rounded = weights.astype(jnp.bfloat16)
        blended = jnp.dot(rounded, v, preferred_element_type=jnp.float32)
        o_ref[:, lanes] = (blended / row_total).astype(o_ref.dtype)


def gather_attend(query_rows, own, cycle_list_sources, far_list_sources, table):
    token_count, width = query_rows.shape
    tile_blocks, block_length = own.shape[1], own.shape[2]
    extra = table.shape[0] // 2
    blocks = tile_blocks + extra
    key_count = blocks * block_length
    heads = width // HEAD_DIM
    n_sources = len(cycle_list_sources) + len(far_list_sources)
    kernel = functools.partial(
        gather_attention_kernel, len(cycle_list_sources), len(far_list_sources)
    )
    return pl.pallas_call(
        kernel,
        out_shape=jax.ShapeDtypeStruct((token_count, width), jnp.bfloat16),
        in_specs=[pl.BlockSpec(memory_space=pltpu.SMEM)]
        + [pl.BlockSpec(memory_space=pl.ANY)] * (2 + n_sources),
        out_specs=pl.BlockSpec(memory_space=pltpu.VMEM),
        scratch_shapes=[
            pltpu.VMEM((token_count, width), jnp.bfloat16),
            pltpu.VMEM((blocks, block_length, width), jnp.bfloat16),
            pltpu.VMEM((blocks, block_length, width), jnp.bfloat16),
            pltpu.SemaphoreType.DMA((2, 2 + extra)),
        ],
        compiler_params=pltpu.CompilerParams(vmem_limit_bytes=48 * 1024 * 1024),
        cost_estimate=pl.CostEstimate(
            flops=4 * token_count * key_count * width,
            transcendentals=token_count * key_count * heads,
            bytes_accessed=2 * (2 * token_count * width + 2 * key_count * width),
        ),
    )(table, query_rows, own, *cycle_list_sources, *far_list_sources)


def per_device(queries, key_mant, key_exp, value_mant, value_exp, cycle_list, dilated_list):
    tile_blocks = queries.shape[0]
    block_length = queries.shape[2]
    width = queries.shape[3]
    col_count = lax.axis_size("col")
    row_count = lax.axis_size("row")
    distant_rows = tile_blocks // 4
    step_spacing = col_count // DILATION_TILES
    me_col = lax.axis_index("col")

    stacked = jnp.stack([dequant(key_mant, key_exp), dequant(value_mant, value_exp)])[:, :, 0]

    above = shift(stacked[:, tile_blocks - 1 :], "row", row_count, 1)
    below = shift(stacked[:, :1], "row", row_count, -1)

    far_source = stacked[:, 0::4]
    dilated_entries = dilated_list[0, 0]
    hop_slot = dilated_entries // distant_rows
    far_row = dilated_entries % distant_rows
    if step_spacing == 1:
        far_sources, lookup, relative = ring_gather(far_source, col_count, me_col)
        hop_slot = relative((me_col + hop_slot + 1) % col_count)
    else:
        far_sources = []
        lookup = []
        for hop in range(1, DILATION_TILES):
            distance = hop * step_spacing
            route = [((i + distance) % col_count, i) for i in range(col_count)]
            far_sources.append(lax.ppermute(far_source, "col", route))
            lookup.append([(hop - 1, r) for r in range(distant_rows)])
    edge_cap = min(3 if row_count >= 2 else 4, tile_blocks)
    main_cap = edge_cap - 1 if col_count >= 3 else edge_cap
    entries = cycle_list[0, 0]
    right_entries = shift(entries, "col", col_count, -1)
    left_entries = shift(entries, "col", col_count, 1)
    to_right, _, _ = side_slots(right_entries, 2, tile_blocks, edge_cap)
    to_left, _, _ = side_slots(left_entries, 2 + tile_blocks, tile_blocks, edge_cap)
    right_payload = jnp.take(stacked, to_right, axis=1)
    left_payload = jnp.take(stacked, to_left, axis=1)
    cycle_sources = [above, below]
    last = col_count - 1
    for slot in range(edge_cap):
        to_r = right_payload[:, slot : slot + 1]
        to_l = left_payload[:, slot : slot + 1]
        later = far_sources[min(2 * slot, len(far_sources) - 1)]
        to_r, to_l, _ = lax.optimization_barrier((to_r, to_l, later))
        if slot < main_cap:
            cycle_sources.append(shift(to_r, "col", col_count, 1))
            cycle_sources.append(shift(to_l, "col", col_count, -1))
        else:
            cycle_sources.append(lax.ppermute(to_r, "col", [(last - 1, last)]))
            cycle_sources.append(lax.ppermute(to_l, "col", [(1, 0)]))

    _, is_left, left_rank = side_slots(entries, 2, tile_blocks, edge_cap)
    _, is_right, right_rank = side_slots(entries, 2 + tile_blocks, tile_blocks, edge_cap)
    side_rank = jnp.where(is_left, left_rank, right_rank)
    cycle_src = jnp.where(
        entries == 0, 0, jnp.where(entries == 1, 1, 2 + is_right.astype(jnp.int32) + 2 * side_rank)
    )
    cycle_idx = jnp.zeros_like(entries)

    lookup_src = jnp.array([[a for a, _ in row] for row in lookup], dtype=jnp.int32)
    lookup_idx = jnp.array([[b for _, b in row] for row in lookup], dtype=jnp.int32)
    far_src = len(cycle_sources) + lookup_src[hop_slot, far_row]
    far_idx = lookup_idx[hop_slot, far_row]

    table = jnp.stack(
        [jnp.concatenate([cycle_src, far_src]), jnp.concatenate([cycle_idx, far_idx])], axis=1
    ).reshape(-1)
    token_count = tile_blocks * block_length
    result = gather_attend(
        queries.reshape(token_count, width), stacked, cycle_sources, far_sources, table
    )
    return result.reshape(queries.shape)


def solution(mesh):
    in_specs = (
        P(("groups", "row"), "col", None, None),
        P(("groups", "row"), "col", None, None),
        P(("groups", "row"), "col", None, None),
        P(("groups", "row"), "col", None, None),
        P(("groups", "row"), "col", None, None),
        P(("groups", "row"), "col", None),
        P(("groups", "row"), "col", None),
    )
    out_specs = P(("groups", "row"), "col", None, None)
    return jax.shard_map(
        per_device, mesh=mesh, in_specs=in_specs, out_specs=out_specs, check_vma=False
    )
```

```python
import functools

import jax
import jax.numpy as jnp
from jax import lax
from jax.experimental import pallas as pl
from jax.experimental.pallas import tpu as pltpu
from jax.sharding import PartitionSpec as P

HEAD_DIM = 128
DILATION_TILES = 8


def dequant(mantissa, exponent):
    tile_rows, tile_cols, block_length, feature_channel_width = mantissa.shape
    groups = exponent.shape[2]
    factor = jnp.exp2(exponent.astype(jnp.float32))[:, :, :, None, :]
    scaled = (
        mantissa.reshape(
            tile_rows, tile_cols, groups, block_length // groups, feature_channel_width
        ).astype(jnp.float32)
        * factor
    )
    return scaled.reshape(mantissa.shape).astype(jnp.bfloat16)


def shift(x, axis, count, step):
    if step > 0:
        pairs = [(i, i + step) for i in range(count - step)]
    else:
        pairs = [(i - step, i) for i in range(count + step)]
    if not pairs:
        return jnp.zeros_like(x)
    return lax.ppermute(x, axis, pairs)


def side_slots(entries, low, tile_blocks, cap):
    inside = (entries >= low) & (entries < low + tile_blocks)
    rank = jnp.cumsum(inside.astype(jnp.int32)) - 1
    slot = jnp.arange(cap, dtype=jnp.int32)[:, None]
    hit = inside[None, :] & (rank[None, :] == slot)
    return jnp.sum(jnp.where(hit, entries[None, :] - low, 0), axis=1), inside, rank


def ring_gather(item, count, me):
    order = list(range(0, count, 2)) + list(range(count - 1 - count % 2, 0, -2))
    position = [0] * count
    for place, col in enumerate(order):
        position[col] = place
    forward = [(order[i], order[(i + 1) % count]) for i in range(count)]
    backward = [(order[(i + 1) % count], order[i]) for i in range(count)]
    half = count // 2
    rows = item.shape[1]
    split = (rows + 1) // 2
    arrays = []
    lookup = [[None] * rows for _ in range(count - 1)]
    for r in range(rows):
        ahead = behind = item[:, r : r + 1]
        for distance in range(1, half + 1):
            if distance == half and count % 2 == 0:
                if r < split:
                    arrays.append(lax.ppermute(ahead, "col", forward))
                else:
                    arrays.append(lax.ppermute(behind, "col", backward))
                lookup[distance - 1][r] = (len(arrays) - 1, 0)
                continue
            ahead = lax.ppermute(ahead, "col", forward)
            arrays.append(ahead)
            lookup[distance - 1][r] = (len(arrays) - 1, 0)
            behind = lax.ppermute(behind, "col", backward)
            arrays.append(behind)
            lookup[count - distance - 1][r] = (len(arrays) - 1, 0)
    table = jnp.array(position, dtype=jnp.int32)

    def relative(col):
        return (table[me] - table[col]) % count - 1

    return arrays, lookup, relative


def gather_attention_kernel(cycle_sources, far_sources, table_ref, q_hbm, own_hbm, *rest):
    sources = rest[: cycle_sources + far_sources]
    o_ref, q_vmem, k_vmem, v_vmem, sems = rest[cycle_sources + far_sources :]
    tile_blocks = own_hbm.shape[1]
    block_length = own_hbm.shape[2]
    extra = table_ref.shape[0] // 2
    heads = q_vmem.shape[1] // HEAD_DIM

    copies = [pltpu.make_async_copy(q_hbm, q_vmem, sems.at[0, 0])]
    copies.append(pltpu.make_async_copy(own_hbm.at[0], k_vmem.at[pl.ds(0, tile_blocks)], sems.at[0, 1]))
    copies.append(pltpu.make_async_copy(own_hbm.at[1], v_vmem.at[pl.ds(0, tile_blocks)], sems.at[1, 1]))
    for c in copies:
        c.start()
    for slot in range(extra):
        src = table_ref[2 * slot]
        index = table_ref[2 * slot + 1]
        lo, hi = (0, cycle_sources) if slot < extra // 2 else (cycle_sources, cycle_sources + far_sources)
        for cand in range(lo, hi):
            @pl.when(src == cand)
            def _():
                for kv, dst in ((0, k_vmem), (1, v_vmem)):
                    pltpu.make_async_copy(
                        sources[cand].at[kv, index], dst.at[tile_blocks + slot], sems.at[kv, 2 + slot]
                    ).start()
    for c in copies:
        c.wait()
    for slot in range(extra):
        for kv, dst in ((0, k_vmem), (1, v_vmem)):
            pltpu.make_async_copy(
                own_hbm.at[kv, 0], dst.at[tile_blocks + slot], sems.at[kv, 2 + slot]
            ).wait()

    key_count = k_vmem.shape[0] * block_length

    for h in range(heads):
        lanes = pl.ds(h * HEAD_DIM, HEAD_DIM)
        q = q_vmem[:, lanes]
        k = k_vmem[:, :, lanes].reshape(key_count, HEAD_DIM)
        v = v_vmem[:, :, lanes].reshape(key_count, HEAD_DIM)
        scores = lax.dot_general(
            k, q, (((1,), (1,)), ((), ())), preferred_element_type=jnp.float32
        ) * HEAD_DIM ** (-0.5)
        col_max = jnp.max(scores, axis=0, keepdims=True)
        weights = jnp.exp(scores - col_max)
        col_total = jnp.sum(weights, axis=0, keepdims=True)
        rounded = weights.astype(jnp.bfloat16)
        blended = lax.dot_general(
            v, rounded, (((0,), (0,)), ((), ())), preferred_element_type=jnp.float32
        )
        o_ref[:, lanes] = (blended / col_total).T.astype(o_ref.dtype)


def gather_attend(query_rows, own, cycle_list_sources, far_list_sources, table):
    token_count, width = query_rows.shape
    tile_blocks, block_length = own.shape[1], own.shape[2]
    extra = table.shape[0] // 2
    blocks = tile_blocks + extra
    key_count = blocks * block_length
    heads = width // HEAD_DIM
    n_sources = len(cycle_list_sources) + len(far_list_sources)
    kernel = functools.partial(
        gather_attention_kernel, len(cycle_list_sources), len(far_list_sources)
    )
    return pl.pallas_call(
        kernel,
        out_shape=jax.ShapeDtypeStruct((token_count, width), jnp.bfloat16),
        in_specs=[pl.BlockSpec(memory_space=pltpu.SMEM)]
        + [pl.BlockSpec(memory_space=pl.ANY)] * (2 + n_sources),
        out_specs=pl.BlockSpec(memory_space=pltpu.VMEM),
        scratch_shapes=[
            pltpu.VMEM((token_count, width), jnp.bfloat16),
            pltpu.VMEM((blocks, block_length, width), jnp.bfloat16),
            pltpu.VMEM((blocks, block_length, width), jnp.bfloat16),
            pltpu.SemaphoreType.DMA((2, 2 + extra)),
        ],
        compiler_params=pltpu.CompilerParams(vmem_limit_bytes=48 * 1024 * 1024),
        cost_estimate=pl.CostEstimate(
            flops=4 * token_count * key_count * width,
            transcendentals=token_count * key_count * heads,
            bytes_accessed=2 * (2 * token_count * width + 2 * key_count * width),
        ),
    )(table, query_rows, own, *cycle_list_sources, *far_list_sources)


def per_device(queries, key_mant, key_exp, value_mant, value_exp, cycle_list, dilated_list):
    tile_blocks = queries.shape[0]
    block_length = queries.shape[2]
    width = queries.shape[3]
    col_count = lax.axis_size("col")
    row_count = lax.axis_size("row")
    distant_rows = tile_blocks // 4
    step_spacing = col_count // DILATION_TILES
    me_col = lax.axis_index("col")

    stacked = jnp.stack([dequant(key_mant, key_exp), dequant(value_mant, value_exp)])[:, :, 0]

    above = shift(stacked[:, tile_blocks - 1 :], "row", row_count, 1)
    below = shift(stacked[:, :1], "row", row_count, -1)

    far_source = stacked[:, 0::4]
    dilated_entries = dilated_list[0, 0]
    hop_slot = dilated_entries // distant_rows
    far_row = dilated_entries % distant_rows
    if step_spacing == 1:
        far_sources, lookup, relative = ring_gather(far_source, col_count, me_col)
        hop_slot = relative((me_col + hop_slot + 1) % col_count)
    else:
        far_sources = []
        lookup = []
        for hop in range(1, DILATION_TILES):
            distance = hop * step_spacing
            route = [((i + distance) % col_count, i) for i in range(col_count)]
            far_sources.append(lax.ppermute(far_source, "col", route))
            lookup.append([(hop - 1, r) for r in range(distant_rows)])
    edge_cap = min(3 if row_count >= 2 else 4, tile_blocks)
    main_cap = edge_cap - 1 if col_count >= 3 else edge_cap
    entries = cycle_list[0, 0]
    right_entries = shift(entries, "col", col_count, -1)
    left_entries = shift(entries, "col", col_count, 1)
    to_right, _, _ = side_slots(right_entries, 2, tile_blocks, edge_cap)
    to_left, _, _ = side_slots(left_entries, 2 + tile_blocks, tile_blocks, edge_cap)
    right_payload = jnp.take(stacked, to_right, axis=1)
    left_payload = jnp.take(stacked, to_left, axis=1)
    cycle_sources = [above, below]
    last = col_count - 1
    for slot in range(edge_cap):
        to_r = right_payload[:, slot : slot + 1]
        to_l = left_payload[:, slot : slot + 1]
        later = far_sources[min(2 * slot, len(far_sources) - 1)]
        to_r, to_l, _ = lax.optimization_barrier((to_r, to_l, later))
        if slot < main_cap:
            cycle_sources.append(shift(to_r, "col", col_count, 1))
            cycle_sources.append(shift(to_l, "col", col_count, -1))
        else:
            cycle_sources.append(lax.ppermute(to_r, "col", [(last - 1, last)]))
            cycle_sources.append(lax.ppermute(to_l, "col", [(1, 0)]))

    _, is_left, left_rank = side_slots(entries, 2, tile_blocks, edge_cap)
    _, is_right, right_rank = side_slots(entries, 2 + tile_blocks, tile_blocks, edge_cap)
    side_rank = jnp.where(is_left, left_rank, right_rank)
    cycle_src = jnp.where(
        entries == 0, 0, jnp.where(entries == 1, 1, 2 + is_right.astype(jnp.int32) + 2 * side_rank)
    )
    cycle_idx = jnp.zeros_like(entries)

    lookup_src = jnp.array([[a for a, _ in row] for row in lookup], dtype=jnp.int32)
    lookup_idx = jnp.array([[b for _, b in row] for row in lookup], dtype=jnp.int32)
    far_src = len(cycle_sources) + lookup_src[hop_slot, far_row]
    far_idx = lookup_idx[hop_slot, far_row]

    table = jnp.stack(
        [jnp.concatenate([cycle_src, far_src]), jnp.concatenate([cycle_idx, far_idx])], axis=1
    ).reshape(-1)
    token_count = tile_blocks * block_length
    result = gather_attend(
        queries.reshape(token_count, width), stacked, cycle_sources, far_sources, table
    )
    return result.reshape(queries.shape)


def solution(mesh):
    in_specs = (
        P(("groups", "row"), "col", None, None),
        P(("groups", "row"), "col", None, None),
        P(("groups", "row"), "col", None, None),
        P(("groups", "row"), "col", None, None),
        P(("groups", "row"), "col", None, None),
        P(("groups", "row"), "col", None),
        P(("groups", "row"), "col", None),
    )
    out_specs = P(("groups", "row"), "col", None, None)
    return jax.shard_map(
        per_device, mesh=mesh, in_specs=in_specs, out_specs=out_specs, check_vma=False
    )
```

```python
import functools

import jax
import jax.numpy as jnp
from jax import lax
from jax.experimental import pallas as pl
from jax.experimental.pallas import tpu as pltpu
from jax.sharding import PartitionSpec as P

HEAD_DIM = 128
DILATION_TILES = 8


def dequant(mantissa, exponent):
    tile_rows, tile_cols, block_length, feature_channel_width = mantissa.shape
    groups = exponent.shape[2]
    factor = jnp.exp2(exponent.astype(jnp.float32))[:, :, :, None, :]
    scaled = (
        mantissa.reshape(
            tile_rows, tile_cols, groups, block_length // groups, feature_channel_width
        ).astype(jnp.float32)
        * factor
    )
    return scaled.reshape(mantissa.shape).astype(jnp.bfloat16)


def shift(x, axis, count, step):
    if step > 0:
        pairs = [(i, i + step) for i in range(count - step)]
    else:
        pairs = [(i - step, i) for i in range(count + step)]
    if not pairs:
        return jnp.zeros_like(x)
    return lax.ppermute(x, axis, pairs)


def side_slots(entries, low, tile_blocks, cap):
    inside = (entries >= low) & (entries < low + tile_blocks)
    rank = jnp.cumsum(inside.astype(jnp.int32)) - 1
    slot = jnp.arange(cap, dtype=jnp.int32)[:, None]
    hit = inside[None, :] & (rank[None, :] == slot)
    return jnp.sum(jnp.where(hit, entries[None, :] - low, 0), axis=1), inside, rank


def ring_gather(item, count, me):
    order = list(range(0, count, 2)) + list(range(count - 1 - count % 2, 0, -2))
    position = [0] * count
    for place, col in enumerate(order):
        position[col] = place
    forward = [(order[i], order[(i + 1) % count]) for i in range(count)]
    backward = [(order[(i + 1) % count], order[i]) for i in range(count)]
    half = count // 2
    rows = item.shape[1]
    split = (rows + 1) // 2
    arrays = []
    lookup = [[None] * rows for _ in range(count - 1)]
    for r in range(rows):
        ahead = behind = item[:, r : r + 1]
        for distance in range(1, half + 1):
            if distance == half and count % 2 == 0:
                if r < split:
                    arrays.append(lax.ppermute(ahead, "col", forward))
                else:
                    arrays.append(lax.ppermute(behind, "col", backward))
                lookup[distance - 1][r] = (len(arrays) - 1, 0)
                continue
            ahead = lax.ppermute(ahead, "col", forward)
            arrays.append(ahead)
            lookup[distance - 1][r] = (len(arrays) - 1, 0)
            behind = lax.ppermute(behind, "col", backward)
            arrays.append(behind)
            lookup[count - distance - 1][r] = (len(arrays) - 1, 0)
    table = jnp.array(position, dtype=jnp.int32)

    def relative(col):
        return (table[me] - table[col]) % count - 1

    return arrays, lookup, relative


def gather_attention_kernel(cycle_sources, far_sources, table_ref, q_hbm, own_hbm, *rest):
    sources = rest[: cycle_sources + far_sources]
    o_ref, q_vmem, k_vmem, v_vmem, sems = rest[cycle_sources + far_sources :]
    tile_blocks = own_hbm.shape[1]
    block_length = own_hbm.shape[2]
    extra = table_ref.shape[0] // 2
    heads = q_vmem.shape[1] // HEAD_DIM

    copies = [pltpu.make_async_copy(q_hbm, q_vmem, sems.at[0, 0])]
    copies.append(pltpu.make_async_copy(own_hbm.at[0], k_vmem.at[pl.ds(0, tile_blocks)], sems.at[0, 1]))
    copies.append(pltpu.make_async_copy(own_hbm.at[1], v_vmem.at[pl.ds(0, tile_blocks)], sems.at[1, 1]))
    for c in copies:
        c.start()
    for slot in range(extra):
        src = table_ref[2 * slot]
        index = table_ref[2 * slot + 1]
        lo, hi = (0, cycle_sources) if slot < extra // 2 else (cycle_sources, cycle_sources + far_sources)
        for cand in range(lo, hi):
            @pl.when(src == cand)
            def _():
                for kv, dst in ((0, k_vmem), (1, v_vmem)):
                    pltpu.make_async_copy(
                        sources[cand].at[kv, index], dst.at[tile_blocks + slot], sems.at[kv, 2 + slot]
                    ).start()
    for c in copies:
        c.wait()
    for slot in range(extra):
        for kv, dst in ((0, k_vmem), (1, v_vmem)):
            pltpu.make_async_copy(
                own_hbm.at[kv, 0], dst.at[tile_blocks + slot], sems.at[kv, 2 + slot]
            ).wait()

    key_count = k_vmem.shape[0] * block_length

    token_count = q_vmem.shape[0]
    part = token_count // 2 if token_count % 32 == 0 else token_count
    for h in range(heads):
      lanes = pl.ds(h * HEAD_DIM, HEAD_DIM)
      k = k_vmem[:, :, lanes].reshape(key_count, HEAD_DIM)
      v = v_vmem[:, :, lanes].reshape(key_count, HEAD_DIM)
      for first in range(0, token_count, part):
        rows = pl.ds(first, part)
        q = q_vmem[rows, lanes]
        scores = lax.dot_general(
            q, k, (((1,), (1,)), ((), ())), preferred_element_type=jnp.float32
        ) * HEAD_DIM ** (-0.5)
        row_max = jnp.max(scores, axis=1, keepdims=True)
        weights = jnp.exp(scores - row_max)
        row_total = jnp.sum(weights, axis=1, keepdims=True)
        rounded = weights.astype(jnp.bfloat16)
        blended = jnp.dot(rounded, v, preferred_element_type=jnp.float32)
        o_ref[rows, lanes] = (blended / row_total).astype(o_ref.dtype)


def gather_attend(query_rows, own, cycle_list_sources, far_list_sources, table):
    token_count, width = query_rows.shape
    tile_blocks, block_length = own.shape[1], own.shape[2]
    extra = table.shape[0] // 2
    blocks = tile_blocks + extra
    key_count = blocks * block_length
    heads = width // HEAD_DIM
    n_sources = len(cycle_list_sources) + len(far_list_sources)
    kernel = functools.partial(
        gather_attention_kernel, len(cycle_list_sources), len(far_list_sources)
    )
    return pl.pallas_call(
        kernel,
        out_shape=jax.ShapeDtypeStruct((token_count, width), jnp.bfloat16),
        in_specs=[pl.BlockSpec(memory_space=pltpu.SMEM)]
        + [pl.BlockSpec(memory_space=pl.ANY)] * (2 + n_sources),
        out_specs=pl.BlockSpec(memory_space=pltpu.VMEM),
        scratch_shapes=[
            pltpu.VMEM((token_count, width), jnp.bfloat16),
            pltpu.VMEM((blocks, block_length, width), jnp.bfloat16),
            pltpu.VMEM((blocks, block_length, width), jnp.bfloat16),
            pltpu.SemaphoreType.DMA((2, 2 + extra)),
        ],
        compiler_params=pltpu.CompilerParams(vmem_limit_bytes=48 * 1024 * 1024),
        cost_estimate=pl.CostEstimate(
            flops=4 * token_count * key_count * width,
            transcendentals=token_count * key_count * heads,
            bytes_accessed=2 * (2 * token_count * width + 2 * key_count * width),
        ),
    )(table, query_rows, own, *cycle_list_sources, *far_list_sources)


def per_device(queries, key_mant, key_exp, value_mant, value_exp, cycle_list, dilated_list):
    tile_blocks = queries.shape[0]
    block_length = queries.shape[2]
    width = queries.shape[3]
    col_count = lax.axis_size("col")
    row_count = lax.axis_size("row")
    distant_rows = tile_blocks // 4
    step_spacing = col_count // DILATION_TILES
    me_col = lax.axis_index("col")

    stacked = jnp.stack([dequant(key_mant, key_exp), dequant(value_mant, value_exp)])[:, :, 0]

    above = shift(stacked[:, tile_blocks - 1 :], "row", row_count, 1)
    below = shift(stacked[:, :1], "row", row_count, -1)

    far_source = stacked[:, 0::4]
    dilated_entries = dilated_list[0, 0]
    hop_slot = dilated_entries // distant_rows
    far_row = dilated_entries % distant_rows
    if step_spacing == 1:
        far_sources, lookup, relative = ring_gather(far_source, col_count, me_col)
        hop_slot = relative((me_col + hop_slot + 1) % col_count)
    else:
        far_sources = []
        lookup = []
        for hop in range(1, DILATION_TILES):
            distance = hop * step_spacing
            route = [((i + distance) % col_count, i) for i in range(col_count)]
            far_sources.append(lax.ppermute(far_source, "col", route))
            lookup.append([(hop - 1, r) for r in range(distant_rows)])
    edge_cap = min(3 if row_count >= 2 else 4, tile_blocks)
    main_cap = edge_cap - 1 if col_count >= 3 else edge_cap
    entries = cycle_list[0, 0]
    right_entries = shift(entries, "col", col_count, -1)
    left_entries = shift(entries, "col", col_count, 1)
    to_right, _, _ = side_slots(right_entries, 2, tile_blocks, edge_cap)
    to_left, _, _ = side_slots(left_entries, 2 + tile_blocks, tile_blocks, edge_cap)
    right_payload = jnp.take(stacked, to_right, axis=1)
    left_payload = jnp.take(stacked, to_left, axis=1)
    cycle_sources = [above, below]
    last = col_count - 1
    for slot in range(edge_cap):
        to_r = right_payload[:, slot : slot + 1]
        to_l = left_payload[:, slot : slot + 1]
        later = far_sources[min(2 * slot, len(far_sources) - 1)]
        to_r, to_l, _ = lax.optimization_barrier((to_r, to_l, later))
        if slot < main_cap:
            cycle_sources.append(shift(to_r, "col", col_count, 1))
            cycle_sources.append(shift(to_l, "col", col_count, -1))
        else:
            cycle_sources.append(lax.ppermute(to_r, "col", [(last - 1, last)]))
            cycle_sources.append(lax.ppermute(to_l, "col", [(1, 0)]))

    _, is_left, left_rank = side_slots(entries, 2, tile_blocks, edge_cap)
    _, is_right, right_rank = side_slots(entries, 2 + tile_blocks, tile_blocks, edge_cap)
    side_rank = jnp.where(is_left, left_rank, right_rank)
    cycle_src = jnp.where(
        entries == 0, 0, jnp.where(entries == 1, 1, 2 + is_right.astype(jnp.int32) + 2 * side_rank)
    )
    cycle_idx = jnp.zeros_like(entries)

    lookup_src = jnp.array([[a for a, _ in row] for row in lookup], dtype=jnp.int32)
    lookup_idx = jnp.array([[b for _, b in row] for row in lookup], dtype=jnp.int32)
    far_src = len(cycle_sources) + lookup_src[hop_slot, far_row]
    far_idx = lookup_idx[hop_slot, far_row]

    table = jnp.stack(
        [jnp.concatenate([cycle_src, far_src]), jnp.concatenate([cycle_idx, far_idx])], axis=1
    ).reshape(-1)
    token_count = tile_blocks * block_length
    result = gather_attend(
        queries.reshape(token_count, width), stacked, cycle_sources, far_sources, table
    )
    return result.reshape(queries.shape)


def solution(mesh):
    in_specs = (
        P(("groups", "row"), "col", None, None),
        P(("groups", "row"), "col", None, None),
        P(("groups", "row"), "col", None, None),
        P(("groups", "row"), "col", None, None),
        P(("groups", "row"), "col", None, None),
        P(("groups", "row"), "col", None),
        P(("groups", "row"), "col", None),
    )
    out_specs = P(("groups", "row"), "col", None, None)
    return jax.shard_map(
        per_device, mesh=mesh, in_specs=in_specs, out_specs=out_specs, check_vma=False
    )
```

```python
import functools

import jax
import jax.numpy as jnp
from jax import lax
from jax.experimental import pallas as pl
from jax.experimental.pallas import tpu as pltpu
from jax.sharding import PartitionSpec as P

HEAD_DIM = 128
DILATION_TILES = 8


def dequant(mantissa, exponent):
    tile_rows, tile_cols, block_length, feature_channel_width = mantissa.shape
    groups = exponent.shape[2]
    factor = jnp.exp2(exponent.astype(jnp.float32))[:, :, :, None, :]
    scaled = (
        mantissa.reshape(
            tile_rows, tile_cols, groups, block_length // groups, feature_channel_width
        ).astype(jnp.float32)
        * factor
    )
    return scaled.reshape(mantissa.shape).astype(jnp.bfloat16)


def shift(x, axis, count, step):
    if step > 0:
        pairs = [(i, i + step) for i in range(count - step)]
    else:
        pairs = [(i - step, i) for i in range(count + step)]
    if not pairs:
        return jnp.zeros_like(x)
    return lax.ppermute(x, axis, pairs)


def side_slots(entries, low, tile_blocks, cap):
    inside = (entries >= low) & (entries < low + tile_blocks)
    rank = jnp.cumsum(inside.astype(jnp.int32)) - 1
    slot = jnp.arange(cap, dtype=jnp.int32)[:, None]
    hit = inside[None, :] & (rank[None, :] == slot)
    return jnp.sum(jnp.where(hit, entries[None, :] - low, 0), axis=1), inside, rank


def ring_gather(item, count, me):
    order = list(range(0, count, 2)) + list(range(count - 1 - count % 2, 0, -2))
    position = [0] * count
    for place, col in enumerate(order):
        position[col] = place
    forward = [(order[i], order[(i + 1) % count]) for i in range(count)]
    backward = [(order[(i + 1) % count], order[i]) for i in range(count)]
    half = count // 2
    rows = item.shape[1]
    split = (rows + 1) // 2
    arrays = []
    lookup = [[None] * rows for _ in range(count - 1)]
    for r in range(rows):
        ahead = behind = item[:, r : r + 1]
        for distance in range(1, half + 1):
            if distance == half and count % 2 == 0:
                if r < split:
                    arrays.append(lax.ppermute(ahead, "col", forward))
                else:
                    arrays.append(lax.ppermute(behind, "col", backward))
                lookup[distance - 1][r] = (len(arrays) - 1, 0)
                continue
            ahead = lax.ppermute(ahead, "col", forward)
            arrays.append(ahead)
            lookup[distance - 1][r] = (len(arrays) - 1, 0)
            behind = lax.ppermute(behind, "col", backward)
            arrays.append(behind)
            lookup[count - distance - 1][r] = (len(arrays) - 1, 0)
    table = jnp.array(position, dtype=jnp.int32)

    def relative(col):
        return (table[me] - table[col]) % count - 1

    return arrays, lookup, relative


def gather_attention_kernel(cycle_sources, far_sources, table_ref, q_hbm, own_hbm, *rest):
    sources = rest[: cycle_sources + far_sources]
    o_hbm, o_vmem, q_vmem, k_vmem, v_vmem, sems, out_sems = rest[cycle_sources + far_sources :]
    tile_blocks = own_hbm.shape[1]
    block_length = own_hbm.shape[2]
    extra = table_ref.shape[0] // 2
    heads = q_vmem.shape[1] // HEAD_DIM

    copies = [pltpu.make_async_copy(q_hbm, q_vmem, sems.at[0, 0])]
    copies.append(pltpu.make_async_copy(own_hbm.at[0], k_vmem.at[pl.ds(0, tile_blocks)], sems.at[0, 1]))
    copies.append(pltpu.make_async_copy(own_hbm.at[1], v_vmem.at[pl.ds(0, tile_blocks)], sems.at[1, 1]))
    for c in copies:
        c.start()
    for slot in range(extra):
        src = table_ref[2 * slot]
        index = table_ref[2 * slot + 1]
        lo, hi = (0, cycle_sources) if slot < extra // 2 else (cycle_sources, cycle_sources + far_sources)
        for cand in range(lo, hi):
            @pl.when(src == cand)
            def _():
                for kv, dst in ((0, k_vmem), (1, v_vmem)):
                    pltpu.make_async_copy(
                        sources[cand].at[kv, index], dst.at[tile_blocks + slot], sems.at[kv, 2 + slot]
                    ).start()
    for c in copies:
        c.wait()
    for slot in range(extra):
        for kv, dst in ((0, k_vmem), (1, v_vmem)):
            pltpu.make_async_copy(
                own_hbm.at[kv, 0], dst.at[tile_blocks + slot], sems.at[kv, 2 + slot]
            ).wait()

    key_count = k_vmem.shape[0] * block_length

    groups = out_sems.shape[0]
    group_heads = heads // groups
    writes = []
    for h in range(heads):
        lanes = pl.ds(h * HEAD_DIM, HEAD_DIM)
        q = q_vmem[:, lanes]
        k = k_vmem[:, :, lanes].reshape(key_count, HEAD_DIM)
        v = v_vmem[:, :, lanes].reshape(key_count, HEAD_DIM)
        scores = lax.dot_general(
            q, k, (((1,), (1,)), ((), ())), preferred_element_type=jnp.float32
        ) * HEAD_DIM ** (-0.5)
        row_max = jnp.max(scores, axis=1, keepdims=True)
        weights = jnp.exp(scores - row_max)
        row_total = jnp.sum(weights, axis=1, keepdims=True)
        rounded = weights.astype(jnp.bfloat16)
        blended = jnp.dot(rounded, v, preferred_element_type=jnp.float32)
        o_vmem[:, lanes] = (blended / row_total).astype(o_vmem.dtype)
        if (h + 1) % group_heads == 0:
            group = h // group_heads
            span = pl.ds(group * group_heads * HEAD_DIM, group_heads * HEAD_DIM)
            writes.append(
                pltpu.make_async_copy(o_vmem.at[:, span], o_hbm.at[:, span], out_sems.at[group])
            )
            writes[-1].start()
    for w in writes:
        w.wait()


def gather_attend(query_rows, own, cycle_list_sources, far_list_sources, table):
    token_count, width = query_rows.shape
    tile_blocks, block_length = own.shape[1], own.shape[2]
    extra = table.shape[0] // 2
    blocks = tile_blocks + extra
    key_count = blocks * block_length
    heads = width // HEAD_DIM
    n_sources = len(cycle_list_sources) + len(far_list_sources)
    kernel = functools.partial(
        gather_attention_kernel, len(cycle_list_sources), len(far_list_sources)
    )
    return pl.pallas_call(
        kernel,
        out_shape=jax.ShapeDtypeStruct((token_count, width), jnp.bfloat16),
        in_specs=[pl.BlockSpec(memory_space=pltpu.SMEM)]
        + [pl.BlockSpec(memory_space=pl.ANY)] * (2 + n_sources),
        out_specs=pl.BlockSpec(memory_space=pl.ANY),
        scratch_shapes=[
            pltpu.VMEM((token_count, width), jnp.bfloat16),
            pltpu.VMEM((token_count, width), jnp.bfloat16),
            pltpu.VMEM((blocks, block_length, width), jnp.bfloat16),
            pltpu.VMEM((blocks, block_length, width), jnp.bfloat16),
            pltpu.SemaphoreType.DMA((2, 2 + extra)),
            pltpu.SemaphoreType.DMA((3 if heads % 3 == 0 else 1,)),
        ],
        compiler_params=pltpu.CompilerParams(vmem_limit_bytes=48 * 1024 * 1024),
        cost_estimate=pl.CostEstimate(
            flops=4 * token_count * key_count * width,
            transcendentals=token_count * key_count * heads,
            bytes_accessed=2 * (2 * token_count * width + 2 * key_count * width),
        ),
    )(table, query_rows, own, *cycle_list_sources, *far_list_sources)


def per_device(queries, key_mant, key_exp, value_mant, value_exp, cycle_list, dilated_list):
    tile_blocks = queries.shape[0]
    block_length = queries.shape[2]
    width = queries.shape[3]
    col_count = lax.axis_size("col")
    row_count = lax.axis_size("row")
    distant_rows = tile_blocks // 4
    step_spacing = col_count // DILATION_TILES
    me_col = lax.axis_index("col")

    stacked = jnp.stack([dequant(key_mant, key_exp), dequant(value_mant, value_exp)])[:, :, 0]

    above = shift(stacked[:, tile_blocks - 1 :], "row", row_count, 1)
    below = shift(stacked[:, :1], "row", row_count, -1)

    far_source = stacked[:, 0::4]
    dilated_entries = dilated_list[0, 0]
    hop_slot = dilated_entries // distant_rows
    far_row = dilated_entries % distant_rows
    if step_spacing == 1:
        far_sources, lookup, relative = ring_gather(far_source, col_count, me_col)
        hop_slot = relative((me_col + hop_slot + 1) % col_count)
    else:
        far_sources = []
        lookup = []
        for hop in range(1, DILATION_TILES):
            distance = hop * step_spacing
            route = [((i + distance) % col_count, i) for i in range(col_count)]
            far_sources.append(lax.ppermute(far_source, "col", route))
            lookup.append([(hop - 1, r) for r in range(distant_rows)])
    edge_cap = min(3 if row_count >= 2 else 4, tile_blocks)
    main_cap = edge_cap - 1 if col_count >= 3 else edge_cap
    entries = cycle_list[0, 0]
    right_entries = shift(entries, "col", col_count, -1)
    left_entries = shift(entries, "col", col_count, 1)
    to_right, _, _ = side_slots(right_entries, 2, tile_blocks, edge_cap)
    to_left, _, _ = side_slots(left_entries, 2 + tile_blocks, tile_blocks, edge_cap)
    right_payload = jnp.take(stacked, to_right, axis=1)
    left_payload = jnp.take(stacked, to_left, axis=1)
    cycle_sources = [above, below]
    last = col_count - 1
    for slot in range(edge_cap):
        to_r = right_payload[:, slot : slot + 1]
        to_l = left_payload[:, slot : slot + 1]
        later = far_sources[min(2 * slot, len(far_sources) - 1)]
        to_r, to_l, _ = lax.optimization_barrier((to_r, to_l, later))
        if slot < main_cap:
            cycle_sources.append(shift(to_r, "col", col_count, 1))
            cycle_sources.append(shift(to_l, "col", col_count, -1))
        else:
            cycle_sources.append(lax.ppermute(to_r, "col", [(last - 1, last)]))
            cycle_sources.append(lax.ppermute(to_l, "col", [(1, 0)]))

    _, is_left, left_rank = side_slots(entries, 2, tile_blocks, edge_cap)
    _, is_right, right_rank = side_slots(entries, 2 + tile_blocks, tile_blocks, edge_cap)
    side_rank = jnp.where(is_left, left_rank, right_rank)
    cycle_src = jnp.where(
        entries == 0, 0, jnp.where(entries == 1, 1, 2 + is_right.astype(jnp.int32) + 2 * side_rank)
    )
    cycle_idx = jnp.zeros_like(entries)

    lookup_src = jnp.array([[a for a, _ in row] for row in lookup], dtype=jnp.int32)
    lookup_idx = jnp.array([[b for _, b in row] for row in lookup], dtype=jnp.int32)
    far_src = len(cycle_sources) + lookup_src[hop_slot, far_row]
    far_idx = lookup_idx[hop_slot, far_row]

    table = jnp.stack(
        [jnp.concatenate([cycle_src, far_src]), jnp.concatenate([cycle_idx, far_idx])], axis=1
    ).reshape(-1)
    token_count = tile_blocks * block_length
    result = gather_attend(
        queries.reshape(token_count, width), stacked, cycle_sources, far_sources, table
    )
    return result.reshape(queries.shape)


def solution(mesh):
    in_specs = (
        P(("groups", "row"), "col", None, None),
        P(("groups", "row"), "col", None, None),
        P(("groups", "row"), "col", None, None),
        P(("groups", "row"), "col", None, None),
        P(("groups", "row"), "col", None, None),
        P(("groups", "row"), "col", None),
        P(("groups", "row"), "col", None),
    )
    out_specs = P(("groups", "row"), "col", None, None)
    return jax.shard_map(
        per_device, mesh=mesh, in_specs=in_specs, out_specs=out_specs, check_vma=False
    )
```

```python
import functools

import jax
import jax.numpy as jnp
from jax import lax
from jax.experimental import pallas as pl
from jax.experimental.pallas import tpu as pltpu
from jax.sharding import PartitionSpec as P

HEAD_DIM = 128
DILATION_TILES = 8


def dequant(mantissa, exponent):
    tile_rows, tile_cols, block_length, feature_channel_width = mantissa.shape
    groups = exponent.shape[2]
    factor = jnp.exp2(exponent.astype(jnp.float32))[:, :, :, None, :]
    scaled = (
        mantissa.reshape(
            tile_rows, tile_cols, groups, block_length // groups, feature_channel_width
        ).astype(jnp.float32)
        * factor
    )
    return scaled.reshape(mantissa.shape).astype(jnp.bfloat16)


def shift(x, axis, count, step):
    if step > 0:
        pairs = [(i, i + step) for i in range(count - step)]
    else:
        pairs = [(i - step, i) for i in range(count + step)]
    if not pairs:
        return jnp.zeros_like(x)
    return lax.ppermute(x, axis, pairs)


def side_slots(entries, low, tile_blocks, cap):
    inside = (entries >= low) & (entries < low + tile_blocks)
    rank = jnp.cumsum(inside.astype(jnp.int32)) - 1
    slot = jnp.arange(cap, dtype=jnp.int32)[:, None]
    hit = inside[None, :] & (rank[None, :] == slot)
    return jnp.sum(jnp.where(hit, entries[None, :] - low, 0), axis=1), inside, rank


def ring_gather(item, count, me):
    order = list(range(0, count, 2)) + list(range(count - 1 - count % 2, 0, -2))
    position = [0] * count
    for place, col in enumerate(order):
        position[col] = place
    forward = [(order[i], order[(i + 1) % count]) for i in range(count)]
    backward = [(order[(i + 1) % count], order[i]) for i in range(count)]
    half = count // 2
    rows = item.shape[1]
    split = (rows + 1) // 2
    arrays = []
    lookup = [[None] * rows for _ in range(count - 1)]
    for r in range(rows):
        ahead = behind = item[:, r : r + 1]
        for distance in range(1, half + 1):
            if distance == half and count % 2 == 0:
                if r < split:
                    arrays.append(lax.ppermute(ahead, "col", forward))
                else:
                    arrays.append(lax.ppermute(behind, "col", backward))
                lookup[distance - 1][r] = (len(arrays) - 1, 0)
                continue
            ahead = lax.ppermute(ahead, "col", forward)
            arrays.append(ahead)
            lookup[distance - 1][r] = (len(arrays) - 1, 0)
            behind = lax.ppermute(behind, "col", backward)
            arrays.append(behind)
            lookup[count - distance - 1][r] = (len(arrays) - 1, 0)
    table = jnp.array(position, dtype=jnp.int32)

    def relative(col):
        return (table[me] - table[col]) % count - 1

    return arrays, lookup, relative


def gather_attention_kernel(cycle_sources, far_sources, table_ref, q_hbm, own_hbm, *rest):
    sources = rest[: cycle_sources + far_sources]
    o_hbm, o_vmem, q_vmem, k_vmem, v_vmem, sems, out_sems = rest[cycle_sources + far_sources :]
    tile_blocks = own_hbm.shape[1]
    block_length = own_hbm.shape[2]
    extra = table_ref.shape[0] // 2
    heads = q_vmem.shape[1] // HEAD_DIM

    copies = [pltpu.make_async_copy(q_hbm, q_vmem, sems.at[0, 0])]
    copies.append(pltpu.make_async_copy(own_hbm.at[0], k_vmem.at[pl.ds(0, tile_blocks)], sems.at[0, 1]))
    copies.append(pltpu.make_async_copy(own_hbm.at[1], v_vmem.at[pl.ds(0, tile_blocks)], sems.at[1, 1]))
    for c in copies:
        c.start()
    for slot in range(extra):
        src = table_ref[2 * slot]
        index = table_ref[2 * slot + 1]
        lo, hi = (0, cycle_sources) if slot < extra // 2 else (cycle_sources, cycle_sources + far_sources)
        for cand in range(lo, hi):
            @pl.when(src == cand)
            def _():
                for kv, dst in ((0, k_vmem), (1, v_vmem)):
                    pltpu.make_async_copy(
                        sources[cand].at[kv, index], dst.at[tile_blocks + slot], sems.at[kv, 2 + slot]
                    ).start()
    for c in copies:
        c.wait()
    for slot in range(extra):
        for kv, dst in ((0, k_vmem), (1, v_vmem)):
            pltpu.make_async_copy(
                own_hbm.at[kv, 0], dst.at[tile_blocks + slot], sems.at[kv, 2 + slot]
            ).wait()

    key_count = k_vmem.shape[0] * block_length

    groups = out_sems.shape[0]
    group_heads = heads // groups
    writes = []
    for h in range(heads):
        lanes = pl.ds(h * HEAD_DIM, HEAD_DIM)
        q = q_vmem[:, lanes]
        k = k_vmem[:, :, lanes].reshape(key_count, HEAD_DIM)
        v = v_vmem[:, :, lanes].reshape(key_count, HEAD_DIM)
        scores = lax.dot_general(
            q, k, (((1,), (1,)), ((), ())), preferred_element_type=jnp.float32
        ) * HEAD_DIM ** (-0.5)
        row_max = jnp.max(scores, axis=1, keepdims=True)
        weights = jnp.exp(scores - row_max)
        row_total = jnp.sum(weights, axis=1, keepdims=True)
        rounded = weights.astype(jnp.bfloat16)
        blended = jnp.dot(rounded, v, preferred_element_type=jnp.float32)
        o_vmem[:, lanes] = (blended / row_total).astype(o_vmem.dtype)
        if (h + 1) % group_heads == 0:
            group = h // group_heads
            span = pl.ds(group * group_heads * HEAD_DIM, group_heads * HEAD_DIM)
            writes.append(
                pltpu.make_async_copy(o_vmem.at[:, span], o_hbm.at[:, span], out_sems.at[group])
            )
            writes[-1].start()
    for w in writes:
        w.wait()


def gather_attend(query_rows, own, cycle_list_sources, far_list_sources, table):
    token_count, width = query_rows.shape
    tile_blocks, block_length = own.shape[1], own.shape[2]
    extra = table.shape[0] // 2
    blocks = tile_blocks + extra
    key_count = blocks * block_length
    heads = width // HEAD_DIM
    n_sources = len(cycle_list_sources) + len(far_list_sources)
    kernel = functools.partial(
        gather_attention_kernel, len(cycle_list_sources), len(far_list_sources)
    )
    return pl.pallas_call(
        kernel,
        out_shape=jax.ShapeDtypeStruct((token_count, width), jnp.bfloat16),
        in_specs=[pl.BlockSpec(memory_space=pltpu.SMEM)]
        + [pl.BlockSpec(memory_space=pl.ANY)] * (2 + n_sources),
        out_specs=pl.BlockSpec(memory_space=pl.ANY),
        scratch_shapes=[
            pltpu.VMEM((token_count, width), jnp.bfloat16),
            pltpu.VMEM((token_count, width), jnp.bfloat16),
            pltpu.VMEM((blocks, block_length, width), jnp.bfloat16),
            pltpu.VMEM((blocks, block_length, width), jnp.bfloat16),
            pltpu.SemaphoreType.DMA((2, 2 + extra)),
            pltpu.SemaphoreType.DMA((3 if heads % 3 == 0 else 1,)),
        ],
        compiler_params=pltpu.CompilerParams(vmem_limit_bytes=48 * 1024 * 1024),
        cost_estimate=pl.CostEstimate(
            flops=4 * token_count * key_count * width,
            transcendentals=token_count * key_count * heads,
            bytes_accessed=2 * (2 * token_count * width + 2 * key_count * width),
        ),
    )(table, query_rows, own, *cycle_list_sources, *far_list_sources)


def per_device(queries, key_mant, key_exp, value_mant, value_exp, cycle_list, dilated_list):
    tile_blocks = queries.shape[0]
    block_length = queries.shape[2]
    width = queries.shape[3]
    col_count = lax.axis_size("col")
    row_count = lax.axis_size("row")
    distant_rows = tile_blocks // 4
    step_spacing = col_count // DILATION_TILES
    me_col = lax.axis_index("col")

    stacked = jnp.stack([dequant(key_mant, key_exp), dequant(value_mant, value_exp)])[:, :, 0]

    if row_count == 2:
        row_edge = jnp.where(lax.axis_index("row") == 0, tile_blocks - 1, 0)
        edge = lax.dynamic_slice_in_dim(stacked, row_edge, 1, axis=1)
        above = below = lax.ppermute(edge, "row", [(0, 1), (1, 0)])
    else:
        above = shift(stacked[:, tile_blocks - 1 :], "row", row_count, 1)
        below = shift(stacked[:, :1], "row", row_count, -1)

    far_source = stacked[:, 0::4]
    dilated_entries = dilated_list[0, 0]
    hop_slot = dilated_entries // distant_rows
    far_row = dilated_entries % distant_rows
    if step_spacing == 1:
        far_sources, lookup, relative = ring_gather(far_source, col_count, me_col)
        hop_slot = relative((me_col + hop_slot + 1) % col_count)
    else:
        far_sources = []
        lookup = []
        for hop in range(1, DILATION_TILES):
            distance = hop * step_spacing
            route = [((i + distance) % col_count, i) for i in range(col_count)]
            far_sources.append(lax.ppermute(far_source, "col", route))
            lookup.append([(hop - 1, r) for r in range(distant_rows)])
    edge_cap = min(3 if row_count >= 2 else 4, tile_blocks)
    main_cap = edge_cap - 1 if col_count >= 3 else edge_cap
    entries = cycle_list[0, 0]
    right_entries = shift(entries, "col", col_count, -1)
    left_entries = shift(entries, "col", col_count, 1)
    to_right, _, _ = side_slots(right_entries, 2, tile_blocks, edge_cap)
    to_left, _, _ = side_slots(left_entries, 2 + tile_blocks, tile_blocks, edge_cap)
    right_payload = jnp.take(stacked, to_right, axis=1)
    left_payload = jnp.take(stacked, to_left, axis=1)
    cycle_sources = [above, below]
    last = col_count - 1
    for slot in range(edge_cap):
        to_r = right_payload[:, slot : slot + 1]
        to_l = left_payload[:, slot : slot + 1]
        later = far_sources[min(2 * slot, len(far_sources) - 1)]
        to_r, to_l, _ = lax.optimization_barrier((to_r, to_l, later))
        if slot < main_cap:
            cycle_sources.append(shift(to_r, "col", col_count, 1))
            cycle_sources.append(shift(to_l, "col", col_count, -1))
        else:
            cycle_sources.append(lax.ppermute(to_r, "col", [(last - 1, last)]))
            cycle_sources.append(lax.ppermute(to_l, "col", [(1, 0)]))

    _, is_left, left_rank = side_slots(entries, 2, tile_blocks, edge_cap)
    _, is_right, right_rank = side_slots(entries, 2 + tile_blocks, tile_blocks, edge_cap)
    side_rank = jnp.where(is_left, left_rank, right_rank)
    cycle_src = jnp.where(
        entries == 0, 0, jnp.where(entries == 1, 1, 2 + is_right.astype(jnp.int32) + 2 * side_rank)
    )
    cycle_idx = jnp.zeros_like(entries)

    lookup_src = jnp.array([[a for a, _ in row] for row in lookup], dtype=jnp.int32)
    lookup_idx = jnp.array([[b for _, b in row] for row in lookup], dtype=jnp.int32)
    far_src = len(cycle_sources) + lookup_src[hop_slot, far_row]
    far_idx = lookup_idx[hop_slot, far_row]

    table = jnp.stack(
        [jnp.concatenate([cycle_src, far_src]), jnp.concatenate([cycle_idx, far_idx])], axis=1
    ).reshape(-1)
    token_count = tile_blocks * block_length
    result = gather_attend(
        queries.reshape(token_count, width), stacked, cycle_sources, far_sources, table
    )
    return result.reshape(queries.shape)


def solution(mesh):
    in_specs = (
        P(("groups", "row"), "col", None, None),
        P(("groups", "row"), "col", None, None),
        P(("groups", "row"), "col", None, None),
        P(("groups", "row"), "col", None, None),
        P(("groups", "row"), "col", None, None),
        P(("groups", "row"), "col", None),
        P(("groups", "row"), "col", None),
    )
    out_specs = P(("groups", "row"), "col", None, None)
    return jax.shard_map(
        per_device, mesh=mesh, in_specs=in_specs, out_specs=out_specs, check_vma=False
    )
```

```python
import functools

import jax
import jax.numpy as jnp
from jax import lax
from jax.experimental import pallas as pl
from jax.experimental.pallas import tpu as pltpu
from jax.sharding import PartitionSpec as P

HEAD_DIM = 128
DILATION_TILES = 8


def dequant(mantissa, exponent):
    tile_rows, tile_cols, block_length, feature_channel_width = mantissa.shape
    groups = exponent.shape[2]
    factor = jnp.exp2(exponent.astype(jnp.float32))[:, :, :, None, :]
    scaled = (
        mantissa.reshape(
            tile_rows, tile_cols, groups, block_length // groups, feature_channel_width
        ).astype(jnp.float32)
        * factor
    )
    return scaled.reshape(mantissa.shape).astype(jnp.bfloat16)


def shift(x, axis, count, step):
    if step > 0:
        pairs = [(i, i + step) for i in range(count - step)]
    else:
        pairs = [(i - step, i) for i in range(count + step)]
    if not pairs:
        return jnp.zeros_like(x)
    return lax.ppermute(x, axis, pairs)


def side_slots(entries, low, tile_blocks, cap):
    inside = (entries >= low) & (entries < low + tile_blocks)
    rank = jnp.cumsum(inside.astype(jnp.int32)) - 1
    slot = jnp.arange(cap, dtype=jnp.int32)[:, None]
    hit = inside[None, :] & (rank[None, :] == slot)
    return jnp.sum(jnp.where(hit, entries[None, :] - low, 0), axis=1), inside, rank


def ring_gather(item, count, me):
    order = list(range(0, count, 2)) + list(range(count - 1 - count % 2, 0, -2))
    position = [0] * count
    for place, col in enumerate(order):
        position[col] = place
    forward = [(order[i], order[(i + 1) % count]) for i in range(count)]
    backward = [(order[(i + 1) % count], order[i]) for i in range(count)]
    half = count // 2
    rows = item.shape[1]
    split = (rows + 1) // 2
    arrays = []
    lookup = [[None] * rows for _ in range(count - 1)]
    for r in range(rows):
        ahead = behind = item[:, r : r + 1]
        for distance in range(1, half + 1):
            if distance == half and count % 2 == 0:
                if r < split:
                    arrays.append(lax.ppermute(ahead, "col", forward))
                else:
                    arrays.append(lax.ppermute(behind, "col", backward))
                lookup[distance - 1][r] = (len(arrays) - 1, 0)
                continue
            ahead = lax.ppermute(ahead, "col", forward)
            arrays.append(ahead)
            lookup[distance - 1][r] = (len(arrays) - 1, 0)
            behind = lax.ppermute(behind, "col", backward)
            arrays.append(behind)
            lookup[count - distance - 1][r] = (len(arrays) - 1, 0)
    table = jnp.array(position, dtype=jnp.int32)

    def relative(col):
        return (table[me] - table[col]) % count - 1

    return arrays, lookup, relative


def gather_attention_kernel(cycle_sources, far_sources, table_ref, q_hbm, own_hbm, *rest):
    sources = rest[: cycle_sources + far_sources]
    o_hbm, o_vmem, q_vmem, k_vmem, v_vmem, sems, out_sems = rest[cycle_sources + far_sources :]
    tile_blocks = own_hbm.shape[1]
    block_length = own_hbm.shape[2]
    extra = table_ref.shape[0] // 2
    heads = q_vmem.shape[1] // HEAD_DIM

    copies = [pltpu.make_async_copy(q_hbm, q_vmem, sems.at[0, 0])]
    copies.append(pltpu.make_async_copy(own_hbm.at[0], k_vmem.at[pl.ds(0, tile_blocks)], sems.at[0, 1]))
    copies.append(pltpu.make_async_copy(own_hbm.at[1], v_vmem.at[pl.ds(0, tile_blocks)], sems.at[1, 1]))
    for c in copies:
        c.start()
    for slot in range(extra):
        src = table_ref[2 * slot]
        index = table_ref[2 * slot + 1]
        lo, hi = (0, cycle_sources) if slot < extra // 2 else (cycle_sources, cycle_sources + far_sources)
        for cand in range(lo, hi):
            @pl.when(src == cand)
            def _():
                for kv, dst in ((0, k_vmem), (1, v_vmem)):
                    pltpu.make_async_copy(
                        sources[cand].at[kv, index], dst.at[tile_blocks + slot], sems.at[kv, 2 + slot]
                    ).start()
    for c in copies:
        c.wait()
    for slot in range(extra):
        for kv, dst in ((0, k_vmem), (1, v_vmem)):
            pltpu.make_async_copy(
                own_hbm.at[kv, 0], dst.at[tile_blocks + slot], sems.at[kv, 2 + slot]
            ).wait()

    key_count = k_vmem.shape[0] * block_length

    groups = out_sems.shape[0]
    group_heads = heads // groups
    writes = []
    for h in range(heads):
        lanes = pl.ds(h * HEAD_DIM, HEAD_DIM)
        q = q_vmem[:, lanes]
        k = k_vmem[:, :, lanes].reshape(key_count, HEAD_DIM)
        v = v_vmem[:, :, lanes].reshape(key_count, HEAD_DIM)
        scores = lax.dot_general(
            q, k, (((1,), (1,)), ((), ())), preferred_element_type=jnp.float32
        ) * HEAD_DIM ** (-0.5)
        row_max = jnp.max(scores, axis=1, keepdims=True)
        weights = jnp.exp(scores - row_max)
        row_total = jnp.sum(weights, axis=1, keepdims=True)
        rounded = weights.astype(jnp.bfloat16)
        blended = jnp.dot(rounded, v, preferred_element_type=jnp.float32)
        o_vmem[:, lanes] = (blended / row_total).astype(o_vmem.dtype)
        if (h + 1) % group_heads == 0:
            group = h // group_heads
            span = pl.ds(group * group_heads * HEAD_DIM, group_heads * HEAD_DIM)
            writes.append(
                pltpu.make_async_copy(o_vmem.at[:, span], o_hbm.at[:, span], out_sems.at[group])
            )
            writes[-1].start()
    for w in writes:
        w.wait()


def gather_attend(query_rows, own, cycle_list_sources, far_list_sources, table):
    token_count, width = query_rows.shape
    tile_blocks, block_length = own.shape[1], own.shape[2]
    extra = table.shape[0] // 2
    blocks = tile_blocks + extra
    key_count = blocks * block_length
    heads = width // HEAD_DIM
    n_sources = len(cycle_list_sources) + len(far_list_sources)
    kernel = functools.partial(
        gather_attention_kernel, len(cycle_list_sources), len(far_list_sources)
    )
    return pl.pallas_call(
        kernel,
        out_shape=jax.ShapeDtypeStruct((token_count, width), jnp.bfloat16),
        in_specs=[pl.BlockSpec(memory_space=pltpu.SMEM)]
        + [pl.BlockSpec(memory_space=pl.ANY)] * (2 + n_sources),
        out_specs=pl.BlockSpec(memory_space=pl.ANY),
        scratch_shapes=[
            pltpu.VMEM((token_count, width), jnp.bfloat16),
            pltpu.VMEM((token_count, width), jnp.bfloat16),
            pltpu.VMEM((blocks, block_length, width), jnp.bfloat16),
            pltpu.VMEM((blocks, block_length, width), jnp.bfloat16),
            pltpu.SemaphoreType.DMA((2, 2 + extra)),
            pltpu.SemaphoreType.DMA((6 if heads % 6 == 0 else 1,)),
        ],
        compiler_params=pltpu.CompilerParams(vmem_limit_bytes=48 * 1024 * 1024),
        cost_estimate=pl.CostEstimate(
            flops=4 * token_count * key_count * width,
            transcendentals=token_count * key_count * heads,
            bytes_accessed=2 * (2 * token_count * width + 2 * key_count * width),
        ),
    )(table, query_rows, own, *cycle_list_sources, *far_list_sources)


def per_device(queries, key_mant, key_exp, value_mant, value_exp, cycle_list, dilated_list):
    tile_blocks = queries.shape[0]
    block_length = queries.shape[2]
    width = queries.shape[3]
    col_count = lax.axis_size("col")
    row_count = lax.axis_size("row")
    distant_rows = tile_blocks // 4
    step_spacing = col_count // DILATION_TILES
    me_col = lax.axis_index("col")

    stacked = jnp.stack([dequant(key_mant, key_exp), dequant(value_mant, value_exp)])[:, :, 0]

    above = shift(stacked[:, tile_blocks - 1 :], "row", row_count, 1)
    below = shift(stacked[:, :1], "row", row_count, -1)

    far_source = stacked[:, 0::4]
    dilated_entries = dilated_list[0, 0]
    hop_slot = dilated_entries // distant_rows
    far_row = dilated_entries % distant_rows
    if step_spacing == 1:
        far_sources, lookup, relative = ring_gather(far_source, col_count, me_col)
        hop_slot = relative((me_col + hop_slot + 1) % col_count)
    else:
        far_sources = []
        lookup = []
        for hop in range(1, DILATION_TILES):
            distance = hop * step_spacing
            route = [((i + distance) % col_count, i) for i in range(col_count)]
            far_sources.append(lax.ppermute(far_source, "col", route))
            lookup.append([(hop - 1, r) for r in range(distant_rows)])
    edge_cap = min(3 if row_count >= 2 else 4, tile_blocks)
    main_cap = edge_cap - 1 if col_count >= 3 else edge_cap
    entries = cycle_list[0, 0]
    right_entries = shift(entries, "col", col_count, -1)
    left_entries = shift(entries, "col", col_count, 1)
    to_right, _, _ = side_slots(right_entries, 2, tile_blocks, edge_cap)
    to_left, _, _ = side_slots(left_entries, 2 + tile_blocks, tile_blocks, edge_cap)
    right_payload = jnp.take(stacked, to_right, axis=1)
    left_payload = jnp.take(stacked, to_left, axis=1)
    cycle_sources = [above, below]
    last = col_count - 1
    for slot in range(edge_cap):
        to_r = right_payload[:, slot : slot + 1]
        to_l = left_payload[:, slot : slot + 1]
        later = far_sources[min(2 * slot, len(far_sources) - 1)]
        to_r, to_l, _ = lax.optimization_barrier((to_r, to_l, later))
        if slot < main_cap:
            cycle_sources.append(shift(to_r, "col", col_count, 1))
            cycle_sources.append(shift(to_l, "col", col_count, -1))
        else:
            cycle_sources.append(lax.ppermute(to_r, "col", [(last - 1, last)]))
            cycle_sources.append(lax.ppermute(to_l, "col", [(1, 0)]))

    _, is_left, left_rank = side_slots(entries, 2, tile_blocks, edge_cap)
    _, is_right, right_rank = side_slots(entries, 2 + tile_blocks, tile_blocks, edge_cap)
    side_rank = jnp.where(is_left, left_rank, right_rank)
    cycle_src = jnp.where(
        entries == 0, 0, jnp.where(entries == 1, 1, 2 + is_right.astype(jnp.int32) + 2 * side_rank)
    )
    cycle_idx = jnp.zeros_like(entries)

    lookup_src = jnp.array([[a for a, _ in row] for row in lookup], dtype=jnp.int32)
    lookup_idx = jnp.array([[b for _, b in row] for row in lookup], dtype=jnp.int32)
    far_src = len(cycle_sources) + lookup_src[hop_slot, far_row]
    far_idx = lookup_idx[hop_slot, far_row]

    table = jnp.stack(
        [jnp.concatenate([cycle_src, far_src]), jnp.concatenate([cycle_idx, far_idx])], axis=1
    ).reshape(-1)
    token_count = tile_blocks * block_length
    result = gather_attend(
        queries.reshape(token_count, width), stacked, cycle_sources, far_sources, table
    )
    return result.reshape(queries.shape)


def solution(mesh):
    in_specs = (
        P(("groups", "row"), "col", None, None),
        P(("groups", "row"), "col", None, None),
        P(("groups", "row"), "col", None, None),
        P(("groups", "row"), "col", None, None),
        P(("groups", "row"), "col", None, None),
        P(("groups", "row"), "col", None),
        P(("groups", "row"), "col", None),
    )
    out_specs = P(("groups", "row"), "col", None, None)
    return jax.shard_map(
        per_device, mesh=mesh, in_specs=in_specs, out_specs=out_specs, check_vma=False
    )
```

```python
import functools

import jax
import jax.numpy as jnp
from jax import lax
from jax.experimental import pallas as pl
from jax.experimental.pallas import tpu as pltpu
from jax.sharding import PartitionSpec as P

HEAD_DIM = 128
DILATION_TILES = 8


def dequant(mantissa, exponent):
    tile_rows, tile_cols, block_length, feature_channel_width = mantissa.shape
    groups = exponent.shape[2]
    factor = jnp.exp2(exponent.astype(jnp.float32))[:, :, :, None, :]
    scaled = (
        mantissa.reshape(
            tile_rows, tile_cols, groups, block_length // groups, feature_channel_width
        ).astype(jnp.float32)
        * factor
    )
    return scaled.reshape(mantissa.shape).astype(jnp.bfloat16)


def shift(x, axis, count, step):
    if step > 0:
        pairs = [(i, i + step) for i in range(count - step)]
    else:
        pairs = [(i - step, i) for i in range(count + step)]
    if not pairs:
        return jnp.zeros_like(x)
    return lax.ppermute(x, axis, pairs)


def side_slots(entries, low, tile_blocks, cap):
    inside = (entries >= low) & (entries < low + tile_blocks)
    rank = jnp.cumsum(inside.astype(jnp.int32)) - 1
    slot = jnp.arange(cap, dtype=jnp.int32)[:, None]
    hit = inside[None, :] & (rank[None, :] == slot)
    return jnp.sum(jnp.where(hit, entries[None, :] - low, 0), axis=1), inside, rank


def ring_gather(item, count, me):
    order = list(range(0, count, 2)) + list(range(count - 1 - count % 2, 0, -2))
    position = [0] * count
    for place, col in enumerate(order):
        position[col] = place
    forward = [(order[i], order[(i + 1) % count]) for i in range(count)]
    backward = [(order[(i + 1) % count], order[i]) for i in range(count)]
    half = count // 2
    rows = item.shape[1]
    split = (rows + 1) // 2
    arrays = []
    lookup = [[None] * rows for _ in range(count - 1)]
    for r in range(rows):
        ahead = behind = item[:, r : r + 1]
        for distance in range(1, half + 1):
            if distance == half and count % 2 == 0:
                if r < split:
                    arrays.append(lax.ppermute(ahead, "col", forward))
                else:
                    arrays.append(lax.ppermute(behind, "col", backward))
                lookup[distance - 1][r] = (len(arrays) - 1, 0)
                continue
            ahead = lax.ppermute(ahead, "col", forward)
            arrays.append(ahead)
            lookup[distance - 1][r] = (len(arrays) - 1, 0)
            behind = lax.ppermute(behind, "col", backward)
            arrays.append(behind)
            lookup[count - distance - 1][r] = (len(arrays) - 1, 0)
    table = jnp.array(position, dtype=jnp.int32)

    def relative(col):
        return (table[me] - table[col]) % count - 1

    return arrays, lookup, relative


def gather_attention_kernel(cycle_sources, far_sources, table_ref, q_hbm, own_hbm, *rest):
    sources = rest[: cycle_sources + far_sources]
    o_hbm, o_vmem, q_vmem, k_vmem, v_vmem, sems, out_sems = rest[cycle_sources + far_sources :]
    tile_blocks = own_hbm.shape[1]
    block_length = own_hbm.shape[2]
    extra = table_ref.shape[0] // 2
    heads = q_vmem.shape[1] // HEAD_DIM

    copies = [pltpu.make_async_copy(q_hbm, q_vmem, sems.at[0, 0])]
    copies.append(pltpu.make_async_copy(own_hbm.at[0], k_vmem.at[pl.ds(0, tile_blocks)], sems.at[0, 1]))
    copies.append(pltpu.make_async_copy(own_hbm.at[1], v_vmem.at[pl.ds(0, tile_blocks)], sems.at[1, 1]))
    for c in copies:
        c.start()
    for slot in range(extra):
        src = table_ref[2 * slot]
        index = table_ref[2 * slot + 1]
        lo, hi = (0, cycle_sources) if slot < extra // 2 else (cycle_sources, cycle_sources + far_sources)
        for cand in range(lo, hi):
            @pl.when(src == cand)
            def _():
                for kv, dst in ((0, k_vmem), (1, v_vmem)):
                    pltpu.make_async_copy(
                        sources[cand].at[kv, index], dst.at[tile_blocks + slot], sems.at[kv, 2 + slot]
                    ).start()
    for c in copies:
        c.wait()
    for slot in range(extra):
        for kv, dst in ((0, k_vmem), (1, v_vmem)):
            pltpu.make_async_copy(
                own_hbm.at[kv, 0], dst.at[tile_blocks + slot], sems.at[kv, 2 + slot]
            ).wait()

    key_count = k_vmem.shape[0] * block_length

    groups = out_sems.shape[0]
    group_heads = heads // groups
    writes = []
    for h in range(heads):
        lanes = pl.ds(h * HEAD_DIM, HEAD_DIM)
        q = q_vmem[:, lanes]
        k = k_vmem[:, :, lanes].reshape(key_count, HEAD_DIM)
        v = v_vmem[:, :, lanes].reshape(key_count, HEAD_DIM)
        scores = lax.dot_general(
            q, k, (((1,), (1,)), ((), ())), preferred_element_type=jnp.float32
        ) * HEAD_DIM ** (-0.5)
        row_max = jnp.max(scores, axis=1, keepdims=True)
        weights = jnp.exp(scores - row_max)
        row_total = jnp.sum(weights, axis=1, keepdims=True)
        rounded = weights.astype(jnp.bfloat16)
        blended = jnp.dot(rounded, v, preferred_element_type=jnp.float32)
        o_vmem[:, lanes] = (blended / row_total).astype(o_vmem.dtype)
        if (h + 1) % group_heads == 0:
            group = h // group_heads
            span = pl.ds(group * group_heads * HEAD_DIM, group_heads * HEAD_DIM)
            writes.append(
                pltpu.make_async_copy(o_vmem.at[:, span], o_hbm.at[:, span], out_sems.at[group])
            )
            writes[-1].start()
    for w in writes:
        w.wait()


def gather_attend(query_rows, own, cycle_list_sources, far_list_sources, table):
    token_count, width = query_rows.shape
    tile_blocks, block_length = own.shape[1], own.shape[2]
    extra = table.shape[0] // 2
    blocks = tile_blocks + extra
    key_count = blocks * block_length
    heads = width // HEAD_DIM
    n_sources = len(cycle_list_sources) + len(far_list_sources)
    kernel = functools.partial(
        gather_attention_kernel, len(cycle_list_sources), len(far_list_sources)
    )
    return pl.pallas_call(
        kernel,
        out_shape=jax.ShapeDtypeStruct((token_count, width), jnp.bfloat16),
        in_specs=[pl.BlockSpec(memory_space=pltpu.SMEM)]
        + [pl.BlockSpec(memory_space=pl.ANY)] * (2 + n_sources),
        out_specs=pl.BlockSpec(memory_space=pl.ANY),
        scratch_shapes=[
            pltpu.VMEM((token_count, width), jnp.bfloat16),
            pltpu.VMEM((token_count, width), jnp.bfloat16),
            pltpu.VMEM((blocks, block_length, width), jnp.bfloat16),
            pltpu.VMEM((blocks, block_length, width), jnp.bfloat16),
            pltpu.SemaphoreType.DMA((2, 2 + extra)),
            pltpu.SemaphoreType.DMA((3 if heads % 3 == 0 else 1,)),
        ],
        compiler_params=pltpu.CompilerParams(vmem_limit_bytes=48 * 1024 * 1024),
        cost_estimate=pl.CostEstimate(
            flops=4 * token_count * key_count * width,
            transcendentals=token_count * key_count * heads,
            bytes_accessed=2 * (2 * token_count * width + 2 * key_count * width),
        ),
    )(table, query_rows, own, *cycle_list_sources, *far_list_sources)


def per_device(queries, key_mant, key_exp, value_mant, value_exp, cycle_list, dilated_list):
    tile_blocks = queries.shape[0]
    block_length = queries.shape[2]
    width = queries.shape[3]
    col_count = lax.axis_size("col")
    row_count = lax.axis_size("row")
    distant_rows = tile_blocks // 4
    step_spacing = col_count // DILATION_TILES
    me_col = lax.axis_index("col")

    stacked = jnp.stack([dequant(key_mant, key_exp), dequant(value_mant, value_exp)])[:, :, 0]

    above = shift(stacked[:, tile_blocks - 1 :], "row", row_count, 1)
    below = shift(stacked[:, :1], "row", row_count, -1)

    far_source = stacked[:, 0::4]
    dilated_entries = dilated_list[0, 0]
    hop_slot = dilated_entries // distant_rows
    far_row = dilated_entries % distant_rows
    if step_spacing == 1:
        far_sources, lookup, relative = ring_gather(far_source, col_count, me_col)
        hop_slot = relative((me_col + hop_slot + 1) % col_count)
    else:
        far_sources = []
        lookup = []
        for hop in range(1, DILATION_TILES):
            distance = hop * step_spacing
            route = [((i + distance) % col_count, i) for i in range(col_count)]
            far_sources.append(lax.ppermute(far_source, "col", route))
            lookup.append([(hop - 1, r) for r in range(distant_rows)])
    edge_cap = min(3 if row_count >= 2 else 4, tile_blocks)
    main_cap = edge_cap - 1 if col_count >= 3 else edge_cap
    entries = cycle_list[0, 0]
    right_entries = shift(entries, "col", col_count, -1)
    left_entries = shift(entries, "col", col_count, 1)
    to_right, _, _ = side_slots(right_entries, 2, tile_blocks, edge_cap)
    to_left, _, _ = side_slots(left_entries, 2 + tile_blocks, tile_blocks, edge_cap)
    right_payload = jnp.take(stacked, to_right, axis=1)
    left_payload = jnp.take(stacked, to_left, axis=1)
    cycle_sources = [above, below]
    last = col_count - 1
    for slot in range(edge_cap):
        to_r = right_payload[:, slot : slot + 1]
        to_l = left_payload[:, slot : slot + 1]
        later = far_sources[min(2 * min(slot, 1), len(far_sources) - 1)]
        to_r, to_l, _ = lax.optimization_barrier((to_r, to_l, later))
        if slot < main_cap:
            cycle_sources.append(shift(to_r, "col", col_count, 1))
            cycle_sources.append(shift(to_l, "col", col_count, -1))
        else:
            cycle_sources.append(lax.ppermute(to_r, "col", [(last - 1, last)]))
            cycle_sources.append(lax.ppermute(to_l, "col", [(1, 0)]))

    _, is_left, left_rank = side_slots(entries, 2, tile_blocks, edge_cap)
    _, is_right, right_rank = side_slots(entries, 2 + tile_blocks, tile_blocks, edge_cap)
    side_rank = jnp.where(is_left, left_rank, right_rank)
    cycle_src = jnp.where(
        entries == 0, 0, jnp.where(entries == 1, 1, 2 + is_right.astype(jnp.int32) + 2 * side_rank)
    )
    cycle_idx = jnp.zeros_like(entries)

    lookup_src = jnp.array([[a for a, _ in row] for row in lookup], dtype=jnp.int32)
    lookup_idx = jnp.array([[b for _, b in row] for row in lookup], dtype=jnp.int32)
    far_src = len(cycle_sources) + lookup_src[hop_slot, far_row]
    far_idx = lookup_idx[hop_slot, far_row]

    table = jnp.stack(
        [jnp.concatenate([cycle_src, far_src]), jnp.concatenate([cycle_idx, far_idx])], axis=1
    ).reshape(-1)
    token_count = tile_blocks * block_length
    result = gather_attend(
        queries.reshape(token_count, width), stacked, cycle_sources, far_sources, table
    )
    return result.reshape(queries.shape)


def solution(mesh):
    in_specs = (
        P(("groups", "row"), "col", None, None),
        P(("groups", "row"), "col", None, None),
        P(("groups", "row"), "col", None, None),
        P(("groups", "row"), "col", None, None),
        P(("groups", "row"), "col", None, None),
        P(("groups", "row"), "col", None),
        P(("groups", "row"), "col", None),
    )
    out_specs = P(("groups", "row"), "col", None, None)
    return jax.shard_map(
        per_device, mesh=mesh, in_specs=in_specs, out_specs=out_specs, check_vma=False
    )
```
